32 devices in a mesh: rep: 2 (over y), grp: 4 (over z), sub: 4 (over x, core).
Axes of the slice: x: 2, y: 2, z: 4, core: 2. Of those that a mesh axis runs over, the one named last changes fastest.
Arguments:
- volume: bfloat16 [256, 8, 8, 128], P(None, ('rep', 'grp'), 'sub'), parts along dimension 1, may hold values from -6 to 6
- cotangent: bfloat16 [256, 8, 8, 128], P(None, ('rep', 'grp'), 'sub'), parts along dimension 1, may hold values from -6 to 6
- first_weight: bfloat16 [256, 256], replicated, may hold values from -0.375 to 0.375
- group_weight: bfloat16 [256, 8, 3, 3, 3], replicated, may hold values from -0.4375 to 0.4375
- third_weight: bfloat16 [256, 256], replicated, may hold values from -0.375 to 0.375
Outputs:
- block_output: bfloat16 [256, 8, 8, 128], P(None, ('rep', 'grp'), 'sub'), parts along dimension 1
- volume_grad: bfloat16 [256, 8, 8, 128], P(None, ('rep', 'grp'), 'sub'), parts along dimension 1
- first_grad: float32 [512, 256], P('rep'), parts along dimension 0
- group_grad: float32 [512, 8, 3, 3, 3], P(('rep', 'grp')), parts along dimension 0
- third_grad: float32 [512, 256], P('rep'), parts along dimension 0
The draws below stay inside these ranges and needn't reach their ends.
There are 2 independent parts, one for each index of `rep`. The reference program is written for one: setup_inputs(seed, part) draws one part's arguments, and reference() takes and returns one part's arrays. A program takes and returns all parts, laid end to end along the dimension named above; an argument that names none is the same for every part. Nothing has to cross between parts.
All inputs are finite; a program needn't handle non-finite values.
Results may differ from the reference program's by a relative error of at most 0.0073.
Values may be sent and summed in bfloat16 or wider, within the bound.
No kernel may reach another device: no remote copies, remote signals or barrier semaphores. Data moves between devices by JAX's collectives and lax.ppermute only.
A program may use at most 64 MiB of HBM per device.

```python
import math
import jax
import jax.numpy as jnp
from jax import lax

G = 32
GW = 8
C = 256
XLEN = 128
Z = 4
Y = 8


def levels(rng, dims, pieces, smallest, top_value):
    gain = 1.0
    for position, blocks in pieces:
        steps = jax.random.uniform(jax.random.fold_in(jax.random.fold_in(rng, 6), position), (blocks,), jnp.float32, smallest / len(pieces), top_value / len(pieces))
        gain = gain * jnp.repeat(jnp.exp(steps), dims[position] // blocks).reshape((-1,) + (1,) * (len(dims) - 1 - position))
    return gain


def scatter_about(rng, dims, scale, limit, shards=(), held_as=jnp.bfloat16):
    values = scale * jax.random.normal(rng, dims, jnp.float32)
    if shards:
        values = values * levels(rng, dims, shards, -0.22, 0.18)
    return jnp.clip(values, -limit, limit).astype(held_as)


def setup_inputs(seed: int = 0, part: int = 0) -> dict:
    key_list = jax.random.split(jax.random.key(seed), 6)
    part_keys = jax.random.split(jax.random.fold_in(key_list[5], part), 6)
    return {
        "volume": scatter_about(part_keys[0], (C, Z, Y, XLEN), 1.0, 6.0, ((1, 4), (2, 4))),
        "cotangent": scatter_about(part_keys[1], (C, Z, Y, XLEN), 1.0, 6.0, ((1, 4), (2, 4))),
        "first_weight": scatter_about(key_list[2], (C, C), C ** -0.5, 0.375),
        "group_weight": scatter_about(key_list[3], (C, GW, 3, 3, 3), (GW * 27) ** -0.5, 0.4375),
        "third_weight": scatter_about(key_list[4], (C, C), C ** -0.5, 0.375),
    }


def silu_slope(values):
    sigma = jax.nn.sigmoid(values)
    return sigma * (1.0 + values * (1.0 - sigma))

def grouped_conv(source, kernel, groups):
    padding = ((1, 1), (1, 1), (1, 1))
    return lax.conv_general_dilated(source[None].astype(jnp.float32), kernel.astype(jnp.float32), (1, 1, 1), padding, dimension_numbers=('NCDHW', 'OIDHW', 'NCDHW'), feature_group_count=groups, precision=lax.Precision.HIGHEST, preferred_element_type=jnp.float32)[0]

def flipped_kernel(kernel, groups):
    shaped = kernel.reshape(groups, GW, GW, 3, 3, 3)
    return shaped.transpose(0, 2, 1, 3, 4, 5)[:, :, :, ::-1, ::-1, ::-1].reshape(groups * GW, GW, 3, 3, 3)

def kernel_grad(padded, deltas, groups):
    channels, depth, height, width = deltas.shape
    shaped_delta = deltas.reshape(groups, GW, -1).astype(jnp.float32)
    results = []
    for offset in range(27):
        depth_tap = offset // 9
        height_tap = offset // 3 % 3
        width_tap = offset % 3
        shifted = padded[:, depth_tap:depth_tap + depth, height_tap:height_tap + height, width_tap:width_tap + width]
        shifted = shifted.reshape(groups, GW, -1).astype(jnp.float32)
        results.append(jnp.einsum('gon,gin->goi', shaped_delta, shifted, precision=lax.Precision.HIGHEST))
    return jnp.stack(results, axis=-1).reshape(channels, GW, 3, 3, 3)

def reference(volume, cotangent, first_weight, group_weight, third_weight):
    channels, depth, height, width = volume.shape
    flattened = volume.reshape(channels, -1)
    factor = 1.0 / math.sqrt(depth * height * width)
    first_pre = jnp.dot(first_weight.T, flattened, preferred_element_type=jnp.float32)
    first_act = jax.nn.silu(first_pre).astype(jnp.bfloat16).reshape(volume.shape)
    group_pre = grouped_conv(first_act, group_weight, G)
    group_act = jax.nn.silu(group_pre).astype(jnp.bfloat16)
    act_flat = group_act.reshape(channels, -1)
    summed = flattened.astype(jnp.float32) + jnp.dot(third_weight.T, act_flat, preferred_element_type=jnp.float32)
    block_output = jax.nn.silu(summed).astype(jnp.bfloat16).reshape(volume.shape)
    third_delta = (cotangent.reshape(channels, -1).astype(jnp.float32) * silu_slope(summed)).astype(jnp.bfloat16)
    third_grad = jnp.dot(act_flat, third_delta.T, preferred_element_type=jnp.float32) * factor
    hidden_grad = jnp.dot(third_weight, third_delta, preferred_element_type=jnp.float32).astype(jnp.bfloat16).reshape(volume.shape)
    group_delta = (hidden_grad.astype(jnp.float32) * silu_slope(group_pre)).astype(jnp.bfloat16)
    padded = jnp.pad(first_act, ((0, 0), (1, 1), (1, 1), (1, 1)))
    group_grad = kernel_grad(padded, group_delta, G) * factor
    inner_grad = grouped_conv(group_delta, flipped_kernel(group_weight, G), G).astype(jnp.bfloat16)
    first_delta = (inner_grad.reshape(channels, -1).astype(jnp.float32) * silu_slope(first_pre)).astype(jnp.bfloat16)
    first_grad = jnp.dot(flattened, first_delta.T, preferred_element_type=jnp.float32) * factor
    volume_grad = (third_delta.astype(jnp.float32) + jnp.dot(first_weight, first_delta, preferred_element_type=jnp.float32)).astype(jnp.bfloat16).reshape(volume.shape)
    return (block_output, volume_grad, first_grad, group_grad, third_grad)
```

```python
import math

import jax
import jax.numpy as jnp
from jax import lax
from jax.sharding import PartitionSpec as P

GW = 8


def padded_2(block, sides, width):
    for axis, dim in sides:
        count = lax.axis_size(axis)
        forward = [(i, i + 1) for i in range(count - 1)]
        backward = [(target, source) for source, target in forward]
        low = lax.ppermute(
            lax.slice_in_dim(block, block.shape[dim] - width, None, axis=dim), axis, forward
        )
        high = lax.ppermute(lax.slice_in_dim(block, 0, width, axis=dim), axis, backward)
        block = jnp.concatenate([low, block, high], axis=dim)
    return block


def silu_slope(values):
    sigma = jax.nn.sigmoid(values)
    return sigma * (1.0 + values * (1.0 - sigma))


def dense_conv(source, kernel, depth_pad):
    padding = ((depth_pad, depth_pad), (0, 0), (1, 1))
    return lax.conv_general_dilated(
        source[None],
        kernel,
        (1, 1, 1),
        padding,
        dimension_numbers=("NCDHW", "OIDHW", "NCDHW"),
        preferred_element_type=jnp.float32,
    )[0]


def block_diagonal(kernel):
    rows = kernel.shape[0]
    tiled = jnp.tile(kernel, (1, rows // GW, 1, 1, 1))
    group_of = jnp.arange(rows) // GW
    mask = (group_of[:, None] == group_of[None, :]).astype(kernel.dtype)
    return tiled * mask[:, :, None, None, None]


def diagonal_blocks(dense):
    rows = dense.shape[1]
    groups = rows // GW
    shaped = dense.reshape(groups, GW, rows, *dense.shape[2:])
    group_of = jnp.arange(rows) // GW
    mask = (jnp.arange(groups)[:, None] == group_of[None, :]).astype(dense.dtype)
    picked = (shaped * mask[:, None, :, None, None, None]).sum(axis=0)
    return picked.transpose(1, 0, 2, 3, 4)


def weight_grad(padded, deltas):
    return lax.conv_general_dilated(
        padded[None],
        deltas[None],
        (1, 1, 1),
        "VALID",
        dimension_numbers=("CNDHW", "IODHW", "NCDHW"),
        preferred_element_type=jnp.float32,
    )


def per_device(volume, cotangent, first_weight, group_weight, third_weight):
    channels, depth, height, width = volume.shape
    flattened = volume.reshape(channels, -1)
    contract_lead = (((0,), (0,)), ((), ()))
    contract_tail = (((1,), (1,)), ((), ()))
    total_cells = depth * lax.axis_size("grp") * height * lax.axis_size("sub") * width
    factor = 1.0 / math.sqrt(total_cells)
    group_rows = channels // lax.axis_size("grp")
    first_pre = lax.dot_general(
        first_weight, flattened, contract_lead, preferred_element_type=jnp.float32
    )
    first_act = jax.nn.silu(first_pre).astype(jnp.bfloat16).reshape(volume.shape)
    own_kernel = lax.dynamic_slice_in_dim(
        group_weight, lax.axis_index("grp") * group_rows, group_rows, 0
    )
    dense_kernel = block_diagonal(own_kernel)
    gathered = lax.all_to_all(first_act, "grp", split_axis=0, concat_axis=1, tiled=True)
    padded_act = padded_2(gathered, (("sub", 2),), 1)
    group_pre = dense_conv(padded_act, dense_kernel, 1)
    group_act = jax.nn.silu(group_pre).astype(jnp.bfloat16)
    returned = lax.all_to_all(group_act, "grp", split_axis=1, concat_axis=0, tiled=True)
    act_flat = returned.reshape(channels, -1)
    summed = flattened.astype(jnp.float32) + lax.dot_general(
        third_weight, act_flat, contract_lead, preferred_element_type=jnp.float32
    )
    block_output = jax.nn.silu(summed).astype(jnp.bfloat16).reshape(volume.shape)
    third_delta = (cotangent.reshape(channels, -1).astype(jnp.float32) * silu_slope(summed)).astype(
        jnp.bfloat16
    )
    third_part = lax.dot_general(
        act_flat, third_delta, contract_tail, preferred_element_type=jnp.float32
    )
    third_grad = lax.psum(third_part, ("grp", "sub")) * factor
    hidden_grad = (
        jnp.dot(third_weight, third_delta, preferred_element_type=jnp.float32)
        .astype(jnp.bfloat16)
        .reshape(volume.shape)
    )
    arriving = lax.all_to_all(hidden_grad, "grp", split_axis=0, concat_axis=1, tiled=True)
    group_delta = (arriving.astype(jnp.float32) * silu_slope(group_pre)).astype(jnp.bfloat16)
    delta_rim = padded_2(group_delta, (("sub", 2),), 1)
    flipped = dense_kernel.transpose(1, 0, 2, 3, 4)[:, :, ::-1, ::-1, ::-1]
    inner_local = dense_conv(delta_rim, flipped, 1).astype(jnp.bfloat16)
    dense_grad = weight_grad(
        jnp.pad(padded_act, ((0, 0), (1, 1), (0, 0), (1, 1))), group_delta
    )
    kernel_part = diagonal_blocks(dense_grad)
    inner_grad = lax.all_to_all(inner_local, "grp", split_axis=1, concat_axis=0, tiled=True)
    group_grad = lax.psum(kernel_part, "sub") * factor
    first_delta = (
        inner_grad.reshape(channels, -1).astype(jnp.float32) * silu_slope(first_pre)
    ).astype(jnp.bfloat16)
    first_part = lax.dot_general(
        flattened, first_delta, contract_tail, preferred_element_type=jnp.float32
    )
    volume_grad = (
        (
            third_delta.astype(jnp.float32)
            + jnp.dot(first_weight, first_delta, preferred_element_type=jnp.float32)
        )
        .astype(jnp.bfloat16)
        .reshape(volume.shape)
    )
    first_grad = lax.psum(first_part, ("grp", "sub")) * factor
    return (block_output, volume_grad, first_grad, group_grad, third_grad)


def solution(mesh):
    in_specs = (
        P(None, ("rep", "grp"), "sub", None),
        P(None, ("rep", "grp"), "sub", None),
        P(),
        P(),
        P(),
    )
    out_specs = (
        P(None, ("rep", "grp"), "sub", None),
        P(None, ("rep", "grp"), "sub", None),
        P("rep", None),
        P(("rep", "grp"), None, None, None, None),
        P("rep", None),
    )
    return jax.shard_map(
        per_device, mesh=mesh, in_specs=in_specs, out_specs=out_specs, check_vma=False
    )
```

```python
import math

import jax
import jax.numpy as jnp
from jax import lax
from jax.sharding import PartitionSpec as P

GW = 8


def padded_2(block, sides, width):
    for axis, dim in sides:
        count = lax.axis_size(axis)
        forward = [(i, i + 1) for i in range(count - 1)]
        backward = [(target, source) for source, target in forward]
        low = lax.ppermute(
            lax.slice_in_dim(block, block.shape[dim] - width, None, axis=dim), axis, forward
        )
        high = lax.ppermute(lax.slice_in_dim(block, 0, width, axis=dim), axis, backward)
        block = jnp.concatenate([low, block, high], axis=dim)
    return block


def tree_sum(block, axes):
    steps = []
    for axis in axes:
        count = lax.axis_size(axis)
        bit = 1
        while bit < count:
            steps.append((axis, bit))
            bit *= 2
    shape = block.shape
    pieces = block.reshape(-1)
    kept = []
    for axis, bit in steps:
        pairs = [(i, i ^ bit) for i in range(lax.axis_size(axis))]
        upper = (lax.axis_index(axis) & bit) != 0
        half = pieces.shape[0] // 2
        low, high = pieces[:half], pieces[half:]
        keep = jnp.where(upper, high, low)
        send = jnp.where(upper, low, high)
        pieces = keep + lax.ppermute(send, axis, pairs)
        kept.append((axis, bit, pairs, upper))
    for axis, bit, pairs, upper in reversed(kept):
        got = lax.ppermute(pieces, axis, pairs)
        pieces = jnp.where(
            upper, jnp.concatenate([got, pieces]), jnp.concatenate([pieces, got])
        )
    return pieces.reshape(shape)


def silu_slope(values):
    sigma = jax.nn.sigmoid(values)
    return sigma * (1.0 + values * (1.0 - sigma))


def dense_conv(source, kernel, depth_pad):
    padding = ((depth_pad, depth_pad), (0, 0), (1, 1))
    return lax.conv_general_dilated(
        source[None],
        kernel,
        (1, 1, 1),
        padding,
        dimension_numbers=("NCDHW", "OIDHW", "NCDHW"),
        preferred_element_type=jnp.float32,
    )[0]


def block_diagonal(kernel):
    rows = kernel.shape[0]
    tiled = jnp.tile(kernel, (1, rows // GW, 1, 1, 1))
    group_of = jnp.arange(rows) // GW
    mask = (group_of[:, None] == group_of[None, :]).astype(kernel.dtype)
    return tiled * mask[:, :, None, None, None]


def diagonal_blocks(dense):
    rows = dense.shape[1]
    groups = rows // GW
    shaped = dense.reshape(groups, GW, rows, *dense.shape[2:])
    group_of = jnp.arange(rows) // GW
    mask = (jnp.arange(groups)[:, None] == group_of[None, :]).astype(dense.dtype)
    picked = (shaped * mask[:, None, :, None, None, None]).sum(axis=0)
    return picked.transpose(1, 0, 2, 3, 4)


def weight_grad(padded, deltas):
    return lax.conv_general_dilated(
        padded[None],
        deltas[None],
        (1, 1, 1),
        "VALID",
        dimension_numbers=("CNDHW", "IODHW", "NCDHW"),
        preferred_element_type=jnp.float32,
    )


def per_device(volume, cotangent, first_weight, group_weight, third_weight):
    channels, depth, height, width = volume.shape
    flattened = volume.reshape(channels, -1)
    contract_lead = (((0,), (0,)), ((), ()))
    contract_tail = (((1,), (1,)), ((), ()))
    total_cells = depth * lax.axis_size("grp") * height * lax.axis_size("sub") * width
    factor = 1.0 / math.sqrt(total_cells)
    group_rows = channels // lax.axis_size("grp")
    first_pre = lax.dot_general(
        first_weight, flattened, contract_lead, preferred_element_type=jnp.float32
    )
    first_act = jax.nn.silu(first_pre).astype(jnp.bfloat16).reshape(volume.shape)
    own_kernel = lax.dynamic_slice_in_dim(
        group_weight, lax.axis_index("grp") * group_rows, group_rows, 0
    )
    dense_kernel = block_diagonal(own_kernel)
    gathered = lax.all_to_all(first_act, "grp", split_axis=0, concat_axis=1, tiled=True)
    padded_act = padded_2(gathered, (("sub", 2),), 1)
    group_pre = dense_conv(padded_act, dense_kernel, 1)
    group_act = jax.nn.silu(group_pre).astype(jnp.bfloat16)
    returned = lax.all_to_all(group_act, "grp", split_axis=1, concat_axis=0, tiled=True)
    act_flat = returned.reshape(channels, -1)
    summed = flattened.astype(jnp.float32) + lax.dot_general(
        third_weight, act_flat, contract_lead, preferred_element_type=jnp.float32
    )
    block_output = jax.nn.silu(summed).astype(jnp.bfloat16).reshape(volume.shape)
    third_delta = (cotangent.reshape(channels, -1).astype(jnp.float32) * silu_slope(summed)).astype(
        jnp.bfloat16
    )
    third_part = lax.dot_general(
        act_flat, third_delta, contract_tail, preferred_element_type=jnp.float32
    )
    third_grad = tree_sum(third_part, ("sub", "grp")) * factor
    hidden_grad = (
        jnp.dot(third_weight, third_delta, preferred_element_type=jnp.float32)
        .astype(jnp.bfloat16)
        .reshape(volume.shape)
    )
    arriving = lax.all_to_all(hidden_grad, "grp", split_axis=0, concat_axis=1, tiled=True)
    group_delta = (arriving.astype(jnp.float32) * silu_slope(group_pre)).astype(jnp.bfloat16)
    delta_rim = padded_2(group_delta, (("sub", 2),), 1)
    flipped = dense_kernel.transpose(1, 0, 2, 3, 4)[:, :, ::-1, ::-1, ::-1]
    inner_local = dense_conv(delta_rim, flipped, 1).astype(jnp.bfloat16)
    dense_grad = weight_grad(
        jnp.pad(padded_act, ((0, 0), (1, 1), (0, 0), (1, 1))), group_delta
    )
    kernel_part = diagonal_blocks(dense_grad)
    inner_grad = lax.all_to_all(inner_local, "grp", split_axis=1, concat_axis=0, tiled=True)
    group_grad = tree_sum(kernel_part, ("sub",)) * factor
    first_delta = (
        inner_grad.reshape(channels, -1).astype(jnp.float32) * silu_slope(first_pre)
    ).astype(jnp.bfloat16)
    first_part = lax.dot_general(
        flattened, first_delta, contract_tail, preferred_element_type=jnp.float32
    )
    volume_grad = (
        (
            third_delta.astype(jnp.float32)
            + jnp.dot(first_weight, first_delta, preferred_element_type=jnp.float32)
        )
        .astype(jnp.bfloat16)
        .reshape(volume.shape)
    )
    first_grad = tree_sum(first_part, ("sub", "grp")) * factor
    return (block_output, volume_grad, first_grad, group_grad, third_grad)


def solution(mesh):
    in_specs = (
        P(None, ("rep", "grp"), "sub", None),
        P(None, ("rep", "grp"), "sub", None),
        P(),
        P(),
        P(),
    )
    out_specs = (
        P(None, ("rep", "grp"), "sub", None),
        P(None, ("rep", "grp"), "sub", None),
        P("rep", None),
        P(("rep", "grp"), None, None, None, None),
        P("rep", None),
    )
    return jax.shard_map(
        per_device, mesh=mesh, in_specs=in_specs, out_specs=out_specs, check_vma=False
    )
```

```python
import math

import jax
import jax.numpy as jnp
from jax import lax
from jax.sharding import PartitionSpec as P

GW = 8


def padded_2(block, sides, width):
    for axis, dim in sides:
        count = lax.axis_size(axis)
        forward = [(i, i + 1) for i in range(count - 1)]
        backward = [(target, source) for source, target in forward]
        low = lax.ppermute(
            lax.slice_in_dim(block, block.shape[dim] - width, None, axis=dim), axis, forward
        )
        high = lax.ppermute(lax.slice_in_dim(block, 0, width, axis=dim), axis, backward)
        block = jnp.concatenate([low, block, high], axis=dim)
    return block


def tree_sum(blocks):
    order = []
    for _, axes in blocks:
        for axis in axes:
            if axis not in order:
                order.append(axis)
    steps = []
    for axis in order:
        bit = 1
        while bit < lax.axis_size(axis):
            steps.append((axis, bit))
            bit *= 2
    pieces = [block.reshape(-1) for block, _ in blocks]
    done = []
    for axis, bit in steps:
        pairs = [(i, i ^ bit) for i in range(lax.axis_size(axis))]
        upper = (lax.axis_index(axis) & bit) != 0
        members = [n for n, (_, axes) in enumerate(blocks) if axis in axes]
        keeps, sends = [], []
        for n in members:
            half = pieces[n].shape[0] // 2
            low, high = pieces[n][:half], pieces[n][half:]
            keeps.append(jnp.where(upper, high, low))
            sends.append(jnp.where(upper, low, high))
        got = lax.ppermute(jnp.concatenate(sends), axis, pairs)
        offset = 0
        for n, keep in zip(members, keeps):
            pieces[n] = keep + got[offset : offset + keep.shape[0]]
            offset += keep.shape[0]
        done.append((axis, pairs, upper, members))
    for axis, pairs, upper, members in reversed(done):
        got = lax.ppermute(jnp.concatenate([pieces[n] for n in members]), axis, pairs)
        offset = 0
        for n in members:
            size = pieces[n].shape[0]
            other = got[offset : offset + size]
            offset += size
            pieces[n] = jnp.where(
                upper,
                jnp.concatenate([other, pieces[n]]),
                jnp.concatenate([pieces[n], other]),
            )
    return [piece.reshape(block.shape) for piece, (block, _) in zip(pieces, blocks)]


def silu_slope(values):
    sigma = jax.nn.sigmoid(values)
    return sigma * (1.0 + values * (1.0 - sigma))


def dense_conv(source, kernel, depth_pad):
    padding = ((depth_pad, depth_pad), (0, 0), (1, 1))
    return lax.conv_general_dilated(
        source[None],
        kernel,
        (1, 1, 1),
        padding,
        dimension_numbers=("NCDHW", "OIDHW", "NCDHW"),
        preferred_element_type=jnp.float32,
    )[0]


def block_diagonal(kernel):
    rows = kernel.shape[0]
    tiled = jnp.tile(kernel, (1, rows // GW, 1, 1, 1))
    group_of = jnp.arange(rows) // GW
    mask = (group_of[:, None] == group_of[None, :]).astype(kernel.dtype)
    return tiled * mask[:, :, None, None, None]


def diagonal_blocks(dense):
    rows = dense.shape[1]
    groups = rows // GW
    shaped = dense.reshape(groups, GW, rows, *dense.shape[2:])
    group_of = jnp.arange(rows) // GW
    mask = (jnp.arange(groups)[:, None] == group_of[None, :]).astype(dense.dtype)
    picked = (shaped * mask[:, None, :, None, None, None]).sum(axis=0)
    return picked.transpose(1, 0, 2, 3, 4)


def weight_grad(padded, deltas):
    return lax.conv_general_dilated(
        padded[None],
        deltas[None],
        (1, 1, 1),
        "VALID",
        dimension_numbers=("CNDHW", "IODHW", "NCDHW"),
        preferred_element_type=jnp.float32,
    )


def per_device(volume, cotangent, first_weight, group_weight, third_weight):
    channels, depth, height, width = volume.shape
    flattened = volume.reshape(channels, -1)
    contract_lead = (((0,), (0,)), ((), ()))
    contract_tail = (((1,), (1,)), ((), ()))
    total_cells = depth * lax.axis_size("grp") * height * lax.axis_size("sub") * width
    factor = 1.0 / math.sqrt(total_cells)
    group_rows = channels // lax.axis_size("grp")
    first_pre = lax.dot_general(
        first_weight, flattened, contract_lead, preferred_element_type=jnp.float32
    )
    first_act = jax.nn.silu(first_pre).astype(jnp.bfloat16).reshape(volume.shape)
    own_kernel = lax.dynamic_slice_in_dim(
        group_weight, lax.axis_index("grp") * group_rows, group_rows, 0
    )
    dense_kernel = block_diagonal(own_kernel)
    gathered = lax.all_to_all(first_act, "grp", split_axis=0, concat_axis=1, tiled=True)
    padded_act = padded_2(gathered, (("sub", 2),), 1)
    group_pre = dense_conv(padded_act, dense_kernel, 1)
    group_act = jax.nn.silu(group_pre).astype(jnp.bfloat16)
    returned = lax.all_to_all(group_act, "grp", split_axis=1, concat_axis=0, tiled=True)
    act_flat = returned.reshape(channels, -1)
    summed = flattened.astype(jnp.float32) + lax.dot_general(
        third_weight, act_flat, contract_lead, preferred_element_type=jnp.float32
    )
    block_output = jax.nn.silu(summed).astype(jnp.bfloat16).reshape(volume.shape)
    third_delta = (cotangent.reshape(channels, -1).astype(jnp.float32) * silu_slope(summed)).astype(
        jnp.bfloat16
    )
    third_part = lax.dot_general(
        act_flat, third_delta, contract_tail, preferred_element_type=jnp.float32
    )
    hidden_grad = (
        jnp.dot(third_weight, third_delta, preferred_element_type=jnp.float32)
        .astype(jnp.bfloat16)
        .reshape(volume.shape)
    )
    arriving = lax.all_to_all(hidden_grad, "grp", split_axis=0, concat_axis=1, tiled=True)
    group_delta = (arriving.astype(jnp.float32) * silu_slope(group_pre)).astype(jnp.bfloat16)
    delta_rim = padded_2(group_delta, (("sub", 2),), 1)
    flipped = dense_kernel.transpose(1, 0, 2, 3, 4)[:, :, ::-1, ::-1, ::-1]
    inner_local = dense_conv(delta_rim, flipped, 1).astype(jnp.bfloat16)
    dense_grad = weight_grad(
        jnp.pad(padded_act, ((0, 0), (1, 1), (0, 0), (1, 1))), group_delta
    )
    kernel_part = diagonal_blocks(dense_grad)
    inner_grad = lax.all_to_all(inner_local, "grp", split_axis=1, concat_axis=0, tiled=True)
    first_delta = (
        inner_grad.reshape(channels, -1).astype(jnp.float32) * silu_slope(first_pre)
    ).astype(jnp.bfloat16)
    first_part = lax.dot_general(
        flattened, first_delta, contract_tail, preferred_element_type=jnp.float32
    )
    volume_grad = (
        (
            third_delta.astype(jnp.float32)
            + jnp.dot(first_weight, first_delta, preferred_element_type=jnp.float32)
        )
        .astype(jnp.bfloat16)
        .reshape(volume.shape)
    )
    first_sum, third_sum, group_sum = tree_sum(
        [(first_part, ("sub", "grp")), (third_part, ("sub", "grp")), (kernel_part, ("sub",))]
    )
    first_grad = first_sum * factor
    third_grad = third_sum * factor
    group_grad = group_sum * factor
    return (block_output, volume_grad, first_grad, group_grad, third_grad)


def solution(mesh):
    in_specs = (
        P(None, ("rep", "grp"), "sub", None),
        P(None, ("rep", "grp"), "sub", None),
        P(),
        P(),
        P(),
    )
    out_specs = (
        P(None, ("rep", "grp"), "sub", None),
        P(None, ("rep", "grp"), "sub", None),
        P("rep", None),
        P(("rep", "grp"), None, None, None, None),
        P("rep", None),
    )
    return jax.shard_map(
        per_device, mesh=mesh, in_specs=in_specs, out_specs=out_specs, check_vma=False
    )
```

```python
import itertools
import math

import jax
import jax.numpy as jnp
from jax import lax
from jax.sharding import PartitionSpec as P

GW = 8


def tree_sum(blocks, order):
    steps = []
    for axis in order:
        bit = lax.axis_size(axis) // 2
        while bit >= 1:
            steps.append((axis, bit))
            bit //= 2
    pieces = [block.reshape(-1) for block, _, _ in blocks]
    done = []
    for axis, bit in steps:
        pairs = [(i, i ^ bit) for i in range(lax.axis_size(axis))]
        upper = (lax.axis_index(axis) & bit) != 0
        members = [n for n, (_, axes, _) in enumerate(blocks) if axis in axes]
        keeps, sends = [], []
        for n in members:
            half = pieces[n].shape[0] // 2
            low, high = pieces[n][:half], pieces[n][half:]
            keeps.append(jnp.where(upper, high, low))
            sends.append(jnp.where(upper, low, high))
        got = lax.ppermute(jnp.concatenate(sends), axis, pairs)
        offset = 0
        for n, keep in zip(members, keeps):
            pieces[n] = keep + got[offset : offset + keep.shape[0]]
            offset += keep.shape[0]
        done.append((axis, pairs, upper))
    for axis, pairs, upper in reversed(done):
        members = [n for n, (_, _, axes) in enumerate(blocks) if axis in axes]
        if not members:
            continue
        got = lax.ppermute(jnp.concatenate([pieces[n] for n in members]), axis, pairs)
        offset = 0
        for n in members:
            size = pieces[n].shape[0]
            other = got[offset : offset + size]
            offset += size
            pieces[n] = jnp.where(
                upper,
                jnp.concatenate([other, pieces[n]]),
                jnp.concatenate([pieces[n], other]),
            )
    return pieces


def halo(block):
    for axis, dim in (("grp", 1), ("sub", 2)):
        count = lax.axis_size(axis)
        up = [(i, i + 1) for i in range(count - 1)]
        down = [(i + 1, i) for i in range(count - 1)]
        size = block.shape[dim]
        low = lax.ppermute(lax.slice_in_dim(block, size - 1, size, axis=dim), axis, up)
        high = lax.ppermute(lax.slice_in_dim(block, 0, 1, axis=dim), axis, down)
        block = jnp.concatenate([low, block, high], axis=dim)
    return jnp.pad(block, ((0, 0), (0, 0), (0, 0), (1, 1)))


def taps(ext, depth, height, width):
    channels = ext.shape[0]
    stacked = jnp.stack(
        [
            ext[:, dz : dz + depth, dy : dy + height, dx : dx + width]
            for dz, dy, dx in itertools.product(range(3), repeat=3)
        ],
        axis=1,
    )
    return stacked.reshape(channels // GW, GW * 27, depth * height * width)


def silu_slope(values):
    sigma = jax.nn.sigmoid(values)
    return sigma * (1.0 + values * (1.0 - sigma))


def per_device(volume, cotangent, first_weight, group_weight, third_weight):
    channels, depth, height, width = volume.shape
    groups = channels // GW
    flattened = volume.reshape(channels, -1)
    contract_lead = (((0,), (0,)), ((), ()))
    contract_tail = (((1,), (1,)), ((), ()))
    grouped_mm = (((2,), (1,)), ((0,), (0,)))
    grouped_nt = (((2,), (2,)), ((0,), (0,)))
    total_cells = depth * lax.axis_size("grp") * height * lax.axis_size("sub") * width
    factor = 1.0 / math.sqrt(total_cells)
    first_pre = lax.dot_general(
        first_weight, flattened, contract_lead, preferred_element_type=jnp.float32
    )
    first_act = jax.nn.silu(first_pre).astype(jnp.bfloat16).reshape(volume.shape)
    act_taps = taps(halo(first_act), depth, height, width)
    kernel = group_weight.reshape(groups, GW, GW * 27)
    group_pre = lax.dot_general(
        kernel, act_taps, grouped_mm, preferred_element_type=jnp.float32
    ).reshape(channels, -1)
    group_act = jax.nn.silu(group_pre).astype(jnp.bfloat16)
    summed = flattened.astype(jnp.float32) + lax.dot_general(
        third_weight, group_act, contract_lead, preferred_element_type=jnp.float32
    )
    block_output = jax.nn.silu(summed).astype(jnp.bfloat16).reshape(volume.shape)
    third_delta = (cotangent.reshape(channels, -1).astype(jnp.float32) * silu_slope(summed)).astype(
        jnp.bfloat16
    )
    third_part = lax.dot_general(
        group_act, third_delta, contract_tail, preferred_element_type=jnp.float32
    )
    hidden_grad = jnp.dot(third_weight, third_delta, preferred_element_type=jnp.float32).astype(
        jnp.bfloat16
    )
    group_delta = (hidden_grad.astype(jnp.float32) * silu_slope(group_pre)).astype(jnp.bfloat16)
    delta_taps = taps(halo(group_delta.reshape(volume.shape)), depth, height, width)
    flipped = (
        group_weight.reshape(groups, GW, GW, 3, 3, 3)
        .transpose(0, 2, 1, 3, 4, 5)[:, :, :, ::-1, ::-1, ::-1]
        .reshape(groups, GW, GW * 27)
    )
    inner_grad = (
        lax.dot_general(flipped, delta_taps, grouped_mm, preferred_element_type=jnp.float32)
        .reshape(channels, -1)
        .astype(jnp.bfloat16)
    )
    kernel_part = lax.dot_general(
        group_delta.reshape(groups, GW, -1), act_taps, grouped_nt, preferred_element_type=jnp.float32
    )
    first_delta = (inner_grad.astype(jnp.float32) * silu_slope(first_pre)).astype(jnp.bfloat16)
    first_part = lax.dot_general(
        flattened, first_delta, contract_tail, preferred_element_type=jnp.float32
    )
    volume_grad = (
        (
            third_delta.astype(jnp.float32)
            + jnp.dot(first_weight, first_delta, preferred_element_type=jnp.float32)
        )
        .astype(jnp.bfloat16)
        .reshape(volume.shape)
    )
    grp_count, sub_count = lax.axis_size("grp"), lax.axis_size("sub")
    kernel_laid = kernel_part.reshape(grp_count, sub_count, -1).transpose(1, 0, 2)
    first_sum, third_sum, group_sum = tree_sum(
        [
            (first_part, ("sub", "grp"), ("sub", "grp")),
            (third_part, ("sub", "grp"), ("sub", "grp")),
            (kernel_laid, ("sub", "grp"), ("sub",)),
        ],
        ("sub", "grp"),
    )
    first_grad = first_sum.reshape(first_part.shape) * factor
    third_grad = third_sum.reshape(third_part.shape) * factor
    group_grad = group_sum.reshape(channels // grp_count, GW, 3, 3, 3) * factor
    return (block_output, volume_grad, first_grad, group_grad, third_grad)


def solution(mesh):
    in_specs = (
        P(None, ("rep", "grp"), "sub", None),
        P(None, ("rep", "grp"), "sub", None),
        P(),
        P(),
        P(),
    )
    out_specs = (
        P(None, ("rep", "grp"), "sub", None),
        P(None, ("rep", "grp"), "sub", None),
        P("rep", None),
        P(("rep", "grp"), None, None, None, None),
        P("rep", None),
    )
    return jax.shard_map(
        per_device, mesh=mesh, in_specs=in_specs, out_specs=out_specs, check_vma=False
    )
```

```python
import functools
import itertools
import math

import jax
import jax.numpy as jnp
from jax import lax
from jax.experimental import pallas as pl
from jax.experimental.pallas import tpu as pltpu
from jax.sharding import PartitionSpec as P

GW = 8
LANES = 128
TAPS_PER_BLOCK = 16


def shift_lanes(block, offset):
    lane = lax.broadcasted_iota(jnp.int32, block.shape, 1)
    rolled = pltpu.roll(block, (-offset) % LANES, 1)
    edge = LANES - 1 if offset > 0 else 0
    return jnp.where(lane == edge, jnp.zeros_like(rolled), rolled)


def conv_body(ext_ref, w_ref, out_ref):
    height, channels = out_ref.shape[0], out_ref.shape[1]
    for y in range(height):
        parts = None
        for dz, dy in itertools.product(range(3), repeat=2):
            product = jnp.dot(
                w_ref[dz * 3 + dy], ext_ref[dz, y + dy], preferred_element_type=jnp.float32
            )
            parts = product if parts is None else parts + product
        out_ref[y] = (
            parts[channels : 2 * channels]
            + shift_lanes(parts[:channels], -1)
            + shift_lanes(parts[2 * channels :], 1)
        )


def conv_call(ext, weights):
    _, rows, channels, width = ext.shape
    height = rows - 2
    return pl.pallas_call(
        conv_body,
        out_shape=jax.ShapeDtypeStruct((height, channels, width), jnp.float32),
        in_specs=[pl.BlockSpec(memory_space=pltpu.VMEM)] * 2,
        out_specs=pl.BlockSpec(memory_space=pltpu.VMEM),
        cost_estimate=pl.CostEstimate(
            flops=2 * 27 * channels * channels * height * width,
            transcendentals=0,
            bytes_accessed=ext.size * 2 + weights.size * 2 + height * channels * width * 4,
        ),
    )(ext, weights)


def wgrad_body(act_ref, delta_ref, mask_ref, sel_ref, out_ref):
    height, channels = delta_ref.shape[0], delta_ref.shape[1]
    stacked = []
    for y in range(height):
        row = delta_ref[y].astype(jnp.float32)
        stacked.append(
            jnp.concatenate([shift_lanes(row, 1), row, shift_lanes(row, -1)], axis=0).astype(
                jnp.bfloat16
            )
        )
    mask = mask_ref[...]
    totals = [jnp.zeros((channels, LANES), jnp.float32) for _ in range(out_ref.shape[0])]
    for dz, dy in itertools.product(range(3), repeat=2):
        grads = None
        for y in range(height):
            term = lax.dot_general(
                stacked[y],
                act_ref[dz, y + dy],
                (((1,), (1,)), ((), ())),
                preferred_element_type=jnp.float32,
            )
            grads = term if grads is None else grads + term
        for dx in range(3):
            tap = dz * 9 + dy * 3 + dx
            picked = grads[dx * channels : (dx + 1) * channels] * mask
            folded = picked[:, :LANES]
            for start in range(LANES, channels, LANES):
                folded = folded + picked[:, start : start + LANES]
            high = folded.astype(jnp.bfloat16)
            low = (folded - high.astype(jnp.float32)).astype(jnp.bfloat16)
            sel = sel_ref[tap % TAPS_PER_BLOCK]
            totals[tap // TAPS_PER_BLOCK] += jnp.dot(
                high, sel, preferred_element_type=jnp.float32
            ) + jnp.dot(low, sel, preferred_element_type=jnp.float32)
    for n, total in enumerate(totals):
        out_ref[n] = total


def wgrad_call(act_ext, delta):
    height, channels, width = delta.shape
    blocks = -(-27 // TAPS_PER_BLOCK)
    group_of = jnp.arange(channels) // GW
    mask = (group_of[:, None] == group_of[None, :]).astype(jnp.float32)
    lane = jnp.arange(LANES)
    sel = (
        lane[None, None, :] == jnp.arange(TAPS_PER_BLOCK)[:, None, None] * GW + (lane % GW)[None, :, None]
    ).astype(jnp.bfloat16)
    out = pl.pallas_call(
        wgrad_body,
        out_shape=jax.ShapeDtypeStruct((blocks, channels, LANES), jnp.float32),
        in_specs=[pl.BlockSpec(memory_space=pltpu.VMEM)] * 4,
        out_specs=pl.BlockSpec(memory_space=pltpu.VMEM),
        cost_estimate=pl.CostEstimate(
            flops=2 * 27 * channels * channels * height * width + 4 * 27 * channels * LANES * LANES,
            transcendentals=0,
            bytes_accessed=act_ext.size * 2 + delta.size * 2 + blocks * channels * LANES * 4,
        ),
    )(act_ext, delta, mask, sel)
    return out.transpose(1, 0, 2).reshape(channels, blocks * LANES)[:, : 27 * GW]


def tree_sum(blocks, order):
    steps = []
    for axis in order:
        bit = lax.axis_size(axis) // 2
        while bit >= 1:
            steps.append((axis, bit))
            bit //= 2
    pieces = [block.reshape(-1) for block, _, _ in blocks]
    done = []
    for axis, bit in steps:
        pairs = [(i, i ^ bit) for i in range(lax.axis_size(axis))]
        upper = (lax.axis_index(axis) & bit) != 0
        members = [n for n, (_, axes, _) in enumerate(blocks) if axis in axes]
        keeps, sends = [], []
        for n in members:
            half = pieces[n].shape[0] // 2
            low, high = pieces[n][:half], pieces[n][half:]
            keeps.append(jnp.where(upper, high, low))
            sends.append(jnp.where(upper, low, high))
        got = lax.ppermute(jnp.concatenate(sends), axis, pairs)
        offset = 0
        for n, keep in zip(members, keeps):
            pieces[n] = keep + got[offset : offset + keep.shape[0]]
            offset += keep.shape[0]
        done.append((axis, pairs, upper))
    for axis, pairs, upper in reversed(done):
        members = [n for n, (_, _, axes) in enumerate(blocks) if axis in axes]
        if not members:
            continue
        got = lax.ppermute(jnp.concatenate([pieces[n] for n in members]), axis, pairs)
        offset = 0
        for n in members:
            size = pieces[n].shape[0]
            other = got[offset : offset + size]
            offset += size
            pieces[n] = jnp.where(
                upper,
                jnp.concatenate([other, pieces[n]]),
                jnp.concatenate([pieces[n], other]),
            )
    return pieces


def halo(block):
    for axis, dim in (("grp", 0), ("sub", 1)):
        count = lax.axis_size(axis)
        up = [(i, i + 1) for i in range(count - 1)]
        down = [(i + 1, i) for i in range(count - 1)]
        size = block.shape[dim]
        low = lax.ppermute(lax.slice_in_dim(block, size - 1, size, axis=dim), axis, up)
        high = lax.ppermute(lax.slice_in_dim(block, 0, 1, axis=dim), axis, down)
        block = jnp.concatenate([low, block, high], axis=dim)
    return block


def silu_slope(values):
    sigma = jax.nn.sigmoid(values)
    return sigma * (1.0 + values * (1.0 - sigma))


def conv_weights(group_weight):
    channels = group_weight.shape[0]
    tiled = jnp.tile(group_weight, (1, channels // GW, 1, 1, 1))
    group_of = jnp.arange(channels) // GW
    mask = (group_of[:, None] == group_of[None, :]).astype(group_weight.dtype)
    dense = tiled * mask[:, :, None, None, None]
    forward = dense.transpose(2, 3, 4, 0, 1).reshape(9, 3 * channels, channels)
    backward = dense[:, :, ::-1, ::-1, ::-1].transpose(2, 3, 4, 1, 0).reshape(9, 3 * channels, channels)
    return forward, backward


def per_device(volume, cotangent, first_weight, group_weight, third_weight):
    channels, depth, height, width = volume.shape
    flattened = volume.reshape(channels, -1)
    contract_lead = (((0,), (0,)), ((), ()))
    contract_tail = (((1,), (1,)), ((), ()))
    total_cells = depth * lax.axis_size("grp") * height * lax.axis_size("sub") * width
    factor = 1.0 / math.sqrt(total_cells)

    def to_rows(block):
        return block.reshape(channels, depth, height, width).transpose(1, 2, 0, 3)

    def from_rows(block):
        return block.transpose(1, 0, 2).reshape(channels, -1)

    forward_kernel, backward_kernel = conv_weights(group_weight)
    first_pre = lax.dot_general(
        first_weight, flattened, contract_lead, preferred_element_type=jnp.float32
    )
    first_act = jax.nn.silu(first_pre).astype(jnp.bfloat16)
    act_ext = halo(to_rows(first_act))
    group_pre = conv_call(act_ext, forward_kernel)
    group_act = jax.nn.silu(group_pre).astype(jnp.bfloat16)
    act_flat = from_rows(group_act)
    summed = flattened.astype(jnp.float32) + lax.dot_general(
        third_weight, act_flat, contract_lead, preferred_element_type=jnp.float32
    )
    block_output = jax.nn.silu(summed).astype(jnp.bfloat16).reshape(volume.shape)
    third_delta = (cotangent.reshape(channels, -1).astype(jnp.float32) * silu_slope(summed)).astype(
        jnp.bfloat16
    )
    third_part = lax.dot_general(
        act_flat, third_delta, contract_tail, preferred_element_type=jnp.float32
    )
    hidden_grad = jnp.dot(third_weight, third_delta, preferred_element_type=jnp.float32).astype(
        jnp.bfloat16
    )
    group_delta = (
        to_rows(hidden_grad)[0].astype(jnp.float32) * silu_slope(group_pre)
    ).astype(jnp.bfloat16)
    delta_ext = halo(group_delta[None])
    inner_grad = from_rows(conv_call(delta_ext, backward_kernel).astype(jnp.bfloat16))
    kernel_part = wgrad_call(act_ext, group_delta)
    first_delta = (inner_grad.astype(jnp.float32) * silu_slope(first_pre)).astype(jnp.bfloat16)
    first_part = lax.dot_general(
        flattened, first_delta, contract_tail, preferred_element_type=jnp.float32
    )
    volume_grad = (
        (
            third_delta.astype(jnp.float32)
            + jnp.dot(first_weight, first_delta, preferred_element_type=jnp.float32)
        )
        .astype(jnp.bfloat16)
        .reshape(volume.shape)
    )
    grp_count, sub_count = lax.axis_size("grp"), lax.axis_size("sub")
    kernel_laid = kernel_part.reshape(grp_count, sub_count, -1).transpose(1, 0, 2)
    first_sum, third_sum, group_sum = tree_sum(
        [
            (first_part, ("sub", "grp"), ("sub", "grp")),
            (third_part, ("sub", "grp"), ("sub", "grp")),
            (kernel_laid, ("sub", "grp"), ("sub",)),
        ],
        ("sub", "grp"),
    )
    first_grad = first_sum.reshape(first_part.shape) * factor
    third_grad = third_sum.reshape(third_part.shape) * factor
    own_rows = channels // grp_count
    group_grad = (
        group_sum.reshape(own_rows, 27, GW).transpose(0, 2, 1).reshape(own_rows, GW, 3, 3, 3) * factor
    )
    return (block_output, volume_grad, first_grad, group_grad, third_grad)


def solution(mesh):
    in_specs = (
        P(None, ("rep", "grp"), "sub", None),
        P(None, ("rep", "grp"), "sub", None),
        P(),
        P(),
        P(),
    )
    out_specs = (
        P(None, ("rep", "grp"), "sub", None),
        P(None, ("rep", "grp"), "sub", None),
        P("rep", None),
        P(("rep", "grp"), None, None, None, None),
        P("rep", None),
    )
    return jax.shard_map(
        per_device, mesh=mesh, in_specs=in_specs, out_specs=out_specs, check_vma=False
    )
```

```python
import functools
import itertools
import math

import jax
import jax.numpy as jnp
from jax import lax
from jax.experimental import pallas as pl
from jax.experimental.pallas import tpu as pltpu
from jax.sharding import PartitionSpec as P

GW = 8
LANES = 128
TAPS_PER_BLOCK = 16


def shift_lanes(block, offset):
    lane = lax.broadcasted_iota(jnp.int32, block.shape, 1)
    rolled = pltpu.roll(block, (-offset) % LANES, 1)
    edge = LANES - 1 if offset > 0 else 0
    return jnp.where(lane == edge, jnp.zeros_like(rolled), rolled)


def conv_body(ext_ref, w_ref, out_ref):
    height, channels = out_ref.shape[0], out_ref.shape[1]
    for y in range(height):
        parts = None
        for dz, dy in itertools.product(range(3), repeat=2):
            product = jnp.dot(
                w_ref[dz * 3 + dy], ext_ref[dz, y + dy], preferred_element_type=jnp.float32
            )
            parts = product if parts is None else parts + product
        out_ref[y] = (
            parts[channels : 2 * channels]
            + shift_lanes(parts[:channels], -1)
            + shift_lanes(parts[2 * channels :], 1)
        )


def conv_call(ext, weights):
    _, rows, channels, width = ext.shape
    height = rows - 2
    return pl.pallas_call(
        conv_body,
        out_shape=jax.ShapeDtypeStruct((height, channels, width), jnp.float32),
        in_specs=[pl.BlockSpec(memory_space=pltpu.VMEM)] * 2,
        out_specs=pl.BlockSpec(memory_space=pltpu.VMEM),
        cost_estimate=pl.CostEstimate(
            flops=2 * 27 * channels * channels * height * width,
            transcendentals=0,
            bytes_accessed=ext.size * 2 + weights.size * 2 + height * channels * width * 4,
        ),
    )(ext, weights)


def wgrad_body(act_ref, delta_ref, mask_ref, sel_ref, out_ref):
    height, channels = delta_ref.shape[0], delta_ref.shape[1]
    stacked = []
    for y in range(height):
        row = delta_ref[y].astype(jnp.float32)
        stacked.append(
            jnp.concatenate([shift_lanes(row, 1), row, shift_lanes(row, -1)], axis=0).astype(
                jnp.bfloat16
            )
        )
    mask = mask_ref[...]
    totals = [jnp.zeros((channels, LANES), jnp.float32) for _ in range(out_ref.shape[0])]
    for dz, dy in itertools.product(range(3), repeat=2):
        grads = None
        for y in range(height):
            term = lax.dot_general(
                stacked[y],
                act_ref[dz, y + dy],
                (((1,), (1,)), ((), ())),
                preferred_element_type=jnp.float32,
            )
            grads = term if grads is None else grads + term
        for dx in range(3):
            tap = dz * 9 + dy * 3 + dx
            picked = grads[dx * channels : (dx + 1) * channels] * mask
            folded = picked[:, :LANES]
            for start in range(LANES, channels, LANES):
                folded = folded + picked[:, start : start + LANES]
            high = folded.astype(jnp.bfloat16)
            low = (folded - high.astype(jnp.float32)).astype(jnp.bfloat16)
            sel = sel_ref[tap % TAPS_PER_BLOCK]
            totals[tap // TAPS_PER_BLOCK] += jnp.dot(
                high, sel, preferred_element_type=jnp.float32
            ) + jnp.dot(low, sel, preferred_element_type=jnp.float32)
    for n, total in enumerate(totals):
        out_ref[n] = total


def wgrad_call(act_ext, delta):
    height, channels, width = delta.shape
    blocks = -(-27 // TAPS_PER_BLOCK)
    group_of = jnp.arange(channels) // GW
    mask = (group_of[:, None] == group_of[None, :]).astype(jnp.float32)
    lane = jnp.arange(LANES)
    sel = (
        lane[None, None, :] == jnp.arange(TAPS_PER_BLOCK)[:, None, None] * GW + (lane % GW)[None, :, None]
    ).astype(jnp.bfloat16)
    out = pl.pallas_call(
        wgrad_body,
        out_shape=jax.ShapeDtypeStruct((blocks, channels, LANES), jnp.float32),
        in_specs=[pl.BlockSpec(memory_space=pltpu.VMEM)] * 4,
        out_specs=pl.BlockSpec(memory_space=pltpu.VMEM),
        cost_estimate=pl.CostEstimate(
            flops=2 * 27 * channels * channels * height * width + 4 * 27 * channels * LANES * LANES,
            transcendentals=0,
            bytes_accessed=act_ext.size * 2 + delta.size * 2 + blocks * channels * LANES * 4,
        ),
    )(act_ext, delta, mask, sel)
    return out.transpose(1, 0, 2).reshape(channels, blocks * LANES)[:, : 27 * GW]


def tree_sum(blocks, order):
    steps = []
    for axis, rising in order:
        bits = []
        bit = 1
        while bit < lax.axis_size(axis):
            bits.append(bit)
            bit *= 2
        steps += [(axis, bit) for bit in (bits if rising else bits[::-1])]
    pieces = [block.reshape(-1) for block, _, _ in blocks]
    done = []
    for axis, bit in steps:
        pairs = [(i, i ^ bit) for i in range(lax.axis_size(axis))]
        upper = (lax.axis_index(axis) & bit) != 0
        members = [n for n, (_, axes, _) in enumerate(blocks) if axis in axes]
        keeps, sends = [], []
        for n in members:
            half = pieces[n].shape[0] // 2
            low, high = pieces[n][:half], pieces[n][half:]
            keeps.append(jnp.where(upper, high, low))
            sends.append(jnp.where(upper, low, high))
        got = lax.ppermute(jnp.concatenate(sends), axis, pairs)
        offset = 0
        for n, keep in zip(members, keeps):
            pieces[n] = keep + got[offset : offset + keep.shape[0]]
            offset += keep.shape[0]
        done.append((axis, pairs, upper))
    for axis, pairs, upper in reversed(done):
        members = [n for n, (_, _, axes) in enumerate(blocks) if axis in axes]
        if not members:
            continue
        got = lax.ppermute(jnp.concatenate([pieces[n] for n in members]), axis, pairs)
        offset = 0
        for n in members:
            size = pieces[n].shape[0]
            other = got[offset : offset + size]
            offset += size
            pieces[n] = jnp.where(
                upper,
                jnp.concatenate([other, pieces[n]]),
                jnp.concatenate([pieces[n], other]),
            )
    return pieces


def halo(block):
    for axis, dim in (("grp", 0), ("sub", 1)):
        count = lax.axis_size(axis)
        up = [(i, i + 1) for i in range(count - 1)]
        down = [(i + 1, i) for i in range(count - 1)]
        size = block.shape[dim]
        low = lax.ppermute(lax.slice_in_dim(block, size - 1, size, axis=dim), axis, up)
        high = lax.ppermute(lax.slice_in_dim(block, 0, 1, axis=dim), axis, down)
        block = jnp.concatenate([low, block, high], axis=dim)
    return block


def silu_slope(values):
    sigma = jax.nn.sigmoid(values)
    return sigma * (1.0 + values * (1.0 - sigma))


def conv_weights(group_weight):
    channels = group_weight.shape[0]
    group_of = jnp.arange(channels) // GW
    mask = (group_of[:, None] == group_of[None, :]).astype(group_weight.dtype)
    compact = group_weight.reshape(channels, GW, 27)
    forward = jnp.broadcast_to(
        compact.transpose(2, 0, 1)[:, :, None, :], (27, channels, channels // GW, GW)
    ).reshape(27, channels, channels)
    backward = jnp.broadcast_to(
        compact[:, :, ::-1].transpose(2, 1, 0)[:, None, :, :], (27, channels // GW, GW, channels)
    ).reshape(27, channels, channels)
    forward = (forward * mask).reshape(9, 3 * channels, channels)
    backward = (backward * mask).reshape(9, 3 * channels, channels)
    return forward, backward


def rounded(values):
    return lax.reduce_precision(values, exponent_bits=8, mantissa_bits=7).astype(jnp.bfloat16)


def per_device(volume, cotangent, first_weight, group_weight, third_weight):
    channels, depth, height, width = volume.shape
    flattened = volume.reshape(channels, -1)
    contract_lead = (((0,), (0,)), ((), ()))
    contract_tail = (((1,), (1,)), ((), ()))
    total_cells = depth * lax.axis_size("grp") * height * lax.axis_size("sub") * width
    factor = 1.0 / math.sqrt(total_cells)

    def to_rows(block):
        return block.reshape(channels, depth, height, width).transpose(1, 2, 0, 3)

    def from_rows(block):
        return block.transpose(1, 0, 2).reshape(channels, -1)

    forward_kernel, backward_kernel = conv_weights(group_weight)
    first_pre = lax.dot_general(
        first_weight, flattened, contract_lead, preferred_element_type=jnp.float32
    )
    first_act = rounded(jax.nn.silu(first_pre))
    act_ext = halo(to_rows(first_act))
    group_pre = conv_call(act_ext, forward_kernel)
    group_act = rounded(jax.nn.silu(group_pre))
    act_flat = from_rows(group_act)
    summed = flattened.astype(jnp.float32) + lax.dot_general(
        third_weight, act_flat, contract_lead, preferred_element_type=jnp.float32
    )
    block_output = jax.nn.silu(summed).astype(jnp.bfloat16).reshape(volume.shape)
    third_delta = rounded(cotangent.reshape(channels, -1).astype(jnp.float32) * silu_slope(summed))
    third_part = lax.dot_general(
        act_flat, third_delta, contract_tail, preferred_element_type=jnp.float32
    )
    hidden_grad = rounded(jnp.dot(third_weight, third_delta, preferred_element_type=jnp.float32))
    group_delta = rounded(to_rows(hidden_grad)[0].astype(jnp.float32) * silu_slope(group_pre))
    delta_ext = halo(group_delta[None])
    inner_grad = from_rows(rounded(conv_call(delta_ext, backward_kernel)))
    kernel_part = wgrad_call(act_ext, group_delta)
    first_delta = rounded(inner_grad.astype(jnp.float32) * silu_slope(first_pre))
    first_part = lax.dot_general(
        flattened, first_delta, contract_tail, preferred_element_type=jnp.float32
    )
    volume_grad = (
        (
            third_delta.astype(jnp.float32)
            + jnp.dot(first_weight, first_delta, preferred_element_type=jnp.float32)
        )
        .astype(jnp.bfloat16)
        .reshape(volume.shape)
    )
    grp_count, sub_count = lax.axis_size("grp"), lax.axis_size("sub")
    kernel_laid = kernel_part.reshape(grp_count, sub_count, -1).transpose(1, 0, 2)
    first_sum, third_sum, group_sum = tree_sum(
        [
            (first_part, ("sub", "grp"), ("sub", "grp")),
            (third_part, ("sub", "grp"), ("sub", "grp")),
            (kernel_laid, ("sub", "grp"), ("sub",)),
        ],
        (("sub", True), ("grp", False)),
    )
    first_grad = first_sum.reshape(first_part.shape) * factor
    third_grad = third_sum.reshape(third_part.shape) * factor
    own_rows = channels // grp_count
    group_grad = (
        group_sum.reshape(own_rows, 27, GW).transpose(0, 2, 1).reshape(own_rows, GW, 3, 3, 3) * factor
    )
    return (block_output, volume_grad, first_grad, group_grad, third_grad)


def solution(mesh):
    in_specs = (
        P(None, ("rep", "grp"), "sub", None),
        P(None, ("rep", "grp"), "sub", None),
        P(),
        P(),
        P(),
    )
    out_specs = (
        P(None, ("rep", "grp"), "sub", None),
        P(None, ("rep", "grp"), "sub", None),
        P("rep", None),
        P(("rep", "grp"), None, None, None, None),
        P("rep", None),
    )
    return jax.shard_map(
        per_device, mesh=mesh, in_specs=in_specs, out_specs=out_specs, check_vma=False
    )
```

```python
import functools
import itertools
import math

import jax
import jax.numpy as jnp
from jax import lax
from jax.experimental import pallas as pl
from jax.experimental.pallas import tpu as pltpu
from jax.sharding import PartitionSpec as P

GW = 8
LANES = 128
TAPS_PER_BLOCK = 16


def shift_lanes(block, offset):
    lane = lax.broadcasted_iota(jnp.int32, block.shape, 1)
    rolled = pltpu.roll(block, (-offset) % LANES, 1)
    edge = LANES - 1 if offset > 0 else 0
    return jnp.where(lane == edge, jnp.zeros_like(rolled), rolled)


def conv_body(ext_ref, w_ref, out_ref):
    height, channels = out_ref.shape[0], out_ref.shape[1]
    for y in range(height):
        parts = None
        for dz, dy in itertools.product(range(3), repeat=2):
            product = jnp.dot(
                w_ref[dz * 3 + dy], ext_ref[dz, y + dy], preferred_element_type=jnp.float32
            )
            parts = product if parts is None else parts + product
        out_ref[y] = (
            parts[channels : 2 * channels]
            + shift_lanes(parts[:channels], -1)
            + shift_lanes(parts[2 * channels :], 1)
        )


def conv_call(ext, weights):
    _, rows, channels, width = ext.shape
    height = rows - 2
    return pl.pallas_call(
        conv_body,
        out_shape=jax.ShapeDtypeStruct((height, channels, width), jnp.float32),
        in_specs=[pl.BlockSpec(memory_space=pltpu.VMEM)] * 2,
        out_specs=pl.BlockSpec(memory_space=pltpu.VMEM),
        cost_estimate=pl.CostEstimate(
            flops=2 * 27 * channels * channels * height * width,
            transcendentals=0,
            bytes_accessed=ext.size * 2 + weights.size * 2 + height * channels * width * 4,
        ),
    )(ext, weights)


def wgrad_body(act_ref, delta_ref, mask_ref, sel_ref, out_ref):
    height, channels = delta_ref.shape[0], delta_ref.shape[1]
    stacked = []
    for y in range(height):
        row = delta_ref[y].astype(jnp.float32)
        stacked.append(
            jnp.concatenate([shift_lanes(row, 1), row, shift_lanes(row, -1)], axis=0).astype(
                jnp.bfloat16
            )
        )
    mask = mask_ref[...]
    totals = [jnp.zeros((channels, LANES), jnp.float32) for _ in range(out_ref.shape[0])]
    for dz, dy in itertools.product(range(3), repeat=2):
        grads = None
        for y in range(height):
            term = lax.dot_general(
                stacked[y],
                act_ref[dz, y + dy],
                (((1,), (1,)), ((), ())),
                preferred_element_type=jnp.float32,
            )
            grads = term if grads is None else grads + term
        for dx in range(3):
            tap = dz * 9 + dy * 3 + dx
            picked = grads[dx * channels : (dx + 1) * channels] * mask
            folded = picked[:, :LANES]
            for start in range(LANES, channels, LANES):
                folded = folded + picked[:, start : start + LANES]
            high = folded.astype(jnp.bfloat16)
            low = (folded - high.astype(jnp.float32)).astype(jnp.bfloat16)
            sel = sel_ref[tap % TAPS_PER_BLOCK]
            totals[tap // TAPS_PER_BLOCK] += jnp.dot(
                high, sel, preferred_element_type=jnp.float32
            ) + jnp.dot(low, sel, preferred_element_type=jnp.float32)
    for n, total in enumerate(totals):
        out_ref[n] = total


def wgrad_call(act_ext, delta):
    height, channels, width = delta.shape
    blocks = -(-27 // TAPS_PER_BLOCK)
    group_of = jnp.arange(channels) // GW
    mask = (group_of[:, None] == group_of[None, :]).astype(jnp.float32)
    lane = jnp.arange(LANES)
    sel = (
        lane[None, None, :] == jnp.arange(TAPS_PER_BLOCK)[:, None, None] * GW + (lane % GW)[None, :, None]
    ).astype(jnp.bfloat16)
    out = pl.pallas_call(
        wgrad_body,
        out_shape=jax.ShapeDtypeStruct((blocks, channels, LANES), jnp.float32),
        in_specs=[pl.BlockSpec(memory_space=pltpu.VMEM)] * 4,
        out_specs=pl.BlockSpec(memory_space=pltpu.VMEM),
        cost_estimate=pl.CostEstimate(
            flops=2 * 27 * channels * channels * height * width + 4 * 27 * channels * LANES * LANES,
            transcendentals=0,
            bytes_accessed=act_ext.size * 2 + delta.size * 2 + blocks * channels * LANES * 4,
        ),
    )(act_ext, delta, mask, sel)
    return out.transpose(1, 0, 2).reshape(channels, blocks * LANES)[:, : 27 * GW]


def all_sum(flat):
    first = [(i, i ^ 1) for i in range(lax.axis_size("sub"))]
    upper = (lax.axis_index("sub") & 1) != 0
    half = flat.shape[0] // 2
    low, high = flat[:half], flat[half:]
    piece = jnp.where(upper, high, low) + lax.ppermute(jnp.where(upper, low, high), "sub", first)
    for axis, start in (("sub", 2), ("grp", 1)):
        bit = start
        while bit < lax.axis_size(axis):
            pairs = [(i, i ^ bit) for i in range(lax.axis_size(axis))]
            piece = piece + lax.ppermute(piece, axis, pairs)
            bit *= 2
    other = lax.ppermute(piece, "sub", first)
    return jnp.where(upper, jnp.concatenate([other, piece]), jnp.concatenate([piece, other]))


def halo(block):
    for axis, dim in (("grp", 0), ("sub", 1)):
        count = lax.axis_size(axis)
        up = [(i, i + 1) for i in range(count - 1)]
        down = [(i + 1, i) for i in range(count - 1)]
        size = block.shape[dim]
        low = lax.ppermute(lax.slice_in_dim(block, size - 1, size, axis=dim), axis, up)
        high = lax.ppermute(lax.slice_in_dim(block, 0, 1, axis=dim), axis, down)
        block = jnp.concatenate([low, block, high], axis=dim)
    return block


def silu_slope(values):
    sigma = jax.nn.sigmoid(values)
    return sigma * (1.0 + values * (1.0 - sigma))


def conv_weights(group_weight):
    channels = group_weight.shape[0]
    group_of = jnp.arange(channels) // GW
    mask = (group_of[:, None] == group_of[None, :]).astype(jnp.float32)
    spread = (jnp.arange(GW)[:, None] == jnp.arange(channels)[None, :] % GW).astype(jnp.float32)
    compact = group_weight.reshape(channels, GW, 27).astype(jnp.float32)
    forward = jnp.einsum("ojt,ji->toi", compact, spread)
    backward = jnp.einsum("ji,ojt->tio", spread, compact[:, :, ::-1])
    forward = (forward * mask).astype(group_weight.dtype).reshape(9, 3 * channels, channels)
    backward = (backward * mask).astype(group_weight.dtype).reshape(9, 3 * channels, channels)
    return forward, backward


def rounded(values):
    return lax.reduce_precision(values, exponent_bits=8, mantissa_bits=7).astype(jnp.bfloat16)


def per_device(volume, cotangent, first_weight, group_weight, third_weight):
    channels, depth, height, width = volume.shape
    flattened = volume.reshape(channels, -1)
    contract_lead = (((0,), (0,)), ((), ()))
    contract_tail = (((1,), (1,)), ((), ()))
    total_cells = depth * lax.axis_size("grp") * height * lax.axis_size("sub") * width
    factor = 1.0 / math.sqrt(total_cells)

    def to_rows(block):
        return block.reshape(channels, depth, height, width).transpose(1, 2, 0, 3)

    def from_rows(block):
        return block.transpose(1, 0, 2).reshape(channels, -1)

    forward_kernel, backward_kernel = conv_weights(group_weight)
    first_pre = lax.dot_general(
        first_weight, flattened, contract_lead, preferred_element_type=jnp.float32
    )
    first_act = rounded(jax.nn.silu(first_pre))
    act_ext = halo(to_rows(first_act))
    group_pre = conv_call(act_ext, forward_kernel)
    group_act = rounded(jax.nn.silu(group_pre))
    act_flat = from_rows(group_act)
    summed = flattened.astype(jnp.float32) + lax.dot_general(
        third_weight, act_flat, contract_lead, preferred_element_type=jnp.float32
    )
    block_output = jax.nn.silu(summed).astype(jnp.bfloat16).reshape(volume.shape)
    third_delta = rounded(cotangent.reshape(channels, -1).astype(jnp.float32) * silu_slope(summed))
    third_part = lax.dot_general(
        act_flat, third_delta, contract_tail, preferred_element_type=jnp.float32
    )
    hidden_grad = rounded(jnp.dot(third_weight, third_delta, preferred_element_type=jnp.float32))
    group_delta = rounded(to_rows(hidden_grad)[0].astype(jnp.float32) * silu_slope(group_pre))
    delta_ext = halo(group_delta[None])
    inner_grad = from_rows(rounded(conv_call(delta_ext, backward_kernel)))
    kernel_part = wgrad_call(act_ext, group_delta)
    first_delta = rounded(inner_grad.astype(jnp.float32) * silu_slope(first_pre))
    first_part = lax.dot_general(
        flattened, first_delta, contract_tail, preferred_element_type=jnp.float32
    )
    volume_grad = (
        (
            third_delta.astype(jnp.float32)
            + jnp.dot(first_weight, first_delta, preferred_element_type=jnp.float32)
        )
        .astype(jnp.bfloat16)
        .reshape(volume.shape)
    )
    total = all_sum(
        jnp.concatenate([first_part.reshape(-1), third_part.reshape(-1), kernel_part.reshape(-1)])
    )
    square = first_part.size
    first_grad = total[:square].reshape(first_part.shape) * factor
    third_grad = total[square : 2 * square].reshape(third_part.shape) * factor
    own_rows = channels // lax.axis_size("grp")
    own = lax.dynamic_slice_in_dim(
        total[2 * square :].reshape(channels, -1), lax.axis_index("grp") * own_rows, own_rows, 0
    )
    group_grad = own.reshape(own_rows, 27, GW).transpose(0, 2, 1).reshape(own_rows, GW, 3, 3, 3) * factor
    return (block_output, volume_grad, first_grad, group_grad, third_grad)


def solution(mesh):
    in_specs = (
        P(None, ("rep", "grp"), "sub", None),
        P(None, ("rep", "grp"), "sub", None),
        P(),
        P(),
        P(),
    )
    out_specs = (
        P(None, ("rep", "grp"), "sub", None),
        P(None, ("rep", "grp"), "sub", None),
        P("rep", None),
        P(("rep", "grp"), None, None, None, None),
        P("rep", None),
    )
    return jax.shard_map(
        per_device, mesh=mesh, in_specs=in_specs, out_specs=out_specs, check_vma=False
    )
```

```python
import functools
import itertools
import math

import jax
import jax.numpy as jnp
from jax import lax
from jax.experimental import pallas as pl
from jax.experimental.pallas import tpu as pltpu
from jax.sharding import PartitionSpec as P

GW = 8
LANES = 128
TAPS_PER_BLOCK = 16


def shift_lanes(block, offset):
    lane = lax.broadcasted_iota(jnp.int32, block.shape, 1)
    rolled = pltpu.roll(block, (-offset) % LANES, 1)
    edge = LANES - 1 if offset > 0 else 0
    return jnp.where(lane == edge, jnp.zeros_like(rolled), rolled)


def conv_body(ext_ref, w_ref, out_ref):
    height, channels = out_ref.shape[0], out_ref.shape[1]
    for y in range(height):
        parts = None
        for dz, dy in itertools.product(range(3), repeat=2):
            product = jnp.dot(
                w_ref[dz * 3 + dy], ext_ref[dz, y + dy], preferred_element_type=jnp.float32
            )
            parts = product if parts is None else parts + product
        out_ref[y] = (
            parts[channels : 2 * channels]
            + shift_lanes(parts[:channels], -1)
            + shift_lanes(parts[2 * channels :], 1)
        )


def conv_call(ext, weights):
    _, rows, channels, width = ext.shape
    height = rows - 2
    return pl.pallas_call(
        conv_body,
        out_shape=jax.ShapeDtypeStruct((height, channels, width), jnp.float32),
        in_specs=[pl.BlockSpec(memory_space=pltpu.VMEM)] * 2,
        out_specs=pl.BlockSpec(memory_space=pltpu.VMEM),
        cost_estimate=pl.CostEstimate(
            flops=2 * 27 * channels * channels * height * width,
            transcendentals=0,
            bytes_accessed=ext.size * 2 + weights.size * 2 + height * channels * width * 4,
        ),
    )(ext, weights)


def wgrad_body(act_ref, delta_ref, mask_ref, sel_ref, out_ref):
    height, channels = delta_ref.shape[0], delta_ref.shape[1]
    stacked = []
    for y in range(height):
        row = delta_ref[y].astype(jnp.float32)
        stacked.append(
            jnp.concatenate([shift_lanes(row, 1), row, shift_lanes(row, -1)], axis=0).astype(
                jnp.bfloat16
            )
        )
    mask = mask_ref[...]
    totals = [jnp.zeros((channels, LANES), jnp.float32) for _ in range(out_ref.shape[0])]
    for dz, dy in itertools.product(range(3), repeat=2):
        grads = None
        for y in range(height):
            term = lax.dot_general(
                stacked[y],
                act_ref[dz, y + dy],
                (((1,), (1,)), ((), ())),
                preferred_element_type=jnp.float32,
            )
            grads = term if grads is None else grads + term
        for dx in range(3):
            tap = dz * 9 + dy * 3 + dx
            picked = grads[dx * channels : (dx + 1) * channels] * mask
            folded = picked[:, :LANES]
            for start in range(LANES, channels, LANES):
                folded = folded + picked[:, start : start + LANES]
            high = folded.astype(jnp.bfloat16)
            low = (folded - high.astype(jnp.float32)).astype(jnp.bfloat16)
            sel = sel_ref[tap % TAPS_PER_BLOCK]
            totals[tap // TAPS_PER_BLOCK] += jnp.dot(
                high, sel, preferred_element_type=jnp.float32
            ) + jnp.dot(low, sel, preferred_element_type=jnp.float32)
    for n, total in enumerate(totals):
        out_ref[n] = total


def wgrad_call(act_ext, delta):
    height, channels, width = delta.shape
    blocks = -(-27 // TAPS_PER_BLOCK)
    group_of = jnp.arange(channels) // GW
    mask = (group_of[:, None] == group_of[None, :]).astype(jnp.float32)
    lane = jnp.arange(LANES)
    sel = (
        lane[None, None, :] == jnp.arange(TAPS_PER_BLOCK)[:, None, None] * GW + (lane % GW)[None, :, None]
    ).astype(jnp.bfloat16)
    out = pl.pallas_call(
        wgrad_body,
        out_shape=jax.ShapeDtypeStruct((blocks, channels, LANES), jnp.float32),
        in_specs=[pl.BlockSpec(memory_space=pltpu.VMEM)] * 4,
        out_specs=pl.BlockSpec(memory_space=pltpu.VMEM),
        cost_estimate=pl.CostEstimate(
            flops=2 * 27 * channels * channels * height * width + 4 * 27 * channels * LANES * LANES,
            transcendentals=0,
            bytes_accessed=act_ext.size * 2 + delta.size * 2 + blocks * channels * LANES * 4,
        ),
    )(act_ext, delta, mask, sel)
    return out.transpose(1, 0, 2).reshape(channels, blocks * LANES)[:, : 27 * GW]


def tree_sum(blocks, order):
    steps = []
    for axis, rising in order:
        bits = []
        bit = 1
        while bit < lax.axis_size(axis):
            bits.append(bit)
            bit *= 2
        steps += [(axis, bit) for bit in (bits if rising else bits[::-1])]
    pieces = [block.reshape(-1) for block, _, _ in blocks]
    done = []
    for axis, bit in steps:
        pairs = [(i, i ^ bit) for i in range(lax.axis_size(axis))]
        upper = (lax.axis_index(axis) & bit) != 0
        members = [n for n, (_, axes, _) in enumerate(blocks) if axis in axes]
        keeps, sends = [], []
        for n in members:
            half = pieces[n].shape[0] // 2
            low, high = pieces[n][:half], pieces[n][half:]
            keeps.append(jnp.where(upper, high, low))
            sends.append(jnp.where(upper, low, high))
        got = lax.ppermute(jnp.concatenate(sends), axis, pairs)
        offset = 0
        for n, keep in zip(members, keeps):
            pieces[n] = keep + got[offset : offset + keep.shape[0]]
            offset += keep.shape[0]
        done.append((axis, pairs, upper))
    for axis, pairs, upper in reversed(done):
        members = [n for n, (_, _, axes) in enumerate(blocks) if axis in axes]
        if not members:
            continue
        got = lax.ppermute(jnp.concatenate([pieces[n] for n in members]), axis, pairs)
        offset = 0
        for n in members:
            size = pieces[n].shape[0]
            other = got[offset : offset + size]
            offset += size
            pieces[n] = jnp.where(
                upper,
                jnp.concatenate([other, pieces[n]]),
                jnp.concatenate([pieces[n], other]),
            )
    return pieces


def halo(block):
    for axis, dim in (("grp", 0), ("sub", 1)):
        count = lax.axis_size(axis)
        up = [(i, i + 1) for i in range(count - 1)]
        down = [(i + 1, i) for i in range(count - 1)]
        size = block.shape[dim]
        low = lax.ppermute(lax.slice_in_dim(block, size - 1, size, axis=dim), axis, up)
        high = lax.ppermute(lax.slice_in_dim(block, 0, 1, axis=dim), axis, down)
        block = jnp.concatenate([low, block, high], axis=dim)
    return block


def silu_slope(values):
    sigma = jax.nn.sigmoid(values)
    return sigma * (1.0 + values * (1.0 - sigma))


def conv_weights(group_weight):
    channels = group_weight.shape[0]
    group_of = jnp.arange(channels) // GW
    mask = (group_of[:, None] == group_of[None, :]).astype(jnp.float32)
    spread = (jnp.arange(GW)[:, None] == jnp.arange(channels)[None, :] % GW).astype(jnp.float32)
    compact = group_weight.reshape(channels, GW, 27).astype(jnp.float32)
    forward = jnp.einsum("ojt,ji->toi", compact, spread)
    backward = jnp.einsum("ji,ojt->tio", spread, compact[:, :, ::-1])
    forward = (forward * mask).astype(group_weight.dtype).reshape(9, 3 * channels, channels)
    backward = (backward * mask).astype(group_weight.dtype).reshape(9, 3 * channels, channels)
    return forward, backward


def rounded(values):
    return lax.reduce_precision(values, exponent_bits=8, mantissa_bits=7).astype(jnp.bfloat16)


def per_device(volume, cotangent, first_weight, group_weight, third_weight):
    channels, depth, height, width = volume.shape
    flattened = volume.reshape(channels, -1)
    contract_lead = (((0,), (0,)), ((), ()))
    contract_tail = (((1,), (1,)), ((), ()))
    total_cells = depth * lax.axis_size("grp") * height * lax.axis_size("sub") * width
    factor = 1.0 / math.sqrt(total_cells)

    def to_rows(block):
        return block.reshape(channels, depth, height, width).transpose(1, 2, 0, 3)

    def from_rows(block):
        return block.transpose(1, 0, 2).reshape(channels, -1)

    forward_kernel, backward_kernel = conv_weights(group_weight)
    first_pre = lax.dot_general(
        first_weight, flattened, contract_lead, preferred_element_type=jnp.float32
    )
    first_act = rounded(jax.nn.silu(first_pre))
    act_ext = halo(to_rows(first_act))
    group_pre = conv_call(act_ext, forward_kernel)
    group_act = rounded(jax.nn.silu(group_pre))
    act_flat = from_rows(group_act)
    summed = flattened.astype(jnp.float32) + lax.dot_general(
        third_weight, act_flat, contract_lead, preferred_element_type=jnp.float32
    )
    block_output = jax.nn.silu(summed).astype(jnp.bfloat16).reshape(volume.shape)
    third_delta = rounded(cotangent.reshape(channels, -1).astype(jnp.float32) * silu_slope(summed))
    third_part = lax.dot_general(
        act_flat, third_delta, contract_tail, preferred_element_type=jnp.float32
    )
    hidden_grad = rounded(jnp.dot(third_weight, third_delta, preferred_element_type=jnp.float32))
    group_delta = rounded(to_rows(hidden_grad)[0].astype(jnp.float32) * silu_slope(group_pre))
    delta_ext = halo(group_delta[None])
    inner_grad = from_rows(rounded(conv_call(delta_ext, backward_kernel)))
    kernel_part = wgrad_call(act_ext, group_delta)
    first_delta = rounded(inner_grad.astype(jnp.float32) * silu_slope(first_pre))
    first_part = lax.dot_general(
        flattened, first_delta, contract_tail, preferred_element_type=jnp.float32
    )
    volume_grad = (
        (
            third_delta.astype(jnp.float32)
            + jnp.dot(first_weight, first_delta, preferred_element_type=jnp.float32)
        )
        .astype(jnp.bfloat16)
        .reshape(volume.shape)
    )
    grp_count, sub_count = lax.axis_size("grp"), lax.axis_size("sub")
    digits = grp_count.bit_length() - 1
    reverse = [int(format(n, f"0{digits}b")[::-1], 2) if digits else 0 for n in range(grp_count)]
    blocks = kernel_part.reshape(grp_count, sub_count, -1)
    kernel_laid = jnp.concatenate([blocks[n : n + 1] for n in reverse]).transpose(1, 0, 2)
    first_sum, third_sum, group_sum = tree_sum(
        [
            (first_part, ("sub", "grp"), ("sub", "grp")),
            (third_part, ("sub", "grp"), ("sub", "grp")),
            (kernel_laid, ("sub", "grp"), ("sub",)),
        ],
        (("sub", True), ("grp", True)),
    )
    first_grad = first_sum.reshape(first_part.shape) * factor
    third_grad = third_sum.reshape(third_part.shape) * factor
    own_rows = channels // grp_count
    group_grad = (
        group_sum.reshape(own_rows, 27, GW).transpose(0, 2, 1).reshape(own_rows, GW, 3, 3, 3) * factor
    )
    return (block_output, volume_grad, first_grad, group_grad, third_grad)


def solution(mesh):
    in_specs = (
        P(None, ("rep", "grp"), "sub", None),
        P(None, ("rep", "grp"), "sub", None),
        P(),
        P(),
        P(),
    )
    out_specs = (
        P(None, ("rep", "grp"), "sub", None),
        P(None, ("rep", "grp"), "sub", None),
        P("rep", None),
        P(("rep", "grp"), None, None, None, None),
        P("rep", None),
    )
    return jax.shard_map(
        per_device, mesh=mesh, in_specs=in_specs, out_specs=out_specs, check_vma=False
    )
```

```python
import functools
import itertools
import math

import jax
import jax.numpy as jnp
from jax import lax
from jax.experimental import pallas as pl
from jax.experimental.pallas import tpu as pltpu
from jax.sharding import PartitionSpec as P

GW = 8
LANES = 128
TAPS_PER_BLOCK = 16


def shift_lanes(block, offset):
    lane = lax.broadcasted_iota(jnp.int32, block.shape, 1)
    rolled = pltpu.roll(block, (-offset) % LANES, 1)
    edge = LANES - 1 if offset > 0 else 0
    return jnp.where(lane == edge, jnp.zeros_like(rolled), rolled)


def conv_body(ext_ref, w_hbm, out_ref, w_vmem, sems):
    height, channels = out_ref.shape[0], out_ref.shape[1]
    copies = [pltpu.make_async_copy(w_hbm.at[k], w_vmem.at[k], sems.at[k]) for k in range(9)]
    for copy in copies:
        copy.start()
    parts = None
    for dz, dy in itertools.product(range(3), repeat=2):
        rows = jnp.concatenate([ext_ref[dz, dy + y] for y in range(height)], axis=1)
        copies[dz * 3 + dy].wait()
        product = jnp.dot(w_vmem[dz * 3 + dy], rows, preferred_element_type=jnp.float32)
        parts = product if parts is None else parts + product
    for y in range(height):
        lanes = slice(y * LANES, (y + 1) * LANES)
        out_ref[y] = (
            parts[channels : 2 * channels, lanes]
            + shift_lanes(parts[:channels, lanes], -1)
            + shift_lanes(parts[2 * channels :, lanes], 1)
        )


def conv_call(ext, weights):
    _, rows, channels, width = ext.shape
    height = rows - 2
    return pl.pallas_call(
        conv_body,
        out_shape=jax.ShapeDtypeStruct((height, channels, width), jnp.float32),
        in_specs=[pl.BlockSpec(memory_space=pltpu.VMEM), pl.BlockSpec(memory_space=pl.ANY)],
        out_specs=pl.BlockSpec(memory_space=pltpu.VMEM),
        scratch_shapes=[pltpu.VMEM(weights.shape, weights.dtype), pltpu.SemaphoreType.DMA((9,))],
        cost_estimate=pl.CostEstimate(
            flops=2 * 27 * channels * channels * height * width,
            transcendentals=0,
            bytes_accessed=ext.size * 2 + weights.size * 2 + height * channels * width * 4,
        ),
    )(ext, weights)


def wgrad_body(act_ref, delta_ref, mask_ref, sel_ref, out_ref):
    height, channels = delta_ref.shape[0], delta_ref.shape[1]
    stacked = []
    for y in range(height):
        row = delta_ref[y].astype(jnp.float32)
        stacked.append(
            jnp.concatenate([shift_lanes(row, 1), row, shift_lanes(row, -1)], axis=0).astype(
                jnp.bfloat16
            )
        )
    stacked = jnp.concatenate(stacked, axis=1)
    mask = mask_ref[...]
    totals = [jnp.zeros((channels, LANES), jnp.float32) for _ in range(out_ref.shape[0])]
    for dz, dy in itertools.product(range(3), repeat=2):
        rows = jnp.concatenate([act_ref[dz, dy + y] for y in range(height)], axis=1)
        grads = lax.dot_general(
            stacked, rows, (((1,), (1,)), ((), ())), preferred_element_type=jnp.float32
        )
        for dx in range(3):
            tap = dz * 9 + dy * 3 + dx
            picked = grads[dx * channels : (dx + 1) * channels] * mask
            folded = picked[:, :LANES]
            for start in range(LANES, channels, LANES):
                folded = folded + picked[:, start : start + LANES]
            high = folded.astype(jnp.bfloat16)
            low = (folded - high.astype(jnp.float32)).astype(jnp.bfloat16)
            sel = sel_ref[tap % TAPS_PER_BLOCK]
            totals[tap // TAPS_PER_BLOCK] += jnp.dot(
                high, sel, preferred_element_type=jnp.float32
            ) + jnp.dot(low, sel, preferred_element_type=jnp.float32)
    for n, total in enumerate(totals):
        out_ref[n] = total


def wgrad_call(act_ext, delta):
    height, channels, width = delta.shape
    blocks = -(-27 // TAPS_PER_BLOCK)
    group_of = jnp.arange(channels) // GW
    mask = (group_of[:, None] == group_of[None, :]).astype(jnp.float32)
    lane = jnp.arange(LANES)
    sel = (
        lane[None, None, :] == jnp.arange(TAPS_PER_BLOCK)[:, None, None] * GW + (lane % GW)[None, :, None]
    ).astype(jnp.bfloat16)
    out = pl.pallas_call(
        wgrad_body,
        out_shape=jax.ShapeDtypeStruct((blocks, channels, LANES), jnp.float32),
        in_specs=[pl.BlockSpec(memory_space=pltpu.VMEM)] * 4,
        out_specs=pl.BlockSpec(memory_space=pltpu.VMEM),
        cost_estimate=pl.CostEstimate(
            flops=2 * 27 * channels * channels * height * width + 4 * 27 * channels * LANES * LANES,
            transcendentals=0,
            bytes_accessed=act_ext.size * 2 + delta.size * 2 + blocks * channels * LANES * 4,
        ),
    )(act_ext, delta, mask, sel)
    return out.transpose(1, 0, 2).reshape(channels, blocks * LANES)[:, : 27 * GW]


def tree_sum(blocks, order):
    steps = []
    for axis, rising in order:
        bits = []
        bit = 1
        while bit < lax.axis_size(axis):
            bits.append(bit)
            bit *= 2
        steps += [(axis, bit) for bit in (bits if rising else bits[::-1])]
    pieces = [block.reshape(-1) for block, _, _ in blocks]
    done = []
    for axis, bit in steps:
        pairs = [(i, i ^ bit) for i in range(lax.axis_size(axis))]
        upper = (lax.axis_index(axis) & bit) != 0
        members = [n for n, (_, axes, _) in enumerate(blocks) if axis in axes]
        keeps, sends = [], []
        for n in members:
            half = pieces[n].shape[0] // 2
            low, high = pieces[n][:half], pieces[n][half:]
            keeps.append(jnp.where(upper, high, low))
            sends.append(jnp.where(upper, low, high))
        got = lax.ppermute(jnp.concatenate(sends), axis, pairs)
        offset = 0
        for n, keep in zip(members, keeps):
            pieces[n] = keep + got[offset : offset + keep.shape[0]]
            offset += keep.shape[0]
        done.append((axis, pairs, upper))
    for axis, pairs, upper in reversed(done):
        members = [n for n, (_, _, axes) in enumerate(blocks) if axis in axes]
        if not members:
            continue
        got = lax.ppermute(jnp.concatenate([pieces[n] for n in members]), axis, pairs)
        offset = 0
        for n in members:
            size = pieces[n].shape[0]
            other = got[offset : offset + size]
            offset += size
            pieces[n] = jnp.where(
                upper,
                jnp.concatenate([other, pieces[n]]),
                jnp.concatenate([pieces[n], other]),
            )
    return pieces


def halo(block):
    for axis, dim in (("grp", 0), ("sub", 1)):
        count = lax.axis_size(axis)
        up = [(i, i + 1) for i in range(count - 1)]
        down = [(i + 1, i) for i in range(count - 1)]
        size = block.shape[dim]
        low = lax.ppermute(lax.slice_in_dim(block, size - 1, size, axis=dim), axis, up)
        high = lax.ppermute(lax.slice_in_dim(block, 0, 1, axis=dim), axis, down)
        block = jnp.concatenate([low, block, high], axis=dim)
    return block


def silu_slope(values):
    sigma = jax.nn.sigmoid(values)
    return sigma * (1.0 + values * (1.0 - sigma))


def conv_weights(group_weight):
    channels = group_weight.shape[0]
    group_of = jnp.arange(channels) // GW
    mask = (group_of[:, None] == group_of[None, :]).astype(jnp.float32)
    spread = (jnp.arange(GW)[:, None] == jnp.arange(channels)[None, :] % GW).astype(jnp.float32)
    compact = group_weight.reshape(channels, GW, 27).astype(jnp.float32)
    forward = jnp.einsum("ojt,ji->toi", compact, spread)
    backward = jnp.einsum("ji,ojt->tio", spread, compact[:, :, ::-1])
    forward = (forward * mask).astype(group_weight.dtype).reshape(9, 3 * channels, channels)
    backward = (backward * mask).astype(group_weight.dtype).reshape(9, 3 * channels, channels)
    return forward, backward


def rounded(values):
    return lax.reduce_precision(values, exponent_bits=8, mantissa_bits=7).astype(jnp.bfloat16)


def per_device(volume, cotangent, first_weight, group_weight, third_weight):
    channels, depth, height, width = volume.shape
    flattened = volume.reshape(channels, -1)
    contract_lead = (((0,), (0,)), ((), ()))
    contract_tail = (((1,), (1,)), ((), ()))
    total_cells = depth * lax.axis_size("grp") * height * lax.axis_size("sub") * width
    factor = 1.0 / math.sqrt(total_cells)

    def to_rows(block):
        return block.reshape(channels, depth, height, width).transpose(1, 2, 0, 3)

    def from_rows(block):
        return block.transpose(1, 0, 2).reshape(channels, -1)

    forward_kernel, backward_kernel = conv_weights(group_weight)
    first_pre = lax.dot_general(
        first_weight, flattened, contract_lead, preferred_element_type=jnp.float32
    )
    first_act = rounded(jax.nn.silu(first_pre))
    act_ext = halo(to_rows(first_act))
    group_pre = conv_call(act_ext, forward_kernel)
    group_act = rounded(jax.nn.silu(group_pre))
    act_flat = from_rows(group_act)
    summed = flattened.astype(jnp.float32) + lax.dot_general(
        third_weight, act_flat, contract_lead, preferred_element_type=jnp.float32
    )
    block_output = jax.nn.silu(summed).astype(jnp.bfloat16).reshape(volume.shape)
    third_delta = rounded(cotangent.reshape(channels, -1).astype(jnp.float32) * silu_slope(summed))
    third_part = lax.dot_general(
        act_flat, third_delta, contract_tail, preferred_element_type=jnp.float32
    )
    hidden_grad = rounded(jnp.dot(third_weight, third_delta, preferred_element_type=jnp.float32))
    group_delta = rounded(to_rows(hidden_grad)[0].astype(jnp.float32) * silu_slope(group_pre))
    delta_ext = halo(group_delta[None])
    inner_grad = from_rows(rounded(conv_call(delta_ext, backward_kernel)))
    kernel_part = wgrad_call(act_ext, group_delta)
    first_delta = rounded(inner_grad.astype(jnp.float32) * silu_slope(first_pre))
    first_part = lax.dot_general(
        flattened, first_delta, contract_tail, preferred_element_type=jnp.float32
    )
    volume_grad = (
        (
            third_delta.astype(jnp.float32)
            + jnp.dot(first_weight, first_delta, preferred_element_type=jnp.float32)
        )
        .astype(jnp.bfloat16)
        .reshape(volume.shape)
    )
    grp_count, sub_count = lax.axis_size("grp"), lax.axis_size("sub")
    digits = grp_count.bit_length() - 1
    reverse = [int(format(n, f"0{digits}b")[::-1], 2) if digits else 0 for n in range(grp_count)]
    blocks = kernel_part.reshape(grp_count, sub_count, -1)
    kernel_laid = jnp.concatenate([blocks[n : n + 1] for n in reverse]).transpose(1, 0, 2)
    first_sum, third_sum, group_sum = tree_sum(
        [
            (first_part, ("sub", "grp"), ("sub", "grp")),
            (third_part, ("sub", "grp"), ("sub", "grp")),
            (kernel_laid, ("sub", "grp"), ("sub",)),
        ],
        (("sub", True), ("grp", True)),
    )
    first_grad = first_sum.reshape(first_part.shape) * factor
    third_grad = third_sum.reshape(third_part.shape) * factor
    own_rows = channels // grp_count
    group_grad = (
        group_sum.reshape(own_rows, 27, GW).transpose(0, 2, 1).reshape(own_rows, GW, 3, 3, 3) * factor
    )
    return (block_output, volume_grad, first_grad, group_grad, third_grad)


def solution(mesh):
    in_specs = (
        P(None, ("rep", "grp"), "sub", None),
        P(None, ("rep", "grp"), "sub", None),
        P(),
        P(),
        P(),
    )
    out_specs = (
        P(None, ("rep", "grp"), "sub", None),
        P(None, ("rep", "grp"), "sub", None),
        P("rep", None),
        P(("rep", "grp"), None, None, None, None),
        P("rep", None),
    )
    return jax.shard_map(
        per_device, mesh=mesh, in_specs=in_specs, out_specs=out_specs, check_vma=False
    )
```

```python
import functools
import itertools
import math

import jax
import jax.numpy as jnp
from jax import lax
from jax.experimental import pallas as pl
from jax.experimental.pallas import tpu as pltpu
from jax.sharding import PartitionSpec as P

GW = 8
LANES = 128
TAPS_PER_BLOCK = 16


def shift_lanes(block, offset):
    lane = lax.broadcasted_iota(jnp.int32, block.shape, 1)
    rolled = pltpu.roll(block, (-offset) % LANES, 1)
    edge = LANES - 1 if offset > 0 else 0
    return jnp.where(lane == edge, jnp.zeros_like(rolled), rolled)


def conv_body(ext_ref, w_ref, out_ref):
    height, channels = out_ref.shape[0], out_ref.shape[1]
    rows = jnp.concatenate(
        [
            jnp.concatenate([ext_ref[dz, dy + y] for y in range(height)], axis=1)
            for dz, dy in itertools.product(range(3), repeat=2)
        ],
        axis=0,
    )
    parts = jnp.dot(w_ref[...], rows, preferred_element_type=jnp.float32)
    for y in range(height):
        lanes = slice(y * LANES, (y + 1) * LANES)
        out_ref[y] = (
            parts[channels : 2 * channels, lanes]
            + shift_lanes(parts[:channels, lanes], -1)
            + shift_lanes(parts[2 * channels :, lanes], 1)
        )


def conv_call(ext, weights):
    _, rows, channels, width = ext.shape
    height = rows - 2
    return pl.pallas_call(
        conv_body,
        out_shape=jax.ShapeDtypeStruct((height, channels, width), jnp.float32),
        in_specs=[pl.BlockSpec(memory_space=pltpu.VMEM)] * 2,
        out_specs=pl.BlockSpec(memory_space=pltpu.VMEM),
        cost_estimate=pl.CostEstimate(
            flops=2 * 27 * channels * channels * height * width,
            transcendentals=0,
            bytes_accessed=ext.size * 2 + weights.size * 2 + height * channels * width * 4,
        ),
    )(ext, weights)


def wgrad_body(act_ref, delta_ref, mask_ref, sel_ref, out_ref):
    height, channels = delta_ref.shape[0], delta_ref.shape[1]
    stacked = []
    for y in range(height):
        row = delta_ref[y].astype(jnp.float32)
        stacked.append(
            jnp.concatenate([shift_lanes(row, 1), row, shift_lanes(row, -1)], axis=0).astype(
                jnp.bfloat16
            )
        )
    stacked = jnp.concatenate(stacked, axis=1)
    mask = mask_ref[...]
    totals = [jnp.zeros((channels, LANES), jnp.float32) for _ in range(out_ref.shape[0])]
    for dz, dy in itertools.product(range(3), repeat=2):
        rows = jnp.concatenate([act_ref[dz, dy + y] for y in range(height)], axis=1)
        grads = lax.dot_general(
            stacked, rows, (((1,), (1,)), ((), ())), preferred_element_type=jnp.float32
        )
        for dx in range(3):
            tap = dz * 9 + dy * 3 + dx
            picked = grads[dx * channels : (dx + 1) * channels] * mask
            folded = picked[:, :LANES]
            for start in range(LANES, channels, LANES):
                folded = folded + picked[:, start : start + LANES]
            high = folded.astype(jnp.bfloat16)
            low = (folded - high.astype(jnp.float32)).astype(jnp.bfloat16)
            sel = sel_ref[tap % TAPS_PER_BLOCK]
            totals[tap // TAPS_PER_BLOCK] += jnp.dot(
                high, sel, preferred_element_type=jnp.float32
            ) + jnp.dot(low, sel, preferred_element_type=jnp.float32)
    for n, total in enumerate(totals):
        out_ref[n] = total


def wgrad_call(act_ext, delta):
    height, channels, width = delta.shape
    blocks = -(-27 // TAPS_PER_BLOCK)
    group_of = jnp.arange(channels) // GW
    mask = (group_of[:, None] == group_of[None, :]).astype(jnp.float32)
    lane = jnp.arange(LANES)
    sel = (
        lane[None, None, :] == jnp.arange(TAPS_PER_BLOCK)[:, None, None] * GW + (lane % GW)[None, :, None]
    ).astype(jnp.bfloat16)
    out = pl.pallas_call(
        wgrad_body,
        out_shape=jax.ShapeDtypeStruct((blocks, channels, LANES), jnp.float32),
        in_specs=[pl.BlockSpec(memory_space=pltpu.VMEM)] * 4,
        out_specs=pl.BlockSpec(memory_space=pltpu.VMEM),
        cost_estimate=pl.CostEstimate(
            flops=2 * 27 * channels * channels * height * width + 4 * 27 * channels * LANES * LANES,
            transcendentals=0,
            bytes_accessed=act_ext.size * 2 + delta.size * 2 + blocks * channels * LANES * 4,
        ),
    )(act_ext, delta, mask, sel)
    return out.transpose(1, 0, 2).reshape(channels, blocks * LANES)[:, : 27 * GW]


def tree_sum(blocks, order):
    steps = []
    for axis, rising in order:
        bits = []
        bit = 1
        while bit < lax.axis_size(axis):
            bits.append(bit)
            bit *= 2
        steps += [(axis, bit) for bit in (bits if rising else bits[::-1])]
    pieces = [block.reshape(-1) for block, _, _ in blocks]
    done = []
    for axis, bit in steps:
        pairs = [(i, i ^ bit) for i in range(lax.axis_size(axis))]
        upper = (lax.axis_index(axis) & bit) != 0
        members = [n for n, (_, axes, _) in enumerate(blocks) if axis in axes]
        keeps, sends = [], []
        for n in members:
            half = pieces[n].shape[0] // 2
            low, high = pieces[n][:half], pieces[n][half:]
            keeps.append(jnp.where(upper, high, low))
            sends.append(jnp.where(upper, low, high))
        got = lax.ppermute(jnp.concatenate(sends), axis, pairs)
        offset = 0
        for n, keep in zip(members, keeps):
            pieces[n] = keep + got[offset : offset + keep.shape[0]]
            offset += keep.shape[0]
        done.append((axis, pairs, upper))
    for axis, pairs, upper in reversed(done):
        members = [n for n, (_, _, axes) in enumerate(blocks) if axis in axes]
        if not members:
            continue
        got = lax.ppermute(jnp.concatenate([pieces[n] for n in members]), axis, pairs)
        offset = 0
        for n in members:
            size = pieces[n].shape[0]
            other = got[offset : offset + size]
            offset += size
            pieces[n] = jnp.where(
                upper,
                jnp.concatenate([other, pieces[n]]),
                jnp.concatenate([pieces[n], other]),
            )
    return pieces


def halo(block):
    for axis, dim in (("grp", 0), ("sub", 1)):
        count = lax.axis_size(axis)
        up = [(i, i + 1) for i in range(count - 1)]
        down = [(i + 1, i) for i in range(count - 1)]
        size = block.shape[dim]
        low = lax.ppermute(lax.slice_in_dim(block, size - 1, size, axis=dim), axis, up)
        high = lax.ppermute(lax.slice_in_dim(block, 0, 1, axis=dim), axis, down)
        block = jnp.concatenate([low, block, high], axis=dim)
    return block


def silu_slope(values):
    sigma = jax.nn.sigmoid(values)
    return sigma * (1.0 + values * (1.0 - sigma))


def conv_weights(group_weight):
    channels = group_weight.shape[0]
    group_of = jnp.arange(channels) // GW
    mask = (group_of[:, None] == group_of[None, :]).astype(jnp.float32)
    spread = (jnp.arange(GW)[:, None] == jnp.arange(channels)[None, :] % GW).astype(jnp.float32)
    compact = group_weight.reshape(channels, GW, 9, 3).astype(jnp.float32)
    flipped = group_weight.reshape(channels, GW, 27)[:, :, ::-1].reshape(channels, GW, 9, 3)
    forward = jnp.einsum("ojkd,ji->doki", compact, spread)
    backward = jnp.einsum("ji,ojkd->diko", spread, flipped.astype(jnp.float32))
    mask4 = mask[None, :, None, :]
    forward = (forward * mask4).astype(group_weight.dtype).reshape(3 * channels, 9 * channels)
    backward = (backward * mask4).astype(group_weight.dtype).reshape(3 * channels, 9 * channels)
    return forward, backward


def rounded(values):
    return lax.reduce_precision(values, exponent_bits=8, mantissa_bits=7).astype(jnp.bfloat16)


def per_device(volume, cotangent, first_weight, group_weight, third_weight):
    channels, depth, height, width = volume.shape
    flattened = volume.reshape(channels, -1)
    contract_lead = (((0,), (0,)), ((), ()))
    contract_tail = (((1,), (1,)), ((), ()))
    total_cells = depth * lax.axis_size("grp") * height * lax.axis_size("sub") * width
    factor = 1.0 / math.sqrt(total_cells)

    def to_rows(block):
        return block.reshape(channels, depth, height, width).transpose(1, 2, 0, 3)

    def from_rows(block):
        return block.transpose(1, 0, 2).reshape(channels, -1)

    forward_kernel, backward_kernel = conv_weights(group_weight)
    first_pre = lax.dot_general(
        first_weight, flattened, contract_lead, preferred_element_type=jnp.float32
    )
    first_act = rounded(jax.nn.silu(first_pre))
    act_ext = halo(to_rows(first_act))
    group_pre = conv_call(act_ext, forward_kernel)
    group_act = rounded(jax.nn.silu(group_pre))
    act_flat = from_rows(group_act)
    summed = flattened.astype(jnp.float32) + lax.dot_general(
        third_weight, act_flat, contract_lead, preferred_element_type=jnp.float32
    )
    block_output = jax.nn.silu(summed).astype(jnp.bfloat16).reshape(volume.shape)
    third_delta = rounded(cotangent.reshape(channels, -1).astype(jnp.float32) * silu_slope(summed))
    third_part = lax.dot_general(
        act_flat, third_delta, contract_tail, preferred_element_type=jnp.float32
    )
    hidden_grad = rounded(jnp.dot(third_weight, third_delta, preferred_element_type=jnp.float32))
    group_delta = rounded(to_rows(hidden_grad)[0].astype(jnp.float32) * silu_slope(group_pre))
    delta_ext = halo(group_delta[None])
    inner_grad = from_rows(rounded(conv_call(delta_ext, backward_kernel)))
    kernel_part = wgrad_call(act_ext, group_delta)
    first_delta = rounded(inner_grad.astype(jnp.float32) * silu_slope(first_pre))
    first_part = lax.dot_general(
        flattened, first_delta, contract_tail, preferred_element_type=jnp.float32
    )
    volume_grad = (
        (
            third_delta.astype(jnp.float32)
            + jnp.dot(first_weight, first_delta, preferred_element_type=jnp.float32)
        )
        .astype(jnp.bfloat16)
        .reshape(volume.shape)
    )
    grp_count, sub_count = lax.axis_size("grp"), lax.axis_size("sub")
    digits = grp_count.bit_length() - 1
    reverse = [int(format(n, f"0{digits}b")[::-1], 2) if digits else 0 for n in range(grp_count)]
    blocks = kernel_part.reshape(grp_count, sub_count, -1)
    kernel_laid = jnp.concatenate([blocks[n : n + 1] for n in reverse]).transpose(1, 0, 2)
    first_sum, third_sum, group_sum = tree_sum(
        [
            (first_part, ("sub", "grp"), ("sub", "grp")),
            (third_part, ("sub", "grp"), ("sub", "grp")),
            (kernel_laid, ("sub", "grp"), ("sub",)),
        ],
        (("sub", True), ("grp", True)),
    )
    first_grad = first_sum.reshape(first_part.shape) * factor
    third_grad = third_sum.reshape(third_part.shape) * factor
    own_rows = channels // grp_count
    group_grad = (
        group_sum.reshape(own_rows, 27, GW).transpose(0, 2, 1).reshape(own_rows, GW, 3, 3, 3) * factor
    )
    return (block_output, volume_grad, first_grad, group_grad, third_grad)


def solution(mesh):
    in_specs = (
        P(None, ("rep", "grp"), "sub", None),
        P(None, ("rep", "grp"), "sub", None),
        P(),
        P(),
        P(),
    )
    out_specs = (
        P(None, ("rep", "grp"), "sub", None),
        P(None, ("rep", "grp"), "sub", None),
        P("rep", None),
        P(("rep", "grp"), None, None, None, None),
        P("rep", None),
    )
    return jax.shard_map(
        per_device, mesh=mesh, in_specs=in_specs, out_specs=out_specs, check_vma=False
    )
```

```python
import functools
import itertools
import math

import jax
import jax.numpy as jnp
from jax import lax
from jax.experimental import pallas as pl
from jax.experimental.pallas import tpu as pltpu
from jax.sharding import PartitionSpec as P

GW = 8
LANES = 128
TAPS_PER_BLOCK = 16


def shift_lanes(block, offset):
    lane = lax.broadcasted_iota(jnp.int32, block.shape, 1)
    rolled = pltpu.roll(block, (-offset) % LANES, 1)
    edge = LANES - 1 if offset > 0 else 0
    return jnp.where(lane == edge, jnp.zeros_like(rolled), rolled)


def conv_body(ext_ref, w_hbm, out_ref, w_vmem, sems):
    height, channels = out_ref.shape[0], out_ref.shape[1]
    copies = [pltpu.make_async_copy(w_hbm.at[k], w_vmem.at[k], sems.at[k]) for k in range(9)]
    for copy in copies:
        copy.start()
    parts = None
    for dz, dy in itertools.product(range(3), repeat=2):
        rows = jnp.concatenate([ext_ref[dz, dy + y] for y in range(height)], axis=1)
        copies[dz * 3 + dy].wait()
        product = jnp.dot(w_vmem[dz * 3 + dy], rows, preferred_element_type=jnp.float32)
        parts = product if parts is None else parts + product
    for y in range(height):
        lanes = slice(y * LANES, (y + 1) * LANES)
        out_ref[y] = (
            parts[channels : 2 * channels, lanes]
            + shift_lanes(parts[:channels, lanes], -1)
            + shift_lanes(parts[2 * channels :, lanes], 1)
        )


def conv_call(ext, weights):
    _, rows, channels, width = ext.shape
    height = rows - 2
    return pl.pallas_call(
        conv_body,
        out_shape=jax.ShapeDtypeStruct((height, channels, width), jnp.float32),
        in_specs=[pl.BlockSpec(memory_space=pltpu.VMEM), pl.BlockSpec(memory_space=pl.ANY)],
        out_specs=pl.BlockSpec(memory_space=pltpu.VMEM),
        scratch_shapes=[pltpu.VMEM(weights.shape, weights.dtype), pltpu.SemaphoreType.DMA((9,))],
        cost_estimate=pl.CostEstimate(
            flops=2 * 27 * channels * channels * height * width,
            transcendentals=0,
            bytes_accessed=ext.size * 2 + weights.size * 2 + height * channels * width * 4,
        ),
    )(ext, weights)


def wgrad_body(act_ref, delta_ref, mask_ref, sel_ref, out_ref):
    height, channels = delta_ref.shape[0], delta_ref.shape[1]
    stacked = []
    for y in range(height):
        row = delta_ref[y].astype(jnp.float32)
        stacked.append(
            jnp.concatenate([shift_lanes(row, 1), row, shift_lanes(row, -1)], axis=0).astype(
                jnp.bfloat16
            )
        )
    stacked = jnp.concatenate(stacked, axis=1)
    mask = mask_ref[...]
    totals = [jnp.zeros((channels, LANES), jnp.float32) for _ in range(out_ref.shape[0])]
    for dz, dy in itertools.product(range(3), repeat=2):
        rows = jnp.concatenate([act_ref[dz, dy + y] for y in range(height)], axis=1)
        grads = lax.dot_general(
            stacked, rows, (((1,), (1,)), ((), ())), preferred_element_type=jnp.float32
        )
        for dx in range(3):
            tap = dz * 9 + dy * 3 + dx
            picked = grads[dx * channels : (dx + 1) * channels] * mask
            folded = picked[:, :LANES]
            for start in range(LANES, channels, LANES):
                folded = folded + picked[:, start : start + LANES]
            high = folded.astype(jnp.bfloat16)
            low = (folded - high.astype(jnp.float32)).astype(jnp.bfloat16)
            sel = sel_ref[tap % TAPS_PER_BLOCK]
            totals[tap // TAPS_PER_BLOCK] += jnp.dot(
                high, sel, preferred_element_type=jnp.float32
            ) + jnp.dot(low, sel, preferred_element_type=jnp.float32)
    for n, total in enumerate(totals):
        out_ref[n] = total


def wgrad_call(act_ext, delta):
    height, channels, width = delta.shape
    blocks = -(-27 // TAPS_PER_BLOCK)
    group_of = jnp.arange(channels) // GW
    mask = (group_of[:, None] == group_of[None, :]).astype(jnp.float32)
    lane = jnp.arange(LANES)
    sel = (
        lane[None, None, :] == jnp.arange(TAPS_PER_BLOCK)[:, None, None] * GW + (lane % GW)[None, :, None]
    ).astype(jnp.bfloat16)
    out = pl.pallas_call(
        wgrad_body,
        out_shape=jax.ShapeDtypeStruct((blocks, channels, LANES), jnp.float32),
        in_specs=[pl.BlockSpec(memory_space=pltpu.VMEM)] * 4,
        out_specs=pl.BlockSpec(memory_space=pltpu.VMEM),
        cost_estimate=pl.CostEstimate(
            flops=2 * 27 * channels * channels * height * width + 4 * 27 * channels * LANES * LANES,
            transcendentals=0,
            bytes_accessed=act_ext.size * 2 + delta.size * 2 + blocks * channels * LANES * 4,
        ),
    )(act_ext, delta, mask, sel)
    return out.transpose(1, 0, 2).reshape(channels, blocks * LANES)[:, : 27 * GW]


def tree_sum(blocks, order):
    steps = []
    for axis, rising in order:
        bits = []
        bit = 1
        while bit < lax.axis_size(axis):
            bits.append(bit)
            bit *= 2
        steps += [(axis, bit) for bit in (bits if rising else bits[::-1])]
    pieces = [block.reshape(-1) for block, _, _ in blocks]
    done = []
    for axis, bit in steps:
        pairs = [(i, i ^ bit) for i in range(lax.axis_size(axis))]
        upper = (lax.axis_index(axis) & bit) != 0
        members = [n for n, (_, axes, _) in enumerate(blocks) if axis in axes]
        keeps, sends = [], []
        for n in members:
            half = pieces[n].shape[0] // 2
            low, high = pieces[n][:half], pieces[n][half:]
            keeps.append(jnp.where(upper, high, low))
            sends.append(jnp.where(upper, low, high))
        got = lax.ppermute(jnp.concatenate(sends), axis, pairs)
        offset = 0
        for n, keep in zip(members, keeps):
            pieces[n] = keep + got[offset : offset + keep.shape[0]]
            offset += keep.shape[0]
        done.append((axis, pairs, upper))
    for axis, pairs, upper in reversed(done):
        members = [n for n, (_, _, axes) in enumerate(blocks) if axis in axes]
        if not members:
            continue
        got = lax.ppermute(jnp.concatenate([pieces[n] for n in members]), axis, pairs)
        offset = 0
        for n in members:
            size = pieces[n].shape[0]
            other = got[offset : offset + size]
            offset += size
            pieces[n] = jnp.where(
                upper,
                jnp.concatenate([other, pieces[n]]),
                jnp.concatenate([pieces[n], other]),
            )
    return pieces


def halo(block):
    for axis, dim in (("grp", 0), ("sub", 1)):
        count = lax.axis_size(axis)
        up = [(i, i + 1) for i in range(count - 1)]
        down = [(i + 1, i) for i in range(count - 1)]
        size = block.shape[dim]
        low = lax.ppermute(lax.slice_in_dim(block, size - 1, size, axis=dim), axis, up)
        high = lax.ppermute(lax.slice_in_dim(block, 0, 1, axis=dim), axis, down)
        block = jnp.concatenate([low, block, high], axis=dim)
    return block


def silu_slope(values):
    sigma = jax.nn.sigmoid(values)
    return sigma * (1.0 + values * (1.0 - sigma))


def conv_weights(group_weight):
    channels = group_weight.shape[0]
    group_of = jnp.arange(channels) // GW
    mask = (group_of[:, None] == group_of[None, :]).astype(jnp.float32)
    spread = (jnp.arange(GW)[:, None] == jnp.arange(channels)[None, :] % GW).astype(jnp.float32)
    compact = group_weight.reshape(channels, GW, 27).astype(jnp.float32)
    forward = jnp.einsum("ojt,ji->toi", compact, spread)
    backward = jnp.einsum("ji,ojt->tio", spread, compact[:, :, ::-1])
    forward = (forward * mask).astype(group_weight.dtype).reshape(9, 3 * channels, channels)
    backward = (backward * mask).astype(group_weight.dtype).reshape(9, 3 * channels, channels)
    return forward, backward


def rounded(values):
    return lax.reduce_precision(values, exponent_bits=8, mantissa_bits=7).astype(jnp.bfloat16)


def per_device(volume, cotangent, first_weight, group_weight, third_weight):
    channels, depth, height, width = volume.shape
    flattened = volume.reshape(channels, -1)
    contract_lead = (((0,), (0,)), ((), ()))
    contract_tail = (((1,), (1,)), ((), ()))
    total_cells = depth * lax.axis_size("grp") * height * lax.axis_size("sub") * width
    factor = 1.0 / math.sqrt(total_cells)

    def to_rows(block):
        return block.reshape(channels, depth, height, width).transpose(1, 2, 0, 3)

    def from_rows(block):
        return block.transpose(1, 0, 2).reshape(channels, -1)

    forward_kernel, backward_kernel = conv_weights(group_weight)
    first_pre = lax.dot_general(
        first_weight, flattened, contract_lead, preferred_element_type=jnp.float32
    )
    first_act = rounded(jax.nn.silu(first_pre))
    act_ext = halo(to_rows(first_act))
    group_pre = conv_call(act_ext, forward_kernel)
    group_act = rounded(jax.nn.silu(group_pre))
    act_flat = from_rows(group_act)
    summed = flattened.astype(jnp.float32) + lax.dot_general(
        third_weight, act_flat, contract_lead, preferred_element_type=jnp.float32
    )
    block_output = jax.nn.silu(summed).astype(jnp.bfloat16).reshape(volume.shape)
    third_delta = rounded(cotangent.reshape(channels, -1).astype(jnp.float32) * silu_slope(summed))
    third_part = lax.dot_general(
        act_flat, third_delta, contract_tail, preferred_element_type=jnp.float32
    )
    hidden_grad = rounded(jnp.dot(third_weight, third_delta, preferred_element_type=jnp.float32))
    group_delta = rounded(to_rows(hidden_grad)[0].astype(jnp.float32) * silu_slope(group_pre))
    delta_ext = halo(group_delta[None])
    inner_grad = from_rows(rounded(conv_call(delta_ext, backward_kernel)))
    kernel_part = wgrad_call(act_ext, group_delta)
    first_delta = rounded(inner_grad.astype(jnp.float32) * silu_slope(first_pre))
    first_part = lax.dot_general(
        flattened, first_delta, contract_tail, preferred_element_type=jnp.float32
    )
    volume_grad = (
        (
            third_delta.astype(jnp.float32)
            + jnp.dot(first_weight, first_delta, preferred_element_type=jnp.float32)
        )
        .astype(jnp.bfloat16)
        .reshape(volume.shape)
    )
    grp_count, sub_count = lax.axis_size("grp"), lax.axis_size("sub")
    digits = grp_count.bit_length() - 1
    reverse = [int(format(n, f"0{digits}b")[::-1], 2) if digits else 0 for n in range(grp_count)]
    blocks = kernel_part.reshape(grp_count, sub_count, -1)
    kernel_laid = jnp.concatenate([blocks[n : n + 1] for n in reverse]).transpose(1, 0, 2)
    order = (("sub", True), ("grp", True))
    third_sum, group_sum = tree_sum(
        [(third_part, ("sub", "grp"), ("sub", "grp")), (kernel_laid, ("sub", "grp"), ("sub",))], order
    )
    (first_sum,) = tree_sum([(first_part, ("sub", "grp"), ("sub", "grp"))], order)
    first_grad = first_sum.reshape(first_part.shape) * factor
    third_grad = third_sum.reshape(third_part.shape) * factor
    own_rows = channels // grp_count
    group_grad = (
        group_sum.reshape(own_rows, 27, GW).transpose(0, 2, 1).reshape(own_rows, GW, 3, 3, 3) * factor
    )
    return (block_output, volume_grad, first_grad, group_grad, third_grad)


def solution(mesh):
    in_specs = (
        P(None, ("rep", "grp"), "sub", None),
        P(None, ("rep", "grp"), "sub", None),
        P(),
        P(),
        P(),
    )
    out_specs = (
        P(None, ("rep", "grp"), "sub", None),
        P(None, ("rep", "grp"), "sub", None),
        P("rep", None),
        P(("rep", "grp"), None, None, None, None),
        P("rep", None),
    )
    return jax.shard_map(
        per_device, mesh=mesh, in_specs=in_specs, out_specs=out_specs, check_vma=False
    )
```

```python
import functools
import itertools
import math

import jax
import jax.numpy as jnp
from jax import lax
from jax.experimental import pallas as pl
from jax.experimental.pallas import tpu as pltpu
from jax.sharding import PartitionSpec as P

GW = 8
LANES = 128
TAPS_PER_BLOCK = 16


def shift_lanes(block, offset):
    lane = lax.broadcasted_iota(jnp.int32, block.shape, 1)
    rolled = pltpu.roll(block, (-offset) % LANES, 1)
    edge = LANES - 1 if offset > 0 else 0
    return jnp.where(lane == edge, jnp.zeros_like(rolled), rolled)


def conv_body(block_ref, below_ref, above_ref, before_ref, after_ref, w_hbm, out_ref, w_vmem, sems):
    pieces = (block_ref, below_ref, above_ref, before_ref, after_ref)
    height, channels = out_ref.shape[0], out_ref.shape[1]
    copies = [pltpu.make_async_copy(w_hbm.at[k], w_vmem.at[k], sems.at[k]) for k in range(9)]
    for copy in copies:
        copy.start()
    parts = None
    for dz, dy in itertools.product(range(3), repeat=2):
        rows = jnp.concatenate([source_row(pieces, dz, dy + y) for y in range(height)], axis=1)
        copies[dz * 3 + dy].wait()
        product = jnp.dot(w_vmem[dz * 3 + dy], rows, preferred_element_type=jnp.float32)
        parts = product if parts is None else parts + product
    for y in range(height):
        lanes = slice(y * LANES, (y + 1) * LANES)
        out_ref[y] = (
            parts[channels : 2 * channels, lanes]
            + shift_lanes(parts[:channels, lanes], -1)
            + shift_lanes(parts[2 * channels :, lanes], 1)
        )


def conv_call(pieces, weights):
    _, height, channels, width = pieces[0].shape
    return pl.pallas_call(
        conv_body,
        out_shape=jax.ShapeDtypeStruct((height, channels, width), jnp.float32),
        in_specs=[pl.BlockSpec(memory_space=pltpu.VMEM)] * 5 + [pl.BlockSpec(memory_space=pl.ANY)],
        out_specs=pl.BlockSpec(memory_space=pltpu.VMEM),
        scratch_shapes=[pltpu.VMEM(weights.shape, weights.dtype), pltpu.SemaphoreType.DMA((9,))],
        cost_estimate=pl.CostEstimate(
            flops=2 * 27 * channels * channels * height * width,
            transcendentals=0,
            bytes_accessed=sum(p.size for p in pieces) * 2 + weights.size * 2 + height * channels * width * 4,
        ),
    )(*pieces, weights)


def wgrad_body(block_ref, below_ref, above_ref, before_ref, after_ref, delta_ref, out_ref):
    pieces = (block_ref, below_ref, above_ref, before_ref, after_ref)
    height, channels = delta_ref.shape[0], delta_ref.shape[1]
    stacked = []
    for y in range(height):
        row = delta_ref[y].astype(jnp.float32)
        stacked.append(
            jnp.concatenate([shift_lanes(row, 1), row, shift_lanes(row, -1)], axis=0).astype(
                jnp.bfloat16
            )
        )
    stacked = jnp.concatenate(stacked, axis=1)
    rows_of = lax.broadcasted_iota(jnp.int32, (channels, channels), 0) >> 3
    cols_of = lax.broadcasted_iota(jnp.int32, (channels, channels), 1) >> 3
    mask = jnp.where(rows_of == cols_of, 1.0, 0.0).astype(jnp.float32)
    entry = lax.broadcasted_iota(jnp.int32, (LANES, LANES), 0) & (GW - 1)
    column = lax.broadcasted_iota(jnp.int32, (LANES, LANES), 1)
    totals = [jnp.zeros((channels, LANES), jnp.float32) for _ in range(out_ref.shape[0])]
    for dz, dy in itertools.product(range(3), repeat=2):
        rows = jnp.concatenate([source_row(pieces, dz, dy + y) for y in range(height)], axis=1)
        grads = lax.dot_general(
            stacked, rows, (((1,), (1,)), ((), ())), preferred_element_type=jnp.float32
        )
        for dx in range(3):
            tap = dz * 9 + dy * 3 + dx
            picked = grads[dx * channels : (dx + 1) * channels] * mask
            folded = picked[:, :LANES]
            for start in range(LANES, channels, LANES):
                folded = folded + picked[:, start : start + LANES]
            high = folded.astype(jnp.bfloat16)
            low = (folded - high.astype(jnp.float32)).astype(jnp.bfloat16)
            slot = (tap % TAPS_PER_BLOCK) * GW
            sel = jnp.where(column == entry + slot, 1.0, 0.0).astype(jnp.bfloat16)
            totals[tap // TAPS_PER_BLOCK] += jnp.dot(
                high, sel, preferred_element_type=jnp.float32
            ) + jnp.dot(low, sel, preferred_element_type=jnp.float32)
    for n, total in enumerate(totals):
        out_ref[n] = total


def wgrad_call(pieces, delta):
    height, channels, width = delta.shape
    blocks = -(-27 // TAPS_PER_BLOCK)
    out = pl.pallas_call(
        wgrad_body,
        out_shape=jax.ShapeDtypeStruct((blocks, channels, LANES), jnp.float32),
        in_specs=[pl.BlockSpec(memory_space=pltpu.VMEM)] * 6,
        out_specs=pl.BlockSpec(memory_space=pltpu.VMEM),
        cost_estimate=pl.CostEstimate(
            flops=2 * 27 * channels * channels * height * width + 4 * 27 * channels * LANES * LANES,
            transcendentals=0,
            bytes_accessed=sum(p.size for p in pieces) * 2 + delta.size * 2 + blocks * channels * LANES * 4,
        ),
    )(*pieces, delta)
    return out.transpose(1, 0, 2).reshape(channels, blocks * LANES)[:, : 27 * GW]


def tree_sum(blocks, order):
    steps = []
    for axis, rising in order:
        bits = []
        bit = 1
        while bit < lax.axis_size(axis):
            bits.append(bit)
            bit *= 2
        steps += [(axis, bit) for bit in (bits if rising else bits[::-1])]
    pieces = [block.reshape(-1) for block, _, _ in blocks]
    done = []
    for axis, bit in steps:
        pairs = [(i, i ^ bit) for i in range(lax.axis_size(axis))]
        upper = (lax.axis_index(axis) & bit) != 0
        members = [n for n, (_, axes, _) in enumerate(blocks) if axis in axes]
        keeps, sends = [], []
        for n in members:
            half = pieces[n].shape[0] // 2
            low, high = pieces[n][:half], pieces[n][half:]
            keeps.append(jnp.where(upper, high, low))
            sends.append(jnp.where(upper, low, high))
        got = lax.ppermute(jnp.concatenate(sends), axis, pairs)
        offset = 0
        for n, keep in zip(members, keeps):
            pieces[n] = keep + got[offset : offset + keep.shape[0]]
            offset += keep.shape[0]
        done.append((axis, pairs, upper))
    for axis, pairs, upper in reversed(done):
        members = [n for n, (_, _, axes) in enumerate(blocks) if axis in axes]
        if not members:
            continue
        got = lax.ppermute(jnp.concatenate([pieces[n] for n in members]), axis, pairs)
        offset = 0
        for n in members:
            size = pieces[n].shape[0]
            other = got[offset : offset + size]
            offset += size
            pieces[n] = jnp.where(
                upper,
                jnp.concatenate([other, pieces[n]]),
                jnp.concatenate([pieces[n], other]),
            )
    return pieces


def halo(block):
    count = lax.axis_size("grp")
    up = [(i, i + 1) for i in range(count - 1)]
    down = [(i + 1, i) for i in range(count - 1)]
    depth, height = block.shape[0], block.shape[1]
    below = lax.ppermute(block[depth - 1 :], "grp", up)
    above = lax.ppermute(block[:1], "grp", down)
    count = lax.axis_size("sub")
    up = [(i, i + 1) for i in range(count - 1)]
    down = [(i + 1, i) for i in range(count - 1)]
    last = jnp.concatenate([below[:, height - 1 :], block[:, height - 1 :], above[:, height - 1 :]])
    first = jnp.concatenate([below[:, :1], block[:, :1], above[:, :1]])
    before = lax.ppermute(last, "sub", up)
    after = lax.ppermute(first, "sub", down)
    return block, below, above, before, after


def source_row(pieces, dz, yy):
    block, below, above, before, after = pieces
    height = block.shape[1]
    if yy == 0:
        return before[dz, 0]
    if yy == height + 1:
        return after[dz, 0]
    return (below, block, above)[dz][0, yy - 1]


def silu_slope(values):
    sigma = jax.nn.sigmoid(values)
    return sigma * (1.0 + values * (1.0 - sigma))


def conv_weights(group_weight):
    channels = group_weight.shape[0]
    group_of = jnp.arange(channels) // GW
    mask = (group_of[:, None] == group_of[None, :]).astype(jnp.float32)
    spread = (jnp.arange(GW)[:, None] == jnp.arange(channels)[None, :] % GW).astype(jnp.float32)
    compact = group_weight.reshape(channels, GW, 27).astype(jnp.float32)
    forward = jnp.einsum("ojt,ji->toi", compact, spread)
    backward = jnp.einsum("ji,ojt->tio", spread, compact[:, :, ::-1])
    forward = (forward * mask).astype(group_weight.dtype).reshape(9, 3 * channels, channels)
    backward = (backward * mask).astype(group_weight.dtype).reshape(9, 3 * channels, channels)
    return forward, backward


def rounded(values):
    return lax.reduce_precision(values, exponent_bits=8, mantissa_bits=7).astype(jnp.bfloat16)


def per_device(volume, cotangent, first_weight, group_weight, third_weight):
    channels, depth, height, width = volume.shape
    flattened = volume.reshape(channels, -1)
    contract_lead = (((0,), (0,)), ((), ()))
    contract_tail = (((1,), (1,)), ((), ()))
    total_cells = depth * lax.axis_size("grp") * height * lax.axis_size("sub") * width
    factor = 1.0 / math.sqrt(total_cells)

    def to_rows(block):
        return block.reshape(channels, depth, height, width).transpose(1, 2, 0, 3)

    def from_rows(block):
        return block.transpose(1, 0, 2).reshape(channels, -1)

    forward_kernel, backward_kernel = conv_weights(group_weight)
    first_pre = lax.dot_general(
        first_weight, flattened, contract_lead, preferred_element_type=jnp.float32
    )
    first_act = rounded(jax.nn.silu(first_pre))
    assert depth == 1
    act_pieces = halo(to_rows(first_act))
    group_pre = conv_call(act_pieces, forward_kernel)
    group_act = rounded(jax.nn.silu(group_pre))
    act_flat = from_rows(group_act)
    summed = flattened.astype(jnp.float32) + lax.dot_general(
        third_weight, act_flat, contract_lead, preferred_element_type=jnp.float32
    )
    block_output = jax.nn.silu(summed).astype(jnp.bfloat16).reshape(volume.shape)
    third_delta = rounded(cotangent.reshape(channels, -1).astype(jnp.float32) * silu_slope(summed))
    third_part = lax.dot_general(
        act_flat, third_delta, contract_tail, preferred_element_type=jnp.float32
    )
    hidden_grad = rounded(jnp.dot(third_weight, third_delta, preferred_element_type=jnp.float32))
    group_delta = rounded(to_rows(hidden_grad)[0].astype(jnp.float32) * silu_slope(group_pre))
    delta_pieces = halo(group_delta[None])
    inner_grad = from_rows(rounded(conv_call(delta_pieces, backward_kernel)))
    kernel_part = wgrad_call(act_pieces, group_delta)
    first_delta = rounded(inner_grad.astype(jnp.float32) * silu_slope(first_pre))
    first_part = lax.dot_general(
        flattened, first_delta, contract_tail, preferred_element_type=jnp.float32
    )
    volume_grad = (
        (
            third_delta.astype(jnp.float32)
            + jnp.dot(first_weight, first_delta, preferred_element_type=jnp.float32)
        )
        .astype(jnp.bfloat16)
        .reshape(volume.shape)
    )
    grp_count, sub_count = lax.axis_size("grp"), lax.axis_size("sub")
    digits = grp_count.bit_length() - 1
    reverse = [int(format(n, f"0{digits}b")[::-1], 2) if digits else 0 for n in range(grp_count)]
    blocks = kernel_part.reshape(grp_count, sub_count, -1)
    kernel_laid = jnp.concatenate([blocks[n : n + 1] for n in reverse]).transpose(1, 0, 2)
    first_sum, third_sum, group_sum = tree_sum(
        [
            (first_part, ("sub", "grp"), ("sub", "grp")),
            (third_part, ("sub", "grp"), ("sub", "grp")),
            (kernel_laid, ("sub", "grp"), ("sub",)),
        ],
        (("sub", True), ("grp", True)),
    )
    first_grad = first_sum.reshape(first_part.shape) * factor
    third_grad = third_sum.reshape(third_part.shape) * factor
    own_rows = channels // grp_count
    group_grad = (
        group_sum.reshape(own_rows, 27, GW).transpose(0, 2, 1).reshape(own_rows, GW, 3, 3, 3) * factor
    )
    return (block_output, volume_grad, first_grad, group_grad, third_grad)


def solution(mesh):
    in_specs = (
        P(None, ("rep", "grp"), "sub", None),
        P(None, ("rep", "grp"), "sub", None),
        P(),
        P(),
        P(),
    )
    out_specs = (
        P(None, ("rep", "grp"), "sub", None),
        P(None, ("rep", "grp"), "sub", None),
        P("rep", None),
        P(("rep", "grp"), None, None, None, None),
        P("rep", None),
    )
    return jax.shard_map(
        per_device, mesh=mesh, in_specs=in_specs, out_specs=out_specs, check_vma=False
    )
```

```python
import functools
import itertools
import math

import jax
import jax.numpy as jnp
from jax import lax
from jax.experimental import pallas as pl
from jax.experimental.pallas import tpu as pltpu
from jax.sharding import PartitionSpec as P

GW = 8
LANES = 128
TAPS_PER_BLOCK = 16


def shift_lanes(block, offset):
    lane = lax.broadcasted_iota(jnp.int32, block.shape, 1)
    rolled = pltpu.roll(block, (-offset) % LANES, 1)
    edge = LANES - 1 if offset > 0 else 0
    return jnp.where(lane == edge, jnp.zeros_like(rolled), rolled)


def conv_body(block_ref, below_ref, above_ref, before_ref, after_ref, w_hbm, out_ref, w_vmem, sems):
    pieces = (block_ref, below_ref, above_ref, before_ref, after_ref)
    height, channels = out_ref.shape[0], out_ref.shape[1]
    copies = [pltpu.make_async_copy(w_hbm.at[k], w_vmem.at[k], sems.at[k]) for k in range(9)]
    for copy in copies:
        copy.start()
    sources = [
        jnp.concatenate([source_row(pieces, dz, dy + y) for y in range(height)], axis=1)
        for dz, dy in itertools.product(range(3), repeat=2)
    ]
    chunks = []
    for start in range(0, 3 * channels, LANES):
        total = None
        for k, source in enumerate(sources):
            if start == 0:
                copies[k].wait()
            product = jnp.dot(
                w_vmem[k, start : start + LANES], source, preferred_element_type=jnp.float32
            )
            total = product if total is None else total + product
        chunks.append(total)
    parts = jnp.concatenate(chunks, axis=0)
    for y in range(height):
        lanes = slice(y * LANES, (y + 1) * LANES)
        out_ref[y] = (
            parts[channels : 2 * channels, lanes]
            + shift_lanes(parts[:channels, lanes], -1)
            + shift_lanes(parts[2 * channels :, lanes], 1)
        )


def conv_call(pieces, weights):
    _, height, channels, width = pieces[0].shape
    return pl.pallas_call(
        conv_body,
        out_shape=jax.ShapeDtypeStruct((height, channels, width), jnp.float32),
        in_specs=[pl.BlockSpec(memory_space=pltpu.VMEM)] * 5 + [pl.BlockSpec(memory_space=pl.ANY)],
        out_specs=pl.BlockSpec(memory_space=pltpu.VMEM),
        scratch_shapes=[pltpu.VMEM(weights.shape, weights.dtype), pltpu.SemaphoreType.DMA((9,))],
        cost_estimate=pl.CostEstimate(
            flops=2 * 27 * channels * channels * height * width,
            transcendentals=0,
            bytes_accessed=sum(p.size for p in pieces) * 2 + weights.size * 2 + height * channels * width * 4,
        ),
    )(*pieces, weights)


def wgrad_body(block_ref, below_ref, above_ref, before_ref, after_ref, delta_ref, out_ref):
    pieces = (block_ref, below_ref, above_ref, before_ref, after_ref)
    height, channels = delta_ref.shape[0], delta_ref.shape[1]
    stacked = []
    for y in range(height):
        row = delta_ref[y].astype(jnp.float32)
        stacked.append(
            jnp.concatenate([shift_lanes(row, 1), row, shift_lanes(row, -1)], axis=0).astype(
                jnp.bfloat16
            )
        )
    stacked = jnp.concatenate(stacked, axis=1)
    rows_of = lax.broadcasted_iota(jnp.int32, (channels, channels), 0) >> 3
    cols_of = lax.broadcasted_iota(jnp.int32, (channels, channels), 1) >> 3
    mask = jnp.where(rows_of == cols_of, 1.0, 0.0).astype(jnp.float32)
    entry = lax.broadcasted_iota(jnp.int32, (LANES, LANES), 0) & (GW - 1)
    column = lax.broadcasted_iota(jnp.int32, (LANES, LANES), 1)
    totals = [jnp.zeros((channels, LANES), jnp.float32) for _ in range(out_ref.shape[0])]
    for dz, dy in itertools.product(range(3), repeat=2):
        rows = jnp.concatenate([source_row(pieces, dz, dy + y) for y in range(height)], axis=1)
        grads = lax.dot_general(
            stacked, rows, (((1,), (1,)), ((), ())), preferred_element_type=jnp.float32
        )
        for dx in range(3):
            tap = dz * 9 + dy * 3 + dx
            picked = grads[dx * channels : (dx + 1) * channels] * mask
            folded = picked[:, :LANES]
            for start in range(LANES, channels, LANES):
                folded = folded + picked[:, start : start + LANES]
            high = folded.astype(jnp.bfloat16)
            low = (folded - high.astype(jnp.float32)).astype(jnp.bfloat16)
            slot = (tap % TAPS_PER_BLOCK) * GW
            sel = jnp.where(column == entry + slot, 1.0, 0.0).astype(jnp.bfloat16)
            totals[tap // TAPS_PER_BLOCK] += jnp.dot(
                high, sel, preferred_element_type=jnp.float32
            ) + jnp.dot(low, sel, preferred_element_type=jnp.float32)
    for n, total in enumerate(totals):
        out_ref[n] = total


def wgrad_call(pieces, delta):
    height, channels, width = delta.shape
    blocks = -(-27 // TAPS_PER_BLOCK)
    out = pl.pallas_call(
        wgrad_body,
        out_shape=jax.ShapeDtypeStruct((blocks, channels, LANES), jnp.float32),
        in_specs=[pl.BlockSpec(memory_space=pltpu.VMEM)] * 6,
        out_specs=pl.BlockSpec(memory_space=pltpu.VMEM),
        cost_estimate=pl.CostEstimate(
            flops=2 * 27 * channels * channels * height * width + 4 * 27 * channels * LANES * LANES,
            transcendentals=0,
            bytes_accessed=sum(p.size for p in pieces) * 2 + delta.size * 2 + blocks * channels * LANES * 4,
        ),
    )(*pieces, delta)
    return out.transpose(1, 0, 2).reshape(channels, blocks * LANES)[:, : 27 * GW]


def tree_sum(blocks, order):
    steps = []
    for axis, rising in order:
        bits = []
        bit = 1
        while bit < lax.axis_size(axis):
            bits.append(bit)
            bit *= 2
        steps += [(axis, bit) for bit in (bits if rising else bits[::-1])]
    pieces = [block.reshape(-1) for block, _, _ in blocks]
    done = []
    for axis, bit in steps:
        pairs = [(i, i ^ bit) for i in range(lax.axis_size(axis))]
        upper = (lax.axis_index(axis) & bit) != 0
        members = [n for n, (_, axes, _) in enumerate(blocks) if axis in axes]
        keeps, sends = [], []
        for n in members:
            half = pieces[n].shape[0] // 2
            low, high = pieces[n][:half], pieces[n][half:]
            keeps.append(jnp.where(upper, high, low))
            sends.append(jnp.where(upper, low, high))
        got = lax.ppermute(jnp.concatenate(sends), axis, pairs)
        offset = 0
        for n, keep in zip(members, keeps):
            pieces[n] = keep + got[offset : offset + keep.shape[0]]
            offset += keep.shape[0]
        done.append((axis, pairs, upper))
    for axis, pairs, upper in reversed(done):
        members = [n for n, (_, _, axes) in enumerate(blocks) if axis in axes]
        if not members:
            continue
        got = lax.ppermute(jnp.concatenate([pieces[n] for n in members]), axis, pairs)
        offset = 0
        for n in members:
            size = pieces[n].shape[0]
            other = got[offset : offset + size]
            offset += size
            pieces[n] = jnp.where(
                upper,
                jnp.concatenate([other, pieces[n]]),
                jnp.concatenate([pieces[n], other]),
            )
    return pieces


def halo(block):
    count = lax.axis_size("grp")
    up = [(i, i + 1) for i in range(count - 1)]
    down = [(i + 1, i) for i in range(count - 1)]
    depth, height = block.shape[0], block.shape[1]
    below = lax.ppermute(block[depth - 1 :], "grp", up)
    above = lax.ppermute(block[:1], "grp", down)
    count = lax.axis_size("sub")
    up = [(i, i + 1) for i in range(count - 1)]
    down = [(i + 1, i) for i in range(count - 1)]
    last = jnp.concatenate([below[:, height - 1 :], block[:, height - 1 :], above[:, height - 1 :]])
    first = jnp.concatenate([below[:, :1], block[:, :1], above[:, :1]])
    before = lax.ppermute(last, "sub", up)
    after = lax.ppermute(first, "sub", down)
    return block, below, above, before, after


def source_row(pieces, dz, yy):
    block, below, above, before, after = pieces
    height = block.shape[1]
    if yy == 0:
        return before[dz, 0]
    if yy == height + 1:
        return after[dz, 0]
    return (below, block, above)[dz][0, yy - 1]


def silu_slope(values):
    sigma = jax.nn.sigmoid(values)
    return sigma * (1.0 + values * (1.0 - sigma))


def conv_weights(group_weight):
    channels = group_weight.shape[0]
    group_of = jnp.arange(channels) // GW
    mask = (group_of[:, None] == group_of[None, :]).astype(jnp.float32)
    spread = (jnp.arange(GW)[:, None] == jnp.arange(channels)[None, :] % GW).astype(jnp.float32)
    compact = group_weight.reshape(channels, GW, 27).astype(jnp.float32)
    forward = jnp.einsum("ojt,ji->toi", compact, spread)
    backward = jnp.einsum("ji,ojt->tio", spread, compact[:, :, ::-1])
    forward = (forward * mask).astype(group_weight.dtype).reshape(9, 3 * channels, channels)
    backward = (backward * mask).astype(group_weight.dtype).reshape(9, 3 * channels, channels)
    return forward, backward


def rounded(values):
    return lax.reduce_precision(values, exponent_bits=8, mantissa_bits=7).astype(jnp.bfloat16)


def per_device(volume, cotangent, first_weight, group_weight, third_weight):
    channels, depth, height, width = volume.shape
    flattened = volume.reshape(channels, -1)
    contract_lead = (((0,), (0,)), ((), ()))
    contract_tail = (((1,), (1,)), ((), ()))
    total_cells = depth * lax.axis_size("grp") * height * lax.axis_size("sub") * width
    factor = 1.0 / math.sqrt(total_cells)

    def to_rows(block):
        return block.reshape(channels, depth, height, width).transpose(1, 2, 0, 3)

    def from_rows(block):
        return block.transpose(1, 0, 2).reshape(channels, -1)

    forward_kernel, backward_kernel = conv_weights(group_weight)
    first_pre = lax.dot_general(
        first_weight, flattened, contract_lead, preferred_element_type=jnp.float32
    )
    first_act = rounded(jax.nn.silu(first_pre))
    assert depth == 1
    act_pieces = halo(to_rows(first_act))
    group_pre = conv_call(act_pieces, forward_kernel)
    group_act = rounded(jax.nn.silu(group_pre))
    act_flat = from_rows(group_act)
    summed = flattened.astype(jnp.float32) + lax.dot_general(
        third_weight, act_flat, contract_lead, preferred_element_type=jnp.float32
    )
    block_output = jax.nn.silu(summed).astype(jnp.bfloat16).reshape(volume.shape)
    third_delta = rounded(cotangent.reshape(channels, -1).astype(jnp.float32) * silu_slope(summed))
    third_part = lax.dot_general(
        act_flat, third_delta, contract_tail, preferred_element_type=jnp.float32
    )
    hidden_grad = rounded(jnp.dot(third_weight, third_delta, preferred_element_type=jnp.float32))
    group_delta = rounded(to_rows(hidden_grad)[0].astype(jnp.float32) * silu_slope(group_pre))
    delta_pieces = halo(group_delta[None])
    inner_grad = from_rows(rounded(conv_call(delta_pieces, backward_kernel)))
    kernel_part = wgrad_call(act_pieces, group_delta)
    first_delta = rounded(inner_grad.astype(jnp.float32) * silu_slope(first_pre))
    first_part = lax.dot_general(
        flattened, first_delta, contract_tail, preferred_element_type=jnp.float32
    )
    volume_grad = (
        (
            third_delta.astype(jnp.float32)
            + jnp.dot(first_weight, first_delta, preferred_element_type=jnp.float32)
        )
        .astype(jnp.bfloat16)
        .reshape(volume.shape)
    )
    grp_count, sub_count = lax.axis_size("grp"), lax.axis_size("sub")
    digits = grp_count.bit_length() - 1
    reverse = [int(format(n, f"0{digits}b")[::-1], 2) if digits else 0 for n in range(grp_count)]
    blocks = kernel_part.reshape(grp_count, sub_count, -1)
    kernel_laid = jnp.concatenate([blocks[n : n + 1] for n in reverse]).transpose(1, 0, 2)
    first_sum, third_sum, group_sum = tree_sum(
        [
            (first_part, ("sub", "grp"), ("sub", "grp")),
            (third_part, ("sub", "grp"), ("sub", "grp")),
            (kernel_laid, ("sub", "grp"), ("sub",)),
        ],
        (("sub", True), ("grp", True)),
    )
    first_grad = first_sum.reshape(first_part.shape) * factor
    third_grad = third_sum.reshape(third_part.shape) * factor
    own_rows = channels // grp_count
    group_grad = (
        group_sum.reshape(own_rows, 27, GW).transpose(0, 2, 1).reshape(own_rows, GW, 3, 3, 3) * factor
    )
    return (block_output, volume_grad, first_grad, group_grad, third_grad)


def solution(mesh):
    in_specs = (
        P(None, ("rep", "grp"), "sub", None),
        P(None, ("rep", "grp"), "sub", None),
        P(),
        P(),
        P(),
    )
    out_specs = (
        P(None, ("rep", "grp"), "sub", None),
        P(None, ("rep", "grp"), "sub", None),
        P("rep", None),
        P(("rep", "grp"), None, None, None, None),
        P("rep", None),
    )
    return jax.shard_map(
        per_device, mesh=mesh, in_specs=in_specs, out_specs=out_specs, check_vma=False
    )
```

```python
import functools
import itertools
import math

import jax
import jax.numpy as jnp
from jax import lax
from jax.experimental import pallas as pl
from jax.experimental.pallas import tpu as pltpu
from jax.sharding import PartitionSpec as P

GW = 8
LANES = 128
TAPS_PER_BLOCK = 16


def shift_lanes(block, offset):
    lane = lax.broadcasted_iota(jnp.int32, block.shape, 1)
    rolled = pltpu.roll(block, (-offset) % LANES, 1)
    edge = LANES - 1 if offset > 0 else 0
    return jnp.where(lane == edge, jnp.zeros_like(rolled), rolled)


def conv_body(block_ref, below_ref, above_ref, before_ref, after_ref, w_hbm, out_ref, w_vmem, sems):
    pieces = (block_ref, below_ref, above_ref, before_ref, after_ref)
    height, channels = out_ref.shape[0], out_ref.shape[1]
    copies = [pltpu.make_async_copy(w_hbm.at[k], w_vmem.at[k], sems.at[k]) for k in range(9)]
    for copy in copies:
        copy.start()
    sources = [
        jnp.concatenate([source_row(pieces, dz, dy + y) for y in range(height)], axis=1)
        for dz, dy in itertools.product(range(3), repeat=2)
    ]
    out_group = lax.broadcasted_iota(jnp.int32, (LANES, channels), 0) >> 3
    in_group = lax.broadcasted_iota(jnp.int32, (LANES, channels), 1) >> 3
    chunks = []
    for start in range(0, 3 * channels, LANES):
        same = out_group + (start % channels) // GW == in_group
        total = None
        for k, source in enumerate(sources):
            if start == 0:
                copies[k].wait()
            weight = w_vmem[k, start : start + LANES]
            weight = jnp.where(same, weight, jnp.zeros_like(weight))
            product = jnp.dot(weight, source, preferred_element_type=jnp.float32)
            total = product if total is None else total + product
        chunks.append(total)
    parts = jnp.concatenate(chunks, axis=0)
    for y in range(height):
        lanes = slice(y * LANES, (y + 1) * LANES)
        out_ref[y] = (
            parts[channels : 2 * channels, lanes]
            + shift_lanes(parts[:channels, lanes], -1)
            + shift_lanes(parts[2 * channels :, lanes], 1)
        )


def conv_call(pieces, weights):
    _, height, channels, width = pieces[0].shape
    return pl.pallas_call(
        conv_body,
        out_shape=jax.ShapeDtypeStruct((height, channels, width), jnp.float32),
        in_specs=[pl.BlockSpec(memory_space=pltpu.VMEM)] * 5 + [pl.BlockSpec(memory_space=pl.ANY)],
        out_specs=pl.BlockSpec(memory_space=pltpu.VMEM),
        scratch_shapes=[pltpu.VMEM(weights.shape, weights.dtype), pltpu.SemaphoreType.DMA((9,))],
        cost_estimate=pl.CostEstimate(
            flops=2 * 27 * channels * channels * height * width,
            transcendentals=0,
            bytes_accessed=sum(p.size for p in pieces) * 2 + weights.size * 2 + height * channels * width * 4,
        ),
    )(*pieces, weights)


def wgrad_body(block_ref, below_ref, above_ref, before_ref, after_ref, delta_ref, out_ref):
    pieces = (block_ref, below_ref, above_ref, before_ref, after_ref)
    height, channels = delta_ref.shape[0], delta_ref.shape[1]
    stacked = []
    for y in range(height):
        row = delta_ref[y].astype(jnp.float32)
        stacked.append(
            jnp.concatenate([shift_lanes(row, 1), row, shift_lanes(row, -1)], axis=0).astype(
                jnp.bfloat16
            )
        )
    stacked = jnp.concatenate(stacked, axis=1)
    rows_of = lax.broadcasted_iota(jnp.int32, (channels, channels), 0) >> 3
    cols_of = lax.broadcasted_iota(jnp.int32, (channels, channels), 1) >> 3
    mask = jnp.where(rows_of == cols_of, 1.0, 0.0).astype(jnp.float32)
    entry = lax.broadcasted_iota(jnp.int32, (LANES, LANES), 0) & (GW - 1)
    column = lax.broadcasted_iota(jnp.int32, (LANES, LANES), 1)
    totals = [jnp.zeros((channels, LANES), jnp.float32) for _ in range(out_ref.shape[0])]
    for dz, dy in itertools.product(range(3), repeat=2):
        rows = jnp.concatenate([source_row(pieces, dz, dy + y) for y in range(height)], axis=1)
        grads = lax.dot_general(
            stacked, rows, (((1,), (1,)), ((), ())), preferred_element_type=jnp.float32
        )
        for dx in range(3):
            tap = dz * 9 + dy * 3 + dx
            picked = grads[dx * channels : (dx + 1) * channels] * mask
            folded = picked[:, :LANES]
            for start in range(LANES, channels, LANES):
                folded = folded + picked[:, start : start + LANES]
            high = folded.astype(jnp.bfloat16)
            low = (folded - high.astype(jnp.float32)).astype(jnp.bfloat16)
            slot = (tap % TAPS_PER_BLOCK) * GW
            sel = jnp.where(column == entry + slot, 1.0, 0.0).astype(jnp.bfloat16)
            totals[tap // TAPS_PER_BLOCK] += jnp.dot(
                high, sel, preferred_element_type=jnp.float32
            ) + jnp.dot(low, sel, preferred_element_type=jnp.float32)
    for n, total in enumerate(totals):
        out_ref[n] = total


def wgrad_call(pieces, delta):
    height, channels, width = delta.shape
    blocks = -(-27 // TAPS_PER_BLOCK)
    out = pl.pallas_call(
        wgrad_body,
        out_shape=jax.ShapeDtypeStruct((blocks, channels, LANES), jnp.float32),
        in_specs=[pl.BlockSpec(memory_space=pltpu.VMEM)] * 6,
        out_specs=pl.BlockSpec(memory_space=pltpu.VMEM),
        cost_estimate=pl.CostEstimate(
            flops=2 * 27 * channels * channels * height * width + 4 * 27 * channels * LANES * LANES,
            transcendentals=0,
            bytes_accessed=sum(p.size for p in pieces) * 2 + delta.size * 2 + blocks * channels * LANES * 4,
        ),
    )(*pieces, delta)
    return out.transpose(1, 0, 2).reshape(channels, blocks * LANES)[:, : 27 * GW]


def tree_sum(blocks, order):
    steps = []
    for axis, rising in order:
        bits = []
        bit = 1
        while bit < lax.axis_size(axis):
            bits.append(bit)
            bit *= 2
        steps += [(axis, bit) for bit in (bits if rising else bits[::-1])]
    pieces = [block.reshape(-1) for block, _, _ in blocks]
    done = []
    for axis, bit in steps:
        pairs = [(i, i ^ bit) for i in range(lax.axis_size(axis))]
        upper = (lax.axis_index(axis) & bit) != 0
        members = [n for n, (_, axes, _) in enumerate(blocks) if axis in axes]
        keeps, sends = [], []
        for n in members:
            half = pieces[n].shape[0] // 2
            low, high = pieces[n][:half], pieces[n][half:]
            keeps.append(jnp.where(upper, high, low))
            sends.append(jnp.where(upper, low, high))
        got = lax.ppermute(jnp.concatenate(sends), axis, pairs)
        offset = 0
        for n, keep in zip(members, keeps):
            pieces[n] = keep + got[offset : offset + keep.shape[0]]
            offset += keep.shape[0]
        done.append((axis, pairs, upper))
    for axis, pairs, upper in reversed(done):
        members = [n for n, (_, _, axes) in enumerate(blocks) if axis in axes]
        if not members:
            continue
        got = lax.ppermute(jnp.concatenate([pieces[n] for n in members]), axis, pairs)
        offset = 0
        for n in members:
            size = pieces[n].shape[0]
            other = got[offset : offset + size]
            offset += size
            pieces[n] = jnp.where(
                upper,
                jnp.concatenate([other, pieces[n]]),
                jnp.concatenate([pieces[n], other]),
            )
    return pieces


def halo(block):
    count = lax.axis_size("grp")
    up = [(i, i + 1) for i in range(count - 1)]
    down = [(i + 1, i) for i in range(count - 1)]
    depth, height = block.shape[0], block.shape[1]
    below = lax.ppermute(block[depth - 1 :], "grp", up)
    above = lax.ppermute(block[:1], "grp", down)
    count = lax.axis_size("sub")
    up = [(i, i + 1) for i in range(count - 1)]
    down = [(i + 1, i) for i in range(count - 1)]
    last = jnp.concatenate([below[:, height - 1 :], block[:, height - 1 :], above[:, height - 1 :]])
    first = jnp.concatenate([below[:, :1], block[:, :1], above[:, :1]])
    before = lax.ppermute(last, "sub", up)
    after = lax.ppermute(first, "sub", down)
    return block, below, above, before, after


def source_row(pieces, dz, yy):
    block, below, above, before, after = pieces
    height = block.shape[1]
    if yy == 0:
        return before[dz, 0]
    if yy == height + 1:
        return after[dz, 0]
    return (below, block, above)[dz][0, yy - 1]


def silu_slope(values):
    sigma = jax.nn.sigmoid(values)
    return sigma * (1.0 + values * (1.0 - sigma))


def conv_weights(group_weight):
    channels = group_weight.shape[0]
    spread = (jnp.arange(GW)[:, None] == jnp.arange(channels)[None, :] % GW).astype(jnp.float32)
    compact = group_weight.reshape(channels, GW, 27).astype(jnp.float32)
    forward = jnp.einsum("ojt,ji->toi", compact, spread)
    backward = jnp.einsum("ji,ojt->tio", spread, compact[:, :, ::-1])
    forward = forward.astype(group_weight.dtype).reshape(9, 3 * channels, channels)
    backward = backward.astype(group_weight.dtype).reshape(9, 3 * channels, channels)
    return forward, backward


def rounded(values):
    return lax.reduce_precision(values, exponent_bits=8, mantissa_bits=7).astype(jnp.bfloat16)


def per_device(volume, cotangent, first_weight, group_weight, third_weight):
    channels, depth, height, width = volume.shape
    flattened = volume.reshape(channels, -1)
    contract_lead = (((0,), (0,)), ((), ()))
    contract_tail = (((1,), (1,)), ((), ()))
    total_cells = depth * lax.axis_size("grp") * height * lax.axis_size("sub") * width
    factor = 1.0 / math.sqrt(total_cells)

    def to_rows(block):
        return block.reshape(channels, depth, height, width).transpose(1, 2, 0, 3)

    def from_rows(block):
        return block.transpose(1, 0, 2).reshape(channels, -1)

    forward_kernel, backward_kernel = conv_weights(group_weight)
    first_pre = lax.dot_general(
        first_weight, flattened, contract_lead, preferred_element_type=jnp.float32
    )
    first_act = rounded(jax.nn.silu(first_pre))
    assert depth == 1
    act_pieces = halo(to_rows(first_act))
    group_pre = conv_call(act_pieces, forward_kernel)
    group_act = rounded(jax.nn.silu(group_pre))
    act_flat = from_rows(group_act)
    summed = flattened.astype(jnp.float32) + lax.dot_general(
        third_weight, act_flat, contract_lead, preferred_element_type=jnp.float32
    )
    block_output = jax.nn.silu(summed).astype(jnp.bfloat16).reshape(volume.shape)
    third_delta = rounded(cotangent.reshape(channels, -1).astype(jnp.float32) * silu_slope(summed))
    third_part = lax.dot_general(
        act_flat, third_delta, contract_tail, preferred_element_type=jnp.float32
    )
    hidden_grad = rounded(jnp.dot(third_weight, third_delta, preferred_element_type=jnp.float32))
    group_delta = rounded(to_rows(hidden_grad)[0].astype(jnp.float32) * silu_slope(group_pre))
    delta_pieces = halo(group_delta[None])
    inner_grad = from_rows(rounded(conv_call(delta_pieces, backward_kernel)))
    kernel_part = wgrad_call(act_pieces, group_delta)
    first_delta = rounded(inner_grad.astype(jnp.float32) * silu_slope(first_pre))
    first_part = lax.dot_general(
        flattened, first_delta, contract_tail, preferred_element_type=jnp.float32
    )
    volume_grad = (
        (
            third_delta.astype(jnp.float32)
            + jnp.dot(first_weight, first_delta, preferred_element_type=jnp.float32)
        )
        .astype(jnp.bfloat16)
        .reshape(volume.shape)
    )
    grp_count, sub_count = lax.axis_size("grp"), lax.axis_size("sub")
    digits = grp_count.bit_length() - 1
    reverse = [int(format(n, f"0{digits}b")[::-1], 2) if digits else 0 for n in range(grp_count)]
    blocks = kernel_part.reshape(grp_count, sub_count, -1)
    kernel_laid = jnp.concatenate([blocks[n : n + 1] for n in reverse]).transpose(1, 0, 2)
    first_sum, third_sum, group_sum = tree_sum(
        [
            (first_part, ("sub", "grp"), ("sub", "grp")),
            (third_part, ("sub", "grp"), ("sub", "grp")),
            (kernel_laid, ("sub", "grp"), ("sub",)),
        ],
        (("sub", True), ("grp", True)),
    )
    first_grad = first_sum.reshape(first_part.shape) * factor
    third_grad = third_sum.reshape(third_part.shape) * factor
    own_rows = channels // grp_count
    group_grad = (
        group_sum.reshape(own_rows, 27, GW).transpose(0, 2, 1).reshape(own_rows, GW, 3, 3, 3) * factor
    )
    return (block_output, volume_grad, first_grad, group_grad, third_grad)


def solution(mesh):
    in_specs = (
        P(None, ("rep", "grp"), "sub", None),
        P(None, ("rep", "grp"), "sub", None),
        P(),
        P(),
        P(),
    )
    out_specs = (
        P(None, ("rep", "grp"), "sub", None),
        P(None, ("rep", "grp"), "sub", None),
        P("rep", None),
        P(("rep", "grp"), None, None, None, None),
        P("rep", None),
    )
    return jax.shard_map(
        per_device, mesh=mesh, in_specs=in_specs, out_specs=out_specs, check_vma=False
    )
```

```python
import functools
import itertools
import math

import jax
import jax.numpy as jnp
from jax import lax
from jax.experimental import pallas as pl
from jax.experimental.pallas import tpu as pltpu
from jax.sharding import PartitionSpec as P

GW = 8
LANES = 128
TAPS_PER_BLOCK = 16


def shift_lanes(block, offset):
    lane = lax.broadcasted_iota(jnp.int32, block.shape, 1)
    rolled = pltpu.roll(block, (-offset) % LANES, 1)
    edge = LANES - 1 if offset > 0 else 0
    return jnp.where(lane == edge, jnp.zeros_like(rolled), rolled)


def conv_body(block_ref, below_ref, above_ref, before_ref, after_ref, w_hbm, out_ref, w_vmem, sems):
    pieces = (block_ref, below_ref, above_ref, before_ref, after_ref)
    height, channels = out_ref.shape[0], out_ref.shape[1]
    copies = [pltpu.make_async_copy(w_hbm.at[k], w_vmem.at[k], sems.at[k]) for k in range(9)]
    for copy in copies:
        copy.start()
    sources = [
        jnp.concatenate([source_row(pieces, dz, dy + y) for y in range(height)], axis=1)
        for dz, dy in itertools.product(range(3), repeat=2)
    ]
    out_group = lax.broadcasted_iota(jnp.int32, (LANES, channels), 0) >> 3
    in_group = lax.broadcasted_iota(jnp.int32, (LANES, channels), 1) >> 3
    chunks = []
    for start in range(0, 3 * channels, LANES):
        same = out_group + (start % channels) // GW == in_group
        total = None
        for k, source in enumerate(sources):
            if start == 0:
                copies[k].wait()
            weight = w_vmem[k, start : start + LANES]
            weight = jnp.where(same, weight, jnp.zeros_like(weight))
            product = jnp.dot(weight, source, preferred_element_type=jnp.float32)
            total = product if total is None else total + product
        chunks.append(total)
    parts = jnp.concatenate(chunks, axis=0)
    for y in range(height):
        lanes = slice(y * LANES, (y + 1) * LANES)
        out_ref[y] = (
            parts[channels : 2 * channels, lanes]
            + shift_lanes(parts[:channels, lanes], -1)
            + shift_lanes(parts[2 * channels :, lanes], 1)
        )


def conv_call(pieces, weights):
    _, height, channels, width = pieces[0].shape
    return pl.pallas_call(
        conv_body,
        out_shape=jax.ShapeDtypeStruct((height, channels, width), jnp.float32),
        in_specs=[pl.BlockSpec(memory_space=pltpu.VMEM)] * 5 + [pl.BlockSpec(memory_space=pl.ANY)],
        out_specs=pl.BlockSpec(memory_space=pltpu.VMEM),
        scratch_shapes=[pltpu.VMEM(weights.shape, weights.dtype), pltpu.SemaphoreType.DMA((9,))],
        cost_estimate=pl.CostEstimate(
            flops=2 * 27 * channels * channels * height * width,
            transcendentals=0,
            bytes_accessed=sum(p.size for p in pieces) * 2 + weights.size * 2 + height * channels * width * 4,
        ),
    )(*pieces, weights)


def wgrad_body(block_ref, below_ref, above_ref, before_ref, after_ref, delta_ref, out_ref):
    pieces = (block_ref, below_ref, above_ref, before_ref, after_ref)
    height, channels = delta_ref.shape[0], delta_ref.shape[1]
    stacked = []
    for y in range(height):
        row = delta_ref[y].astype(jnp.float32)
        stacked.append(
            jnp.concatenate([shift_lanes(row, 1), row, shift_lanes(row, -1)], axis=0).astype(
                jnp.bfloat16
            )
        )
    stacked = jnp.concatenate(stacked, axis=1)
    rows_of = lax.broadcasted_iota(jnp.int32, (channels, channels), 0) >> 3
    cols_of = lax.broadcasted_iota(jnp.int32, (channels, channels), 1) >> 3
    mask = jnp.where(rows_of == cols_of, 1.0, 0.0).astype(jnp.float32)
    entry = lax.broadcasted_iota(jnp.int32, (LANES, LANES), 0) & (GW - 1)
    column = lax.broadcasted_iota(jnp.int32, (LANES, LANES), 1)
    totals = [jnp.zeros((channels, LANES), jnp.float32) for _ in range(out_ref.shape[0])]
    for dz, dy in itertools.product(range(3), repeat=2):
        rows = jnp.concatenate([source_row(pieces, dz, dy + y) for y in range(height)], axis=1)
        grads = lax.dot_general(
            stacked, rows, (((1,), (1,)), ((), ())), preferred_element_type=jnp.float32
        )
        for dx in range(3):
            tap = dz * 9 + dy * 3 + dx
            picked = grads[dx * channels : (dx + 1) * channels] * mask
            folded = picked[:, :LANES]
            for start in range(LANES, channels, LANES):
                folded = folded + picked[:, start : start + LANES]
            high = folded.astype(jnp.bfloat16)
            low = (folded - high.astype(jnp.float32)).astype(jnp.bfloat16)
            slot = (tap % TAPS_PER_BLOCK) * GW
            sel = jnp.where(column == entry + slot, 1.0, 0.0).astype(jnp.bfloat16)
            totals[tap // TAPS_PER_BLOCK] += jnp.dot(
                high, sel, preferred_element_type=jnp.float32
            ) + jnp.dot(low, sel, preferred_element_type=jnp.float32)
    for n, total in enumerate(totals):
        out_ref[n] = total


def wgrad_call(pieces, delta):
    height, channels, width = delta.shape
    blocks = -(-27 // TAPS_PER_BLOCK)
    out = pl.pallas_call(
        wgrad_body,
        out_shape=jax.ShapeDtypeStruct((blocks, channels, LANES), jnp.float32),
        in_specs=[pl.BlockSpec(memory_space=pltpu.VMEM)] * 6,
        out_specs=pl.BlockSpec(memory_space=pltpu.VMEM),
        cost_estimate=pl.CostEstimate(
            flops=2 * 27 * channels * channels * height * width + 4 * 27 * channels * LANES * LANES,
            transcendentals=0,
            bytes_accessed=sum(p.size for p in pieces) * 2 + delta.size * 2 + blocks * channels * LANES * 4,
        ),
    )(*pieces, delta)
    return out.transpose(1, 0, 2).reshape(channels, blocks * LANES)[:, : 27 * GW]


def tree_sum(blocks, order):
    steps = []
    for axis, rising in order:
        bits = []
        bit = 1
        while bit < lax.axis_size(axis):
            bits.append(bit)
            bit *= 2
        steps += [(axis, bit) for bit in (bits if rising else bits[::-1])]
    pieces = [block.reshape(-1) for block, _, _ in blocks]
    done = []
    for axis, bit in steps:
        pairs = [(i, i ^ bit) for i in range(lax.axis_size(axis))]
        upper = (lax.axis_index(axis) & bit) != 0
        members = [n for n, (_, axes, _) in enumerate(blocks) if axis in axes]
        keeps, sends = [], []
        for n in members:
            half = pieces[n].shape[0] // 2
            low, high = pieces[n][:half], pieces[n][half:]
            keeps.append(jnp.where(upper, high, low))
            sends.append(jnp.where(upper, low, high))
        got = lax.ppermute(jnp.concatenate(sends), axis, pairs)
        offset = 0
        for n, keep in zip(members, keeps):
            pieces[n] = keep + got[offset : offset + keep.shape[0]]
            offset += keep.shape[0]
        done.append((axis, pairs, upper))
    for axis, pairs, upper in reversed(done):
        members = [n for n, (_, _, axes) in enumerate(blocks) if axis in axes]
        if not members:
            continue
        got = lax.ppermute(jnp.concatenate([pieces[n] for n in members]), axis, pairs)
        offset = 0
        for n in members:
            size = pieces[n].shape[0]
            other = got[offset : offset + size]
            offset += size
            pieces[n] = jnp.where(
                upper,
                jnp.concatenate([other, pieces[n]]),
                jnp.concatenate([pieces[n], other]),
            )
    return pieces


def halo(block):
    count = lax.axis_size("grp")
    up = [(i, i + 1) for i in range(count - 1)]
    down = [(i + 1, i) for i in range(count - 1)]
    depth, height = block.shape[0], block.shape[1]
    below = lax.ppermute(block[depth - 1 :], "grp", up)
    above = lax.ppermute(block[:1], "grp", down)
    count = lax.axis_size("sub")
    up = [(i, i + 1) for i in range(count - 1)]
    down = [(i + 1, i) for i in range(count - 1)]
    last = jnp.concatenate([below[:, height - 1 :], block[:, height - 1 :], above[:, height - 1 :]])
    first = jnp.concatenate([below[:, :1], block[:, :1], above[:, :1]])
    before = lax.ppermute(last, "sub", up)
    after = lax.ppermute(first, "sub", down)
    return block, below, above, before, after


def source_row(pieces, dz, yy):
    block, below, above, before, after = pieces
    height = block.shape[1]
    if yy == 0:
        return before[dz, 0]
    if yy == height + 1:
        return after[dz, 0]
    return (below, block, above)[dz][0, yy - 1]


def silu_slope(values):
    sigma = jax.nn.sigmoid(values)
    return sigma * (1.0 + values * (1.0 - sigma))


def conv_weights(group_weight):
    channels = group_weight.shape[0]
    spread = (jnp.arange(GW)[:, None] == jnp.arange(channels)[None, :] % GW).astype(jnp.float32)
    compact = group_weight.reshape(channels, GW, 27).astype(jnp.float32)
    forward = jnp.einsum("ojt,ji->toi", compact, spread)
    backward = jnp.einsum("ji,ojt->tio", spread, compact[:, :, ::-1])
    forward = forward.astype(group_weight.dtype).reshape(9, 3 * channels, channels)
    backward = backward.astype(group_weight.dtype).reshape(9, 3 * channels, channels)
    return forward, backward


def rounded(values):
    return lax.reduce_precision(values, exponent_bits=8, mantissa_bits=7).astype(jnp.bfloat16)


def per_device(volume, cotangent, first_weight, group_weight, third_weight):
    channels, depth, height, width = volume.shape
    flattened = volume.reshape(channels, -1)
    contract_lead = (((0,), (0,)), ((), ()))
    contract_tail = (((1,), (1,)), ((), ()))
    total_cells = depth * lax.axis_size("grp") * height * lax.axis_size("sub") * width
    factor = 1.0 / math.sqrt(total_cells)

    def to_rows(block):
        return block.reshape(channels, depth, height, width).transpose(1, 2, 0, 3)

    def from_rows(block):
        return block.transpose(1, 0, 2).reshape(channels, -1)

    forward_kernel, _ = conv_weights(group_weight)
    first_pre = lax.dot_general(
        first_weight, flattened, contract_lead, preferred_element_type=jnp.float32
    )
    first_act = rounded(jax.nn.silu(first_pre))
    assert depth == 1
    act_pieces = halo(to_rows(first_act))
    group_pre = conv_call(act_pieces, forward_kernel)
    late_weight, group_pre = lax.optimization_barrier((group_weight, group_pre))
    _, backward_kernel = conv_weights(late_weight)
    group_act = rounded(jax.nn.silu(group_pre))
    act_flat = from_rows(group_act)
    summed = flattened.astype(jnp.float32) + lax.dot_general(
        third_weight, act_flat, contract_lead, preferred_element_type=jnp.float32
    )
    block_output = jax.nn.silu(summed).astype(jnp.bfloat16).reshape(volume.shape)
    third_delta = rounded(cotangent.reshape(channels, -1).astype(jnp.float32) * silu_slope(summed))
    third_part = lax.dot_general(
        act_flat, third_delta, contract_tail, preferred_element_type=jnp.float32
    )
    hidden_grad = rounded(jnp.dot(third_weight, third_delta, preferred_element_type=jnp.float32))
    group_delta = rounded(to_rows(hidden_grad)[0].astype(jnp.float32) * silu_slope(group_pre))
    delta_pieces = halo(group_delta[None])
    inner_grad = from_rows(rounded(conv_call(delta_pieces, backward_kernel)))
    kernel_part = wgrad_call(act_pieces, group_delta)
    first_delta = rounded(inner_grad.astype(jnp.float32) * silu_slope(first_pre))
    first_part = lax.dot_general(
        flattened, first_delta, contract_tail, preferred_element_type=jnp.float32
    )
    volume_grad = (
        (
            third_delta.astype(jnp.float32)
            + jnp.dot(first_weight, first_delta, preferred_element_type=jnp.float32)
        )
        .astype(jnp.bfloat16)
        .reshape(volume.shape)
    )
    grp_count, sub_count = lax.axis_size("grp"), lax.axis_size("sub")
    digits = grp_count.bit_length() - 1
    reverse = [int(format(n, f"0{digits}b")[::-1], 2) if digits else 0 for n in range(grp_count)]
    blocks = kernel_part.reshape(grp_count, sub_count, -1)
    kernel_laid = jnp.concatenate([blocks[n : n + 1] for n in reverse]).transpose(1, 0, 2)
    first_sum, third_sum, group_sum = tree_sum(
        [
            (first_part, ("sub", "grp"), ("sub", "grp")),
            (third_part, ("sub", "grp"), ("sub", "grp")),
            (kernel_laid, ("sub", "grp"), ("sub",)),
        ],
        (("sub", True), ("grp", True)),
    )
    first_grad = first_sum.reshape(first_part.shape) * factor
    third_grad = third_sum.reshape(third_part.shape) * factor
    own_rows = channels // grp_count
    group_grad = (
        group_sum.reshape(own_rows, 27, GW).transpose(0, 2, 1).reshape(own_rows, GW, 3, 3, 3) * factor
    )
    return (block_output, volume_grad, first_grad, group_grad, third_grad)


def solution(mesh):
    in_specs = (
        P(None, ("rep", "grp"), "sub", None),
        P(None, ("rep", "grp"), "sub", None),
        P(),
        P(),
        P(),
    )
    out_specs = (
        P(None, ("rep", "grp"), "sub", None),
        P(None, ("rep", "grp"), "sub", None),
        P("rep", None),
        P(("rep", "grp"), None, None, None, None),
        P("rep", None),
    )
    return jax.shard_map(
        per_device, mesh=mesh, in_specs=in_specs, out_specs=out_specs, check_vma=False
    )
```

```python
import functools
import itertools
import math

import jax
import jax.numpy as jnp
from jax import lax
from jax.experimental import pallas as pl
from jax.experimental.pallas import tpu as pltpu
from jax.sharding import PartitionSpec as P

GW = 8
LANES = 128
TAPS_PER_BLOCK = 16


def shift_lanes(block, offset):
    lane = lax.broadcasted_iota(jnp.int32, block.shape, 1)
    rolled = pltpu.roll(block, (-offset) % LANES, 1)
    edge = LANES - 1 if offset > 0 else 0
    return jnp.where(lane == edge, jnp.zeros_like(rolled), rolled)


def conv_body(block_ref, below_ref, above_ref, before_ref, after_ref, w_hbm, out_ref, w_vmem, sems):
    pieces = (block_ref, below_ref, above_ref, before_ref, after_ref)
    height, channels = out_ref.shape[0], out_ref.shape[1]
    copies = [pltpu.make_async_copy(w_hbm.at[k], w_vmem.at[k], sems.at[k]) for k in range(9)]
    for copy in copies:
        copy.start()
    sources = [
        jnp.concatenate([source_row(pieces, dz, dy + y) for y in range(height)], axis=1)
        for dz, dy in itertools.product(range(3), repeat=2)
    ]
    out_group = lax.broadcasted_iota(jnp.int32, (LANES, channels), 0) >> 3
    in_group = lax.broadcasted_iota(jnp.int32, (LANES, channels), 1) >> 3
    chunks = []
    for start in range(0, 3 * channels, LANES):
        same = out_group + (start % channels) // GW == in_group
        total = None
        for k, source in enumerate(sources):
            if start == 0:
                copies[k].wait()
            weight = w_vmem[k, start : start + LANES]
            weight = jnp.where(same, weight, jnp.zeros_like(weight))
            product = jnp.dot(weight, source, preferred_element_type=jnp.float32)
            total = product if total is None else total + product
        chunks.append(total)
    parts = jnp.concatenate(chunks, axis=0)
    for y in range(height):
        lanes = slice(y * LANES, (y + 1) * LANES)
        out_ref[y] = (
            parts[channels : 2 * channels, lanes]
            + shift_lanes(parts[:channels, lanes], -1)
            + shift_lanes(parts[2 * channels :, lanes], 1)
        )


def conv_call(pieces, weights):
    _, height, channels, width = pieces[0].shape
    return pl.pallas_call(
        conv_body,
        out_shape=jax.ShapeDtypeStruct((height, channels, width), jnp.float32),
        in_specs=[pl.BlockSpec(memory_space=pltpu.VMEM)] * 5 + [pl.BlockSpec(memory_space=pl.ANY)],
        out_specs=pl.BlockSpec(memory_space=pltpu.VMEM),
        scratch_shapes=[pltpu.VMEM(weights.shape, weights.dtype), pltpu.SemaphoreType.DMA((9,))],
        cost_estimate=pl.CostEstimate(
            flops=2 * 27 * channels * channels * height * width,
            transcendentals=0,
            bytes_accessed=sum(p.size for p in pieces) * 2 + weights.size * 2 + height * channels * width * 4,
        ),
    )(*pieces, weights)


def wgrad_body(block_ref, below_ref, above_ref, before_ref, after_ref, delta_ref, out_ref):
    pieces = (block_ref, below_ref, above_ref, before_ref, after_ref)
    height, channels = delta_ref.shape[0], delta_ref.shape[1]
    stacked = []
    for y in range(height):
        row = delta_ref[y].astype(jnp.float32)
        stacked.append(
            jnp.concatenate([shift_lanes(row, 1), row, shift_lanes(row, -1)], axis=0).astype(
                jnp.bfloat16
            )
        )
    stacked = jnp.concatenate(stacked, axis=1)
    rows_of = lax.broadcasted_iota(jnp.int32, (channels, channels), 0) >> 3
    cols_of = lax.broadcasted_iota(jnp.int32, (channels, channels), 1) >> 3
    mask = jnp.where(rows_of == cols_of, 1.0, 0.0).astype(jnp.float32)
    entry = lax.broadcasted_iota(jnp.int32, (LANES, LANES), 0) & (GW - 1)
    column = lax.broadcasted_iota(jnp.int32, (LANES, LANES), 1)
    totals = [jnp.zeros((channels, LANES), jnp.float32) for _ in range(out_ref.shape[0])]
    for dz, dy in itertools.product(range(3), repeat=2):
        rows = jnp.concatenate([source_row(pieces, dz, dy + y) for y in range(height)], axis=1)
        grads = lax.dot_general(
            stacked, rows, (((1,), (1,)), ((), ())), preferred_element_type=jnp.float32
        )
        for dx in range(3):
            tap = dz * 9 + dy * 3 + dx
            picked = grads[dx * channels : (dx + 1) * channels] * mask
            folded = picked[:, :LANES]
            for start in range(LANES, channels, LANES):
                folded = folded + picked[:, start : start + LANES]
            high = folded.astype(jnp.bfloat16)
            low = (folded - high.astype(jnp.float32)).astype(jnp.bfloat16)
            slot = (tap % TAPS_PER_BLOCK) * GW
            sel = jnp.where(column == entry + slot, 1.0, 0.0).astype(jnp.bfloat16)
            totals[tap // TAPS_PER_BLOCK] += jnp.dot(
                high, sel, preferred_element_type=jnp.float32
            ) + jnp.dot(low, sel, preferred_element_type=jnp.float32)
    for n, total in enumerate(totals):
        out_ref[n] = total


def wgrad_call(pieces, delta):
    height, channels, width = delta.shape
    blocks = -(-27 // TAPS_PER_BLOCK)
    out = pl.pallas_call(
        wgrad_body,
        out_shape=jax.ShapeDtypeStruct((blocks, channels, LANES), jnp.float32),
        in_specs=[pl.BlockSpec(memory_space=pltpu.VMEM)] * 6,
        out_specs=pl.BlockSpec(memory_space=pltpu.VMEM),
        cost_estimate=pl.CostEstimate(
            flops=2 * 27 * channels * channels * height * width + 4 * 27 * channels * LANES * LANES,
            transcendentals=0,
            bytes_accessed=sum(p.size for p in pieces) * 2 + delta.size * 2 + blocks * channels * LANES * 4,
        ),
    )(*pieces, delta)
    return out.transpose(1, 0, 2).reshape(channels, blocks * LANES)[:, : 27 * GW]


def tree_sum(blocks, order):
    steps = []
    for axis, rising in order:
        bits = []
        bit = 1
        while bit < lax.axis_size(axis):
            bits.append(bit)
            bit *= 2
        steps += [(axis, bit) for bit in (bits if rising else bits[::-1])]
    pieces = [block.reshape(-1) for block, _, _ in blocks]
    done = []
    for axis, bit in steps:
        pairs = [(i, i ^ bit) for i in range(lax.axis_size(axis))]
        upper = (lax.axis_index(axis) & bit) != 0
        members = [n for n, (_, axes, _) in enumerate(blocks) if axis in axes]
        keeps, sends = [], []
        for n in members:
            half = pieces[n].shape[0] // 2
            low, high = pieces[n][:half], pieces[n][half:]
            keeps.append(jnp.where(upper, high, low))
            sends.append(jnp.where(upper, low, high))
        got = lax.ppermute(jnp.concatenate(sends), axis, pairs)
        offset = 0
        for n, keep in zip(members, keeps):
            pieces[n] = keep + got[offset : offset + keep.shape[0]]
            offset += keep.shape[0]
        done.append((axis, pairs, upper))
    for axis, pairs, upper in reversed(done):
        members = [n for n, (_, _, axes) in enumerate(blocks) if axis in axes]
        if not members:
            continue
        got = lax.ppermute(jnp.concatenate([pieces[n] for n in members]), axis, pairs)
        offset = 0
        for n in members:
            size = pieces[n].shape[0]
            other = got[offset : offset + size]
            offset += size
            pieces[n] = jnp.where(
                upper,
                jnp.concatenate([other, pieces[n]]),
                jnp.concatenate([pieces[n], other]),
            )
    return pieces


def halo(block, planes=None):
    count = lax.axis_size("grp")
    up = [(i, i + 1) for i in range(count - 1)]
    down = [(i + 1, i) for i in range(count - 1)]
    depth, height = block.shape[0], block.shape[1]
    if planes is None:
        below = lax.ppermute(block[depth - 1 :], "grp", up)
        above = lax.ppermute(block[:1], "grp", down)
    else:
        below, above = planes
    count = lax.axis_size("sub")
    up = [(i, i + 1) for i in range(count - 1)]
    down = [(i + 1, i) for i in range(count - 1)]
    last = jnp.concatenate([below[:, height - 1 :], block[:, height - 1 :], above[:, height - 1 :]])
    first = jnp.concatenate([below[:, :1], block[:, :1], above[:, :1]])
    before = lax.ppermute(last, "sub", up)
    after = lax.ppermute(first, "sub", down)
    return block, below, above, before, after


def source_row(pieces, dz, yy):
    block, below, above, before, after = pieces
    height = block.shape[1]
    if yy == 0:
        return before[dz, 0]
    if yy == height + 1:
        return after[dz, 0]
    return (below, block, above)[dz][0, yy - 1]


def silu_slope(values):
    sigma = jax.nn.sigmoid(values)
    return sigma * (1.0 + values * (1.0 - sigma))


def conv_weights(group_weight):
    channels = group_weight.shape[0]
    spread = (jnp.arange(GW)[:, None] == jnp.arange(channels)[None, :] % GW).astype(jnp.float32)
    compact = group_weight.reshape(channels, GW, 27).astype(jnp.float32)
    forward = jnp.einsum("ojt,ji->toi", compact, spread)
    backward = jnp.einsum("ji,ojt->tio", spread, compact[:, :, ::-1])
    forward = forward.astype(group_weight.dtype).reshape(9, 3 * channels, channels)
    backward = backward.astype(group_weight.dtype).reshape(9, 3 * channels, channels)
    return forward, backward


def rounded(values):
    return lax.reduce_precision(values, exponent_bits=8, mantissa_bits=7).astype(jnp.bfloat16)


def per_device(volume, cotangent, first_weight, group_weight, third_weight):
    channels, depth, height, width = volume.shape
    flattened = volume.reshape(channels, -1)
    contract_lead = (((0,), (0,)), ((), ()))
    contract_tail = (((1,), (1,)), ((), ()))
    total_cells = depth * lax.axis_size("grp") * height * lax.axis_size("sub") * width
    factor = 1.0 / math.sqrt(total_cells)

    def to_rows(block):
        return block.reshape(channels, depth, height, width).transpose(1, 2, 0, 3)

    def from_rows(block):
        return block.transpose(1, 0, 2).reshape(channels, -1)

    forward_kernel, backward_kernel = conv_weights(group_weight)
    first_pre = lax.dot_general(
        first_weight, flattened, contract_lead, preferred_element_type=jnp.float32
    )
    first_act = rounded(jax.nn.silu(first_pre))
    assert depth == 1
    count = lax.axis_size("grp")
    up = [(i, i + 1) for i in range(count - 1)]
    down = [(i + 1, i) for i in range(count - 1)]
    near = [lax.ppermute(volume, "grp", up), lax.ppermute(volume, "grp", down)]
    near = [
        to_rows(
            rounded(
                jax.nn.silu(
                    lax.dot_general(
                        first_weight,
                        plane.reshape(channels, -1),
                        contract_lead,
                        preferred_element_type=jnp.float32,
                    )
                )
            )
        )
        for plane in near
    ]
    act_pieces = halo(to_rows(first_act), near)
    group_pre = conv_call(act_pieces, forward_kernel)
    group_act = rounded(jax.nn.silu(group_pre))
    act_flat = from_rows(group_act)
    summed = flattened.astype(jnp.float32) + lax.dot_general(
        third_weight, act_flat, contract_lead, preferred_element_type=jnp.float32
    )
    block_output = jax.nn.silu(summed).astype(jnp.bfloat16).reshape(volume.shape)
    third_delta = rounded(cotangent.reshape(channels, -1).astype(jnp.float32) * silu_slope(summed))
    third_part = lax.dot_general(
        act_flat, third_delta, contract_tail, preferred_element_type=jnp.float32
    )
    hidden_grad = rounded(jnp.dot(third_weight, third_delta, preferred_element_type=jnp.float32))
    group_delta = rounded(to_rows(hidden_grad)[0].astype(jnp.float32) * silu_slope(group_pre))
    delta_pieces = halo(group_delta[None])
    inner_grad = from_rows(rounded(conv_call(delta_pieces, backward_kernel)))
    kernel_part = wgrad_call(act_pieces, group_delta)
    first_delta = rounded(inner_grad.astype(jnp.float32) * silu_slope(first_pre))
    first_part = lax.dot_general(
        flattened, first_delta, contract_tail, preferred_element_type=jnp.float32
    )
    volume_grad = (
        (
            third_delta.astype(jnp.float32)
            + jnp.dot(first_weight, first_delta, preferred_element_type=jnp.float32)
        )
        .astype(jnp.bfloat16)
        .reshape(volume.shape)
    )
    grp_count, sub_count = lax.axis_size("grp"), lax.axis_size("sub")
    digits = grp_count.bit_length() - 1
    reverse = [int(format(n, f"0{digits}b")[::-1], 2) if digits else 0 for n in range(grp_count)]
    blocks = kernel_part.reshape(grp_count, sub_count, -1)
    kernel_laid = jnp.concatenate([blocks[n : n + 1] for n in reverse]).transpose(1, 0, 2)
    first_sum, third_sum, group_sum = tree_sum(
        [
            (first_part, ("sub", "grp"), ("sub", "grp")),
            (third_part, ("sub", "grp"), ("sub", "grp")),
            (kernel_laid, ("sub", "grp"), ("sub",)),
        ],
        (("sub", True), ("grp", True)),
    )
    first_grad = first_sum.reshape(first_part.shape) * factor
    third_grad = third_sum.reshape(third_part.shape) * factor
    own_rows = channels // grp_count
    group_grad = (
        group_sum.reshape(own_rows, 27, GW).transpose(0, 2, 1).reshape(own_rows, GW, 3, 3, 3) * factor
    )
    return (block_output, volume_grad, first_grad, group_grad, third_grad)


def solution(mesh):
    in_specs = (
        P(None, ("rep", "grp"), "sub", None),
        P(None, ("rep", "grp"), "sub", None),
        P(),
        P(),
        P(),
    )
    out_specs = (
        P(None, ("rep", "grp"), "sub", None),
        P(None, ("rep", "grp"), "sub", None),
        P("rep", None),
        P(("rep", "grp"), None, None, None, None),
        P("rep", None),
    )
    return jax.shard_map(
        per_device, mesh=mesh, in_specs=in_specs, out_specs=out_specs, check_vma=False
    )
```

```python
import functools
import itertools
import math

import jax
import jax.numpy as jnp
from jax import lax
from jax.experimental import pallas as pl
from jax.experimental.pallas import tpu as pltpu
from jax.sharding import PartitionSpec as P

GW = 8
LANES = 128
TAPS_PER_BLOCK = 16


def shift_lanes(block, offset):
    lane = lax.broadcasted_iota(jnp.int32, block.shape, 1)
    rolled = pltpu.roll(block, (-offset) % LANES, 1)
    edge = LANES - 1 if offset > 0 else 0
    return jnp.where(lane == edge, jnp.zeros_like(rolled), rolled)


def conv_body(block_ref, below_ref, above_ref, before_ref, after_ref, w_hbm, out_ref, w_vmem, sems):
    pieces = (block_ref, below_ref, above_ref, before_ref, after_ref)
    height, channels = out_ref.shape[0], out_ref.shape[1]
    copies = [pltpu.make_async_copy(w_hbm.at[k], w_vmem.at[k], sems.at[k]) for k in range(9)]
    for copy in copies:
        copy.start()
    sources = [
        jnp.concatenate([source_row(pieces, dz, dy + y) for y in range(height)], axis=1)
        for dz, dy in itertools.product(range(3), repeat=2)
    ]
    out_group = lax.broadcasted_iota(jnp.int32, (LANES, channels), 0) >> 3
    in_group = lax.broadcasted_iota(jnp.int32, (LANES, channels), 1) >> 3
    chunks = []
    for start in range(0, 3 * channels, LANES):
        same = out_group + (start % channels) // GW == in_group
        total = None
        for k, source in enumerate(sources):
            if start == 0:
                copies[k].wait()
            weight = w_vmem[k, start : start + LANES]
            weight = jnp.where(same, weight, jnp.zeros_like(weight))
            product = jnp.dot(weight, source, preferred_element_type=jnp.float32)
            total = product if total is None else total + product
        chunks.append(total)
    parts = jnp.concatenate(chunks, axis=0)
    for y in range(height):
        lanes = slice(y * LANES, (y + 1) * LANES)
        out_ref[y] = (
            parts[channels : 2 * channels, lanes]
            + shift_lanes(parts[:channels, lanes], -1)
            + shift_lanes(parts[2 * channels :, lanes], 1)
        )


def conv_call(pieces, weights):
    _, height, channels, width = pieces[0].shape
    return pl.pallas_call(
        conv_body,
        out_shape=jax.ShapeDtypeStruct((height, channels, width), jnp.float32),
        in_specs=[pl.BlockSpec(memory_space=pltpu.VMEM)] * 5 + [pl.BlockSpec(memory_space=pl.ANY)],
        out_specs=pl.BlockSpec(memory_space=pltpu.VMEM),
        scratch_shapes=[pltpu.VMEM(weights.shape, weights.dtype), pltpu.SemaphoreType.DMA((9,))],
        cost_estimate=pl.CostEstimate(
            flops=2 * 27 * channels * channels * height * width,
            transcendentals=0,
            bytes_accessed=sum(p.size for p in pieces) * 2 + weights.size * 2 + height * channels * width * 4,
        ),
    )(*pieces, weights)


def wgrad_body(block_ref, below_ref, above_ref, before_ref, after_ref, delta_ref, out_ref):
    pieces = (block_ref, below_ref, above_ref, before_ref, after_ref)
    height, channels = delta_ref.shape[0], delta_ref.shape[1]
    stacked = []
    for y in range(height):
        row = delta_ref[y].astype(jnp.float32)
        stacked.append(
            jnp.concatenate([shift_lanes(row, 1), row, shift_lanes(row, -1)], axis=0).astype(
                jnp.bfloat16
            )
        )
    stacked = jnp.concatenate(stacked, axis=1)
    rows_of = lax.broadcasted_iota(jnp.int32, (channels, channels), 0) >> 3
    cols_of = lax.broadcasted_iota(jnp.int32, (channels, channels), 1) >> 3
    mask = jnp.where(rows_of == cols_of, 1.0, 0.0).astype(jnp.float32)
    entry = lax.broadcasted_iota(jnp.int32, (LANES, LANES), 0) & (GW - 1)
    column = lax.broadcasted_iota(jnp.int32, (LANES, LANES), 1)
    totals = [jnp.zeros((channels, LANES), jnp.float32) for _ in range(out_ref.shape[0])]
    for dz, dy in itertools.product(range(3), repeat=2):
        rows = jnp.concatenate([source_row(pieces, dz, dy + y) for y in range(height)], axis=1)
        grads = lax.dot_general(
            stacked, rows, (((1,), (1,)), ((), ())), preferred_element_type=jnp.float32
        )
        for dx in range(3):
            tap = dz * 9 + dy * 3 + dx
            picked = grads[dx * channels : (dx + 1) * channels] * mask
            folded = picked[:, :LANES]
            for start in range(LANES, channels, LANES):
                folded = folded + picked[:, start : start + LANES]
            high = folded.astype(jnp.bfloat16)
            low = (folded - high.astype(jnp.float32)).astype(jnp.bfloat16)
            slot = (tap % TAPS_PER_BLOCK) * GW
            sel = jnp.where(column == entry + slot, 1.0, 0.0).astype(jnp.bfloat16)
            totals[tap // TAPS_PER_BLOCK] += jnp.dot(
                high, sel, preferred_element_type=jnp.float32
            ) + jnp.dot(low, sel, preferred_element_type=jnp.float32)
    for n, total in enumerate(totals):
        out_ref[n] = total


def wgrad_call(pieces, delta):
    height, channels, width = delta.shape
    blocks = -(-27 // TAPS_PER_BLOCK)
    out = pl.pallas_call(
        wgrad_body,
        out_shape=jax.ShapeDtypeStruct((blocks, channels, LANES), jnp.float32),
        in_specs=[pl.BlockSpec(memory_space=pltpu.VMEM)] * 6,
        out_specs=pl.BlockSpec(memory_space=pltpu.VMEM),
        cost_estimate=pl.CostEstimate(
            flops=2 * 27 * channels * channels * height * width + 4 * 27 * channels * LANES * LANES,
            transcendentals=0,
            bytes_accessed=sum(p.size for p in pieces) * 2 + delta.size * 2 + blocks * channels * LANES * 4,
        ),
    )(*pieces, delta)
    return out.transpose(1, 0, 2).reshape(channels, blocks * LANES)[:, : 27 * GW]


def tree_sum(blocks, order, scale):
    steps = []
    for axis, rising in order:
        bits = []
        bit = 1
        while bit < lax.axis_size(axis):
            bits.append(bit)
            bit *= 2
        steps += [(axis, bit) for bit in (bits if rising else bits[::-1])]
    pieces = [block.reshape(-1) for block, _, _ in blocks]
    done = []
    for axis, bit in steps:
        pairs = [(i, i ^ bit) for i in range(lax.axis_size(axis))]
        upper = (lax.axis_index(axis) & bit) != 0
        members = [n for n, (_, axes, _) in enumerate(blocks) if axis in axes]
        keeps, sends = [], []
        for n in members:
            half = pieces[n].shape[0] // 2
            low, high = pieces[n][:half], pieces[n][half:]
            keeps.append(jnp.where(upper, high, low))
            sends.append(jnp.where(upper, low, high))
        got = lax.ppermute(jnp.concatenate(sends), axis, pairs)
        offset = 0
        for n, keep in zip(members, keeps):
            pieces[n] = keep + got[offset : offset + keep.shape[0]]
            offset += keep.shape[0]
        done.append((axis, pairs, upper))
    pieces = [piece * scale for piece in pieces]
    for axis, pairs, upper in reversed(done):
        members = [n for n, (_, _, axes) in enumerate(blocks) if axis in axes]
        if not members:
            continue
        got = lax.ppermute(jnp.concatenate([pieces[n] for n in members]), axis, pairs)
        offset = 0
        for n in members:
            size = pieces[n].shape[0]
            other = got[offset : offset + size]
            offset += size
            pieces[n] = jnp.where(
                upper,
                jnp.concatenate([other, pieces[n]]),
                jnp.concatenate([pieces[n], other]),
            )
    return pieces


def halo(block, planes=None):
    count = lax.axis_size("grp")
    up = [(i, i + 1) for i in range(count - 1)]
    down = [(i + 1, i) for i in range(count - 1)]
    depth, height = block.shape[0], block.shape[1]
    if planes is None:
        below = lax.ppermute(block[depth - 1 :], "grp", up)
        above = lax.ppermute(block[:1], "grp", down)
    else:
        below, above = planes
    count = lax.axis_size("sub")
    up = [(i, i + 1) for i in range(count - 1)]
    down = [(i + 1, i) for i in range(count - 1)]
    last = jnp.concatenate([below[:, height - 1 :], block[:, height - 1 :], above[:, height - 1 :]])
    first = jnp.concatenate([below[:, :1], block[:, :1], above[:, :1]])
    before = lax.ppermute(last, "sub", up)
    after = lax.ppermute(first, "sub", down)
    return block, below, above, before, after


def source_row(pieces, dz, yy):
    block, below, above, before, after = pieces
    height = block.shape[1]
    if yy == 0:
        return before[dz, 0]
    if yy == height + 1:
        return after[dz, 0]
    return (below, block, above)[dz][0, yy - 1]


def silu_slope(values):
    sigma = jax.nn.sigmoid(values)
    return sigma * (1.0 + values * (1.0 - sigma))


def conv_weights(group_weight):
    channels = group_weight.shape[0]
    spread = (jnp.arange(GW)[:, None] == jnp.arange(channels)[None, :] % GW).astype(jnp.float32)
    compact = group_weight.reshape(channels, GW, 27).astype(jnp.float32)
    forward = jnp.einsum("ojt,ji->toi", compact, spread)
    backward = jnp.einsum("ji,ojt->tio", spread, compact[:, :, ::-1])
    forward = forward.astype(group_weight.dtype).reshape(9, 3 * channels, channels)
    backward = backward.astype(group_weight.dtype).reshape(9, 3 * channels, channels)
    return forward, backward


def rounded(values):
    return lax.reduce_precision(values, exponent_bits=8, mantissa_bits=7).astype(jnp.bfloat16)


def per_device(volume, cotangent, first_weight, group_weight, third_weight):
    channels, depth, height, width = volume.shape
    flattened = volume.reshape(channels, -1)
    contract_lead = (((0,), (0,)), ((), ()))
    contract_tail = (((1,), (1,)), ((), ()))
    total_cells = depth * lax.axis_size("grp") * height * lax.axis_size("sub") * width
    factor = 1.0 / math.sqrt(total_cells)

    def to_rows(block):
        return block.reshape(channels, depth, height, width).transpose(1, 2, 0, 3)

    def from_rows(block):
        return block.transpose(1, 0, 2).reshape(channels, -1)

    forward_kernel, backward_kernel = conv_weights(group_weight)
    first_pre = lax.dot_general(
        first_weight, flattened, contract_lead, preferred_element_type=jnp.float32
    )
    first_act = rounded(jax.nn.silu(first_pre))
    assert depth == 1
    count = lax.axis_size("grp")
    up = [(i, i + 1) for i in range(count - 1)]
    down = [(i + 1, i) for i in range(count - 1)]
    near = [lax.ppermute(volume, "grp", up), lax.ppermute(volume, "grp", down)]
    near = [
        to_rows(
            rounded(
                jax.nn.silu(
                    lax.dot_general(
                        first_weight,
                        plane.reshape(channels, -1),
                        contract_lead,
                        preferred_element_type=jnp.float32,
                    )
                )
            )
        )
        for plane in near
    ]
    act_pieces = halo(to_rows(first_act), near)
    group_pre = conv_call(act_pieces, forward_kernel)
    group_act = rounded(jax.nn.silu(group_pre))
    act_flat = from_rows(group_act)
    summed = flattened.astype(jnp.float32) + lax.dot_general(
        third_weight, act_flat, contract_lead, preferred_element_type=jnp.float32
    )
    block_output = jax.nn.silu(summed).astype(jnp.bfloat16).reshape(volume.shape)
    third_delta = rounded(cotangent.reshape(channels, -1).astype(jnp.float32) * silu_slope(summed))
    third_part = lax.dot_general(
        act_flat, third_delta, contract_tail, preferred_element_type=jnp.float32
    )
    hidden_grad = rounded(jnp.dot(third_weight, third_delta, preferred_element_type=jnp.float32))
    group_delta = rounded(to_rows(hidden_grad)[0].astype(jnp.float32) * silu_slope(group_pre))
    delta_pieces = halo(group_delta[None])
    inner_grad = from_rows(rounded(conv_call(delta_pieces, backward_kernel)))
    kernel_part = wgrad_call(act_pieces, group_delta)
    first_delta = rounded(inner_grad.astype(jnp.float32) * silu_slope(first_pre))
    first_part = lax.dot_general(
        flattened, first_delta, contract_tail, preferred_element_type=jnp.float32
    )
    volume_grad = (
        (
            third_delta.astype(jnp.float32)
            + jnp.dot(first_weight, first_delta, preferred_element_type=jnp.float32)
        )
        .astype(jnp.bfloat16)
        .reshape(volume.shape)
    )
    grp_count, sub_count = lax.axis_size("grp"), lax.axis_size("sub")
    digits = grp_count.bit_length() - 1
    reverse = [int(format(n, f"0{digits}b")[::-1], 2) if digits else 0 for n in range(grp_count)]
    blocks = kernel_part.reshape(grp_count, sub_count, -1)
    kernel_laid = jnp.concatenate([blocks[n : n + 1] for n in reverse]).transpose(1, 0, 2)
    first_sum, third_sum, group_sum = tree_sum(
        [
            (first_part, ("sub", "grp"), ("sub", "grp")),
            (third_part, ("sub", "grp"), ("sub", "grp")),
            (kernel_laid, ("sub", "grp"), ("sub",)),
        ],
        (("sub", True), ("grp", True)),
        factor,
    )
    first_grad = first_sum.reshape(first_part.shape)
    third_grad = third_sum.reshape(third_part.shape)
    own_rows = channels // grp_count
    group_grad = (
        group_sum.reshape(own_rows, 27, GW).transpose(0, 2, 1).reshape(own_rows, GW, 3, 3, 3)
    )
    return (block_output, volume_grad, first_grad, group_grad, third_grad)


def solution(mesh):
    in_specs = (
        P(None, ("rep", "grp"), "sub", None),
        P(None, ("rep", "grp"), "sub", None),
        P(),
        P(),
        P(),
    )
    out_specs = (
        P(None, ("rep", "grp"), "sub", None),
        P(None, ("rep", "grp"), "sub", None),
        P("rep", None),
        P(("rep", "grp"), None, None, None, None),
        P("rep", None),
    )
    return jax.shard_map(
        per_device, mesh=mesh, in_specs=in_specs, out_specs=out_specs, check_vma=False
    )
```

```python
import functools
import itertools
import math

import jax
import jax.numpy as jnp
from jax import lax
from jax.experimental import pallas as pl
from jax.experimental.pallas import tpu as pltpu
from jax.sharding import PartitionSpec as P

GW = 8
LANES = 128
TAPS_PER_BLOCK = 16


def shift_lanes(block, offset):
    lane = lax.broadcasted_iota(jnp.int32, block.shape, 1)
    rolled = pltpu.roll(block, (-offset) % LANES, 1)
    edge = LANES - 1 if offset > 0 else 0
    return jnp.where(lane == edge, jnp.zeros_like(rolled), rolled)


def conv_body(block_ref, below_ref, above_ref, before_ref, after_ref, w_hbm, out_ref, w_vmem, sems):
    pieces = (block_ref, below_ref, above_ref, before_ref, after_ref)
    height, channels = out_ref.shape[0], out_ref.shape[1]
    copies = [pltpu.make_async_copy(w_hbm.at[k], w_vmem.at[k], sems.at[k]) for k in range(9)]
    for copy in copies:
        copy.start()
    sources = [
        jnp.concatenate([source_row(pieces, dz, dy + y) for y in range(height)], axis=1)
        for dz, dy in itertools.product(range(3), repeat=2)
    ]
    out_group = lax.broadcasted_iota(jnp.int32, (LANES, channels), 0) >> 3
    in_group = lax.broadcasted_iota(jnp.int32, (LANES, channels), 1) >> 3
    chunks = []
    for start in range(0, 3 * channels, LANES):
        same = out_group + (start % channels) // GW == in_group
        total = None
        for k, source in enumerate(sources):
            if start == 0:
                copies[k].wait()
            weight = w_vmem[k, start : start + LANES]
            weight = jnp.where(same, weight, jnp.zeros_like(weight))
            product = jnp.dot(weight, source, preferred_element_type=jnp.float32)
            total = product if total is None else total + product
        chunks.append(total)
    parts = jnp.concatenate(chunks, axis=0)
    for y in range(height):
        lanes = slice(y * LANES, (y + 1) * LANES)
        out_ref[y] = (
            parts[channels : 2 * channels, lanes]
            + shift_lanes(parts[:channels, lanes], -1)
            + shift_lanes(parts[2 * channels :, lanes], 1)
        )


def conv_call(pieces, weights):
    _, height, channels, width = pieces[0].shape
    return pl.pallas_call(
        conv_body,
        out_shape=jax.ShapeDtypeStruct((height, channels, width), jnp.float32),
        in_specs=[pl.BlockSpec(memory_space=pltpu.VMEM)] * 5 + [pl.BlockSpec(memory_space=pl.ANY)],
        out_specs=pl.BlockSpec(memory_space=pltpu.VMEM),
        scratch_shapes=[pltpu.VMEM(weights.shape, weights.dtype), pltpu.SemaphoreType.DMA((9,))],
        cost_estimate=pl.CostEstimate(
            flops=2 * 27 * channels * channels * height * width,
            transcendentals=0,
            bytes_accessed=sum(p.size for p in pieces) * 2 + weights.size * 2 + height * channels * width * 4,
        ),
    )(*pieces, weights)


def wgrad_body(block_ref, below_ref, above_ref, before_ref, after_ref, delta_ref, out_ref):
    pieces = (block_ref, below_ref, above_ref, before_ref, after_ref)
    height, channels = delta_ref.shape[0], delta_ref.shape[1]
    stacked = []
    for y in range(height):
        row = delta_ref[y].astype(jnp.float32)
        stacked.append(
            jnp.concatenate([shift_lanes(row, 1), row, shift_lanes(row, -1)], axis=0).astype(
                jnp.bfloat16
            )
        )
    stacked = jnp.concatenate(stacked, axis=1)
    rows_of = lax.broadcasted_iota(jnp.int32, (channels, channels), 0) >> 3
    cols_of = lax.broadcasted_iota(jnp.int32, (channels, channels), 1) >> 3
    mask = jnp.where(rows_of == cols_of, 1.0, 0.0).astype(jnp.float32)
    entry = lax.broadcasted_iota(jnp.int32, (LANES, LANES), 0) & (GW - 1)
    column = lax.broadcasted_iota(jnp.int32, (LANES, LANES), 1)
    totals = [jnp.zeros((channels, LANES), jnp.float32) for _ in range(out_ref.shape[0])]
    for dz, dy in itertools.product(range(3), repeat=2):
        rows = jnp.concatenate([source_row(pieces, dz, dy + y) for y in range(height)], axis=1)
        grads = lax.dot_general(
            stacked, rows, (((1,), (1,)), ((), ())), preferred_element_type=jnp.float32
        )
        for dx in range(3):
            tap = dz * 9 + dy * 3 + dx
            picked = grads[dx * channels : (dx + 1) * channels] * mask
            folded = picked[:, :LANES]
            for start in range(LANES, channels, LANES):
                folded = folded + picked[:, start : start + LANES]
            high = folded.astype(jnp.bfloat16)
            low = (folded - high.astype(jnp.float32)).astype(jnp.bfloat16)
            slot = (tap % TAPS_PER_BLOCK) * GW
            sel = jnp.where(column == entry + slot, 1.0, 0.0).astype(jnp.bfloat16)
            totals[tap // TAPS_PER_BLOCK] += jnp.dot(
                high, sel, preferred_element_type=jnp.float32
            ) + jnp.dot(low, sel, preferred_element_type=jnp.float32)
    for n, total in enumerate(totals):
        out_ref[n] = total


def wgrad_call(pieces, delta):
    height, channels, width = delta.shape
    blocks = -(-27 // TAPS_PER_BLOCK)
    out = pl.pallas_call(
        wgrad_body,
        out_shape=jax.ShapeDtypeStruct((blocks, channels, LANES), jnp.float32),
        in_specs=[pl.BlockSpec(memory_space=pltpu.VMEM)] * 6,
        out_specs=pl.BlockSpec(memory_space=pltpu.VMEM),
        cost_estimate=pl.CostEstimate(
            flops=2 * 27 * channels * channels * height * width + 4 * 27 * channels * LANES * LANES,
            transcendentals=0,
            bytes_accessed=sum(p.size for p in pieces) * 2 + delta.size * 2 + blocks * channels * LANES * 4,
        ),
    )(*pieces, delta)
    return out.transpose(1, 0, 2).reshape(channels, blocks * LANES)[:, : 27 * GW]


def tree_sum(blocks, order, scale):
    steps = []
    for axis, rising in order:
        bits = []
        bit = 1
        while bit < lax.axis_size(axis):
            bits.append(bit)
            bit *= 2
        steps += [(axis, bit) for bit in (bits if rising else bits[::-1])]
    pieces = [block.reshape(-1) for block, _, _ in blocks]
    done = []
    for axis, bit in steps:
        pairs = [(i, i ^ bit) for i in range(lax.axis_size(axis))]
        upper = (lax.axis_index(axis) & bit) != 0
        members = [n for n, (_, axes, _) in enumerate(blocks) if axis in axes]
        keeps, sends = [], []
        for n in members:
            half = pieces[n].shape[0] // 2
            low, high = pieces[n][:half], pieces[n][half:]
            keeps.append(jnp.where(upper, high, low))
            sends.append(jnp.where(upper, low, high))
        got = lax.ppermute(jnp.concatenate(sends), axis, pairs)
        offset = 0
        for n, keep in zip(members, keeps):
            pieces[n] = keep + got[offset : offset + keep.shape[0]]
            offset += keep.shape[0]
        done.append((axis, pairs, upper))
    pieces = [piece * scale for piece in pieces]
    for axis, pairs, upper in reversed(done):
        members = [n for n, (_, _, axes) in enumerate(blocks) if axis in axes]
        if not members:
            continue
        got = lax.ppermute(jnp.concatenate([pieces[n] for n in members]), axis, pairs)
        offset = 0
        for n in members:
            size = pieces[n].shape[0]
            other = got[offset : offset + size]
            offset += size
            mine = upper.astype(jnp.int32) * size
            joined = lax.dynamic_update_slice_in_dim(
                jnp.concatenate([other, other]), pieces[n], mine, 0
            )
            pieces[n] = joined
    return pieces


def halo(block, planes=None):
    count = lax.axis_size("grp")
    up = [(i, i + 1) for i in range(count - 1)]
    down = [(i + 1, i) for i in range(count - 1)]
    depth, height = block.shape[0], block.shape[1]
    if planes is None:
        below = lax.ppermute(block[depth - 1 :], "grp", up)
        above = lax.ppermute(block[:1], "grp", down)
    else:
        below, above = planes
    count = lax.axis_size("sub")
    up = [(i, i + 1) for i in range(count - 1)]
    down = [(i + 1, i) for i in range(count - 1)]
    last = jnp.concatenate([below[:, height - 1 :], block[:, height - 1 :], above[:, height - 1 :]])
    first = jnp.concatenate([below[:, :1], block[:, :1], above[:, :1]])
    before = lax.ppermute(last, "sub", up)
    after = lax.ppermute(first, "sub", down)
    return block, below, above, before, after


def source_row(pieces, dz, yy):
    block, below, above, before, after = pieces
    height = block.shape[1]
    if yy == 0:
        return before[dz, 0]
    if yy == height + 1:
        return after[dz, 0]
    return (below, block, above)[dz][0, yy - 1]


def silu_slope(values):
    sigma = jax.nn.sigmoid(values)
    return sigma * (1.0 + values * (1.0 - sigma))


def conv_weights(group_weight):
    channels = group_weight.shape[0]
    spread = (jnp.arange(GW)[:, None] == jnp.arange(channels)[None, :] % GW).astype(jnp.float32)
    compact = group_weight.reshape(channels, GW, 27).astype(jnp.float32)
    forward = jnp.einsum("ojt,ji->toi", compact, spread)
    backward = jnp.einsum("ji,ojt->tio", spread, compact[:, :, ::-1])
    forward = forward.astype(group_weight.dtype).reshape(9, 3 * channels, channels)
    backward = backward.astype(group_weight.dtype).reshape(9, 3 * channels, channels)
    return forward, backward


def rounded(values):
    return lax.reduce_precision(values, exponent_bits=8, mantissa_bits=7).astype(jnp.bfloat16)


def per_device(volume, cotangent, first_weight, group_weight, third_weight):
    channels, depth, height, width = volume.shape
    flattened = volume.reshape(channels, -1)
    contract_lead = (((0,), (0,)), ((), ()))
    contract_tail = (((1,), (1,)), ((), ()))
    total_cells = depth * lax.axis_size("grp") * height * lax.axis_size("sub") * width
    factor = 1.0 / math.sqrt(total_cells)

    def to_rows(block):
        return block.reshape(channels, depth, height, width).transpose(1, 2, 0, 3)

    def from_rows(block):
        return block.transpose(1, 0, 2).reshape(channels, -1)

    forward_kernel, backward_kernel = conv_weights(group_weight)
    first_pre = lax.dot_general(
        first_weight, flattened, contract_lead, preferred_element_type=jnp.float32
    )
    first_act = rounded(jax.nn.silu(first_pre))
    assert depth == 1
    count = lax.axis_size("grp")
    up = [(i, i + 1) for i in range(count - 1)]
    down = [(i + 1, i) for i in range(count - 1)]
    near = [lax.ppermute(volume, "grp", up), lax.ppermute(volume, "grp", down)]
    near = [
        to_rows(
            rounded(
                jax.nn.silu(
                    lax.dot_general(
                        first_weight,
                        plane.reshape(channels, -1),
                        contract_lead,
                        preferred_element_type=jnp.float32,
                    )
                )
            )
        )
        for plane in near
    ]
    act_pieces = halo(to_rows(first_act), near)
    group_pre = conv_call(act_pieces, forward_kernel)
    group_act = rounded(jax.nn.silu(group_pre))
    act_flat = from_rows(group_act)
    summed = flattened.astype(jnp.float32) + lax.dot_general(
        third_weight, act_flat, contract_lead, preferred_element_type=jnp.float32
    )
    block_output = jax.nn.silu(summed).astype(jnp.bfloat16).reshape(volume.shape)
    third_delta = rounded(cotangent.reshape(channels, -1).astype(jnp.float32) * silu_slope(summed))
    third_part = lax.dot_general(
        act_flat, third_delta, contract_tail, preferred_element_type=jnp.float32
    )
    hidden_grad = rounded(jnp.dot(third_weight, third_delta, preferred_element_type=jnp.float32))
    group_delta = rounded(to_rows(hidden_grad)[0].astype(jnp.float32) * silu_slope(group_pre))
    delta_pieces = halo(group_delta[None])
    inner_grad = from_rows(rounded(conv_call(delta_pieces, backward_kernel)))
    kernel_part = wgrad_call(act_pieces, group_delta)
    first_delta = rounded(inner_grad.astype(jnp.float32) * silu_slope(first_pre))
    first_part = lax.dot_general(
        flattened, first_delta, contract_tail, preferred_element_type=jnp.float32
    )
    volume_grad = (
        (
            third_delta.astype(jnp.float32)
            + jnp.dot(first_weight, first_delta, preferred_element_type=jnp.float32)
        )
        .astype(jnp.bfloat16)
        .reshape(volume.shape)
    )
    grp_count, sub_count = lax.axis_size("grp"), lax.axis_size("sub")
    digits = grp_count.bit_length() - 1
    reverse = [int(format(n, f"0{digits}b")[::-1], 2) if digits else 0 for n in range(grp_count)]
    blocks = kernel_part.reshape(grp_count, sub_count, -1)
    kernel_laid = jnp.concatenate([blocks[n : n + 1] for n in reverse]).transpose(1, 0, 2)
    first_sum, third_sum, group_sum = tree_sum(
        [
            (first_part, ("sub", "grp"), ("sub", "grp")),
            (third_part, ("sub", "grp"), ("sub", "grp")),
            (kernel_laid, ("sub", "grp"), ("sub",)),
        ],
        (("sub", True), ("grp", True)),
        factor,
    )
    first_grad = first_sum.reshape(first_part.shape)
    third_grad = third_sum.reshape(third_part.shape)
    own_rows = channels // grp_count
    group_grad = (
        group_sum.reshape(own_rows, 27, GW).transpose(0, 2, 1).reshape(own_rows, GW, 3, 3, 3)
    )
    return (block_output, volume_grad, first_grad, group_grad, third_grad)


def solution(mesh):
    in_specs = (
        P(None, ("rep", "grp"), "sub", None),
        P(None, ("rep", "grp"), "sub", None),
        P(),
        P(),
        P(),
    )
    out_specs = (
        P(None, ("rep", "grp"), "sub", None),
        P(None, ("rep", "grp"), "sub", None),
        P("rep", None),
        P(("rep", "grp"), None, None, None, None),
        P("rep", None),
    )
    return jax.shard_map(
        per_device, mesh=mesh, in_specs=in_specs, out_specs=out_specs, check_vma=False
    )
```

```python
import functools
import itertools
import math

import jax
import jax.numpy as jnp
from jax import lax
from jax.experimental import pallas as pl
from jax.experimental.pallas import tpu as pltpu
from jax.sharding import PartitionSpec as P

GW = 8
LANES = 128
TAPS_PER_BLOCK = 16


def shift_lanes(block, offset):
    lane = lax.broadcasted_iota(jnp.int32, block.shape, 1)
    rolled = pltpu.roll(block, (-offset) % LANES, 1)
    edge = LANES - 1 if offset > 0 else 0
    return jnp.where(lane == edge, jnp.zeros_like(rolled), rolled)


def conv_body(block_ref, below_ref, above_ref, before_ref, after_ref, w_hbm, out_ref, w_vmem, sems):
    pieces = (block_ref, below_ref, above_ref, before_ref, after_ref)
    height, channels = out_ref.shape[0], out_ref.shape[1]
    copies = [pltpu.make_async_copy(w_hbm.at[k], w_vmem.at[k], sems.at[k]) for k in range(9)]
    for copy in copies:
        copy.start()
    sources = [
        jnp.concatenate([source_row(pieces, dz, dy + y) for y in range(height)], axis=1)
        for dz, dy in itertools.product(range(3), repeat=2)
    ]
    out_group = lax.broadcasted_iota(jnp.int32, (LANES, channels), 0) >> 3
    in_group = lax.broadcasted_iota(jnp.int32, (LANES, channels), 1) >> 3
    chunks = []
    for start in range(0, 3 * channels, LANES):
        same = out_group + (start % channels) // GW == in_group
        total = None
        for k, source in enumerate(sources):
            if start == 0:
                copies[k].wait()
            weight = w_vmem[k, start : start + LANES]
            weight = jnp.where(same, weight, jnp.zeros_like(weight))
            product = jnp.dot(weight, source, preferred_element_type=jnp.float32)
            total = product if total is None else total + product
        chunks.append(total)
    parts = jnp.concatenate(chunks, axis=0)
    for y in range(height):
        lanes = slice(y * LANES, (y + 1) * LANES)
        out_ref[y] = (
            parts[channels : 2 * channels, lanes]
            + shift_lanes(parts[:channels, lanes], -1)
            + shift_lanes(parts[2 * channels :, lanes], 1)
        )


def conv_call(pieces, weights):
    _, height, channels, width = pieces[0].shape
    return pl.pallas_call(
        conv_body,
        out_shape=jax.ShapeDtypeStruct((height, channels, width), jnp.float32),
        in_specs=[pl.BlockSpec(memory_space=pltpu.VMEM)] * 5 + [pl.BlockSpec(memory_space=pl.ANY)],
        out_specs=pl.BlockSpec(memory_space=pltpu.VMEM),
        scratch_shapes=[pltpu.VMEM(weights.shape, weights.dtype), pltpu.SemaphoreType.DMA((9,))],
        cost_estimate=pl.CostEstimate(
            flops=2 * 27 * channels * channels * height * width,
            transcendentals=0,
            bytes_accessed=sum(p.size for p in pieces) * 2 + weights.size * 2 + height * channels * width * 4,
        ),
    )(*pieces, weights)


def wgrad_body(block_ref, below_ref, above_ref, before_ref, after_ref, delta_ref, out_ref):
    pieces = (block_ref, below_ref, above_ref, before_ref, after_ref)
    height, channels = delta_ref.shape[0], delta_ref.shape[1]
    stacked = []
    for y in range(height):
        row = delta_ref[y].astype(jnp.float32)
        stacked.append(
            jnp.concatenate([shift_lanes(row, 1), row, shift_lanes(row, -1)], axis=0).astype(
                jnp.bfloat16
            )
        )
    stacked = jnp.concatenate(stacked, axis=1)
    rows_of = lax.broadcasted_iota(jnp.int32, (channels, channels), 0) >> 3
    cols_of = lax.broadcasted_iota(jnp.int32, (channels, channels), 1) >> 3
    mask = jnp.where(rows_of == cols_of, 1.0, 0.0).astype(jnp.float32)
    entry = lax.broadcasted_iota(jnp.int32, (LANES, LANES), 0) & (GW - 1)
    column = lax.broadcasted_iota(jnp.int32, (LANES, LANES), 1)
    totals = [jnp.zeros((channels, LANES), jnp.float32) for _ in range(out_ref.shape[0])]
    for dz, dy in itertools.product(range(3), repeat=2):
        rows = jnp.concatenate([source_row(pieces, dz, dy + y) for y in range(height)], axis=1)
        grads = lax.dot_general(
            stacked, rows, (((1,), (1,)), ((), ())), preferred_element_type=jnp.float32
        )
        for dx in range(3):
            tap = dz * 9 + dy * 3 + dx
            picked = grads[dx * channels : (dx + 1) * channels] * mask
            folded = picked[:, :LANES]
            for start in range(LANES, channels, LANES):
                folded = folded + picked[:, start : start + LANES]
            high = folded.astype(jnp.bfloat16)
            low = (folded - high.astype(jnp.float32)).astype(jnp.bfloat16)
            slot = (tap % TAPS_PER_BLOCK) * GW
            sel = jnp.where(column == entry + slot, 1.0, 0.0).astype(jnp.bfloat16)
            totals[tap // TAPS_PER_BLOCK] += jnp.dot(
                high, sel, preferred_element_type=jnp.float32
            ) + jnp.dot(low, sel, preferred_element_type=jnp.float32)
    for n, total in enumerate(totals):
        out_ref[n] = total


def wgrad_call(pieces, delta):
    height, channels, width = delta.shape
    blocks = -(-27 // TAPS_PER_BLOCK)
    out = pl.pallas_call(
        wgrad_body,
        out_shape=jax.ShapeDtypeStruct((blocks, channels, LANES), jnp.float32),
        in_specs=[pl.BlockSpec(memory_space=pltpu.VMEM)] * 6,
        out_specs=pl.BlockSpec(memory_space=pltpu.VMEM),
        cost_estimate=pl.CostEstimate(
            flops=2 * 27 * channels * channels * height * width + 4 * 27 * channels * LANES * LANES,
            transcendentals=0,
            bytes_accessed=sum(p.size for p in pieces) * 2 + delta.size * 2 + blocks * channels * LANES * 4,
        ),
    )(*pieces, delta)
    return out.transpose(1, 0, 2).reshape(channels, blocks * LANES)[:, : 27 * GW]


def tree_sum(blocks, order, scale):
    steps = []
    for axis, rising in order:
        bits = []
        bit = 1
        while bit < lax.axis_size(axis):
            bits.append(bit)
            bit *= 2
        steps += [(axis, bit) for bit in (bits if rising else bits[::-1])]
    pieces = [block.reshape(-1) for block, _, _ in blocks]
    done = []
    for axis, bit in steps:
        pairs = [(i, i ^ bit) for i in range(lax.axis_size(axis))]
        upper = (lax.axis_index(axis) & bit) != 0
        members = [n for n, (_, axes, _) in enumerate(blocks) if axis in axes]
        keeps, sends = [], []
        for n in members:
            half = pieces[n].shape[0] // 2
            low, high = pieces[n][:half], pieces[n][half:]
            keeps.append(jnp.where(upper, high, low))
            sends.append(jnp.where(upper, low, high))
        got = lax.ppermute(jnp.concatenate(sends), axis, pairs)
        offset = 0
        for n, keep in zip(members, keeps):
            pieces[n] = keep + got[offset : offset + keep.shape[0]]
            offset += keep.shape[0]
        done.append((axis, pairs, upper))
    pieces = [piece * scale for piece in pieces]
    for axis, pairs, upper in reversed(done):
        members = [n for n, (_, _, axes) in enumerate(blocks) if axis in axes]
        if not members:
            continue
        got = lax.ppermute(jnp.concatenate([pieces[n] for n in members]), axis, pairs)
        offset = 0
        for n in members:
            size = pieces[n].shape[0]
            other = got[offset : offset + size]
            offset += size
            pieces[n] = jnp.concatenate(
                [jnp.where(upper, other, pieces[n]), jnp.where(upper, pieces[n], other)]
            )
    return pieces


def halo(block, planes=None):
    count = lax.axis_size("grp")
    up = [(i, i + 1) for i in range(count - 1)]
    down = [(i + 1, i) for i in range(count - 1)]
    depth, height = block.shape[0], block.shape[1]
    if planes is None:
        below = lax.ppermute(block[depth - 1 :], "grp", up)
        above = lax.ppermute(block[:1], "grp", down)
    else:
        below, above = planes
    count = lax.axis_size("sub")
    up = [(i, i + 1) for i in range(count - 1)]
    down = [(i + 1, i) for i in range(count - 1)]
    last = jnp.concatenate([below[:, height - 1 :], block[:, height - 1 :], above[:, height - 1 :]])
    first = jnp.concatenate([below[:, :1], block[:, :1], above[:, :1]])
    before = lax.ppermute(last, "sub", up)
    after = lax.ppermute(first, "sub", down)
    return block, below, above, before, after


def source_row(pieces, dz, yy):
    block, below, above, before, after = pieces
    height = block.shape[1]
    if yy == 0:
        return before[dz, 0]
    if yy == height + 1:
        return after[dz, 0]
    return (below, block, above)[dz][0, yy - 1]


def silu_slope(values):
    sigma = jax.nn.sigmoid(values)
    return sigma * (1.0 + values * (1.0 - sigma))


def conv_weights(group_weight):
    channels = group_weight.shape[0]
    spread = (jnp.arange(GW)[:, None] == jnp.arange(channels)[None, :] % GW).astype(jnp.float32)
    compact = group_weight.reshape(channels, GW, 27).astype(jnp.float32)
    forward = jnp.einsum("ojt,ji->toi", compact, spread)
    backward = jnp.einsum("ji,ojt->tio", spread, compact[:, :, ::-1])
    forward = forward.astype(group_weight.dtype).reshape(9, 3 * channels, channels)
    backward = backward.astype(group_weight.dtype).reshape(9, 3 * channels, channels)
    return forward, backward


def rounded(values):
    return lax.reduce_precision(values, exponent_bits=8, mantissa_bits=7).astype(jnp.bfloat16)


def per_device(volume, cotangent, first_weight, group_weight, third_weight):
    channels, depth, height, width = volume.shape
    flattened = volume.reshape(channels, -1)
    contract_lead = (((0,), (0,)), ((), ()))
    contract_tail = (((1,), (1,)), ((), ()))
    total_cells = depth * lax.axis_size("grp") * height * lax.axis_size("sub") * width
    factor = 1.0 / math.sqrt(total_cells)

    def to_rows(block):
        return block.reshape(channels, depth, height, width).transpose(1, 2, 0, 3)

    def from_rows(block):
        return block.transpose(1, 0, 2).reshape(channels, -1)

    forward_kernel, backward_kernel = conv_weights(group_weight)
    first_pre = lax.dot_general(
        first_weight, flattened, contract_lead, preferred_element_type=jnp.float32
    )
    first_act = rounded(jax.nn.silu(first_pre))
    assert depth == 1
    count = lax.axis_size("grp")
    up = [(i, i + 1) for i in range(count - 1)]
    down = [(i + 1, i) for i in range(count - 1)]
    near = [lax.ppermute(volume, "grp", up), lax.ppermute(volume, "grp", down)]
    near = [
        to_rows(
            rounded(
                jax.nn.silu(
                    lax.dot_general(
                        first_weight,
                        plane.reshape(channels, -1),
                        contract_lead,
                        preferred_element_type=jnp.float32,
                    )
                )
            )
        )
        for plane in near
    ]
    act_pieces = halo(to_rows(first_act), near)
    group_pre = conv_call(act_pieces, forward_kernel)
    group_act = rounded(jax.nn.silu(group_pre))
    act_flat = from_rows(group_act)
    summed = flattened.astype(jnp.float32) + lax.dot_general(
        third_weight, act_flat, contract_lead, preferred_element_type=jnp.float32
    )
    block_output = jax.nn.silu(summed).astype(jnp.bfloat16).reshape(volume.shape)
    third_delta = rounded(cotangent.reshape(channels, -1).astype(jnp.float32) * silu_slope(summed))
    third_part = lax.dot_general(
        act_flat, third_delta, contract_tail, preferred_element_type=jnp.float32
    )
    hidden_grad = rounded(jnp.dot(third_weight, third_delta, preferred_element_type=jnp.float32))
    group_delta = rounded(to_rows(hidden_grad)[0].astype(jnp.float32) * silu_slope(group_pre))
    delta_pieces = halo(group_delta[None])
    inner_grad = from_rows(rounded(conv_call(delta_pieces, backward_kernel)))
    kernel_part = wgrad_call(act_pieces, group_delta)
    first_delta = rounded(inner_grad.astype(jnp.float32) * silu_slope(first_pre))
    first_part = lax.dot_general(
        flattened, first_delta, contract_tail, preferred_element_type=jnp.float32
    )
    volume_grad = (
        (
            third_delta.astype(jnp.float32)
            + jnp.dot(first_weight, first_delta, preferred_element_type=jnp.float32)
        )
        .astype(jnp.bfloat16)
        .reshape(volume.shape)
    )
    grp_count, sub_count = lax.axis_size("grp"), lax.axis_size("sub")
    digits = grp_count.bit_length() - 1
    reverse = [int(format(n, f"0{digits}b")[::-1], 2) if digits else 0 for n in range(grp_count)]
    blocks = kernel_part.reshape(grp_count, sub_count, -1)
    kernel_laid = jnp.concatenate([blocks[n : n + 1] for n in reverse]).transpose(1, 0, 2)
    first_sum, third_sum, group_sum = tree_sum(
        [
            (first_part, ("sub", "grp"), ("sub", "grp")),
            (third_part, ("sub", "grp"), ("sub", "grp")),
            (kernel_laid, ("sub", "grp"), ("sub",)),
        ],
        (("sub", True), ("grp", True)),
        factor,
    )
    first_grad = first_sum.reshape(first_part.shape)
    third_grad = third_sum.reshape(third_part.shape)
    own_rows = channels // grp_count
    group_grad = (
        group_sum.reshape(own_rows, 27, GW).transpose(0, 2, 1).reshape(own_rows, GW, 3, 3, 3)
    )
    return (block_output, volume_grad, first_grad, group_grad, third_grad)


def solution(mesh):
    in_specs = (
        P(None, ("rep", "grp"), "sub", None),
        P(None, ("rep", "grp"), "sub", None),
        P(),
        P(),
        P(),
    )
    out_specs = (
        P(None, ("rep", "grp"), "sub", None),
        P(None, ("rep", "grp"), "sub", None),
        P("rep", None),
        P(("rep", "grp"), None, None, None, None),
        P("rep", None),
    )
    return jax.shard_map(
        per_device, mesh=mesh, in_specs=in_specs, out_specs=out_specs, check_vma=False
    )
```
